32 devices in a mesh: gx: 4 (over x, core), gy: 8 (over z, y).
Axes of the slice: x: 2, y: 2, z: 4, core: 2. Of those that a mesh axis runs over, the one named last changes fastest.
Arguments:
- forcing: float32 [16, 16, 2, 4096], P('gx', 'gy'), may hold values from -6 to 6
- initial: float32 [16, 16, 2, 4096], P('gx', 'gy'), may hold values from -6 to 6
- blocks: float32 [16, 16, 2, 4096], P('gx', 'gy'), as said below
- face_blocks: float32 [6, 64, 64], replicated, may hold values from -0.75 to 0.75
- strength: float32 [6, 16, 16, 2], P(None, 'gx', 'gy'), may hold values from 0.2 to 2
- strong: int32 [6, 16, 16, 2], P(None, 'gx', 'gy'), may hold values 0 or 1
- colour: int32 [16, 16, 2], P('gx', 'gy'), may hold values from 0 to 1, as said below
- neighbours: int32 [6, 16, 16, 2], P(None, 'gx', 'gy'), may hold values from 2 to 48, as said below
Outputs:
- smoothed: float32 [16, 16, 2, 4096], P('gx', 'gy')
The draws below stay inside these ranges and needn't reach their ends.
Inputs may be any that keep to these rules, and one draw needn't show every extreme that they name: Elements of a column along z are stored in an order drawn per column. colour is (global x index + global y index + physical position along z + one flip common to all elements) mod 2, so elements that share a face differ in colour and every column holds one element of each colour. `neighbours`: each entry is the slot, in the extended block of the device holding the element, of the element across that face, as in the reference program; faces on the domain's boundary hold 48. Slots of the four corner columns are never named. `blocks`: each block is symmetric, and each diagonal entry exceeds the sum of the magnitudes of the other entries of its row by 0.5 or more.
All inputs are finite; a program needn't handle non-finite values. No bound on the sum of `strong` on one device may be relied on, other than what follows from the above.
Results may differ from the reference program's by a relative error of at most 0.00011.
Values sent between devices are 32-bit elements; how exact they have to be, the bound alone decides.
No kernel may reach another device: no remote copies, remote signals or barrier semaphores. Data moves between devices by JAX's collectives and lax.ppermute only.
A program may use at most 64 MiB of HBM per device.

```python
import math
import jax
import jax.numpy as jnp
from jax import lax

P_SIZE = 64
R = 64
EX = 4
EY = 2
EZ = 2
SWEEPS = 4
NX = 16
NY = 16


def column_layout(key):
    seeded = jax.random.fold_in(key, 7)
    scores = jax.random.randint(seeded, (NX, NY, EZ), 0, 1 << 20)
    distinct = scores * EZ + jnp.arange(EZ, dtype=jnp.int32)
    placed = jnp.argsort(distinct, axis=2, stable=True).astype(jnp.int32)
    slot_of = jnp.argsort(placed, axis=2, stable=True).astype(jnp.int32)
    parity_flip = jax.random.randint(jax.random.fold_in(seeded, 1), (), 0, 2)
    return (placed, slot_of, parity_flip)


def draw_colour(key, part):
    placed, slot_of, parity_flip = column_layout(key)
    grid_x = jnp.arange(NX, dtype=jnp.int32)[:, None, None]
    grid_y = jnp.arange(NY, dtype=jnp.int32)[None, :, None]
    return ((grid_x + grid_y + placed + parity_flip) % 2).astype(jnp.int32)


def draw_neighbours(key, part):
    placed, slot_of, parity_flip = column_layout(key)
    empty_slot = (EX + 2) * (EY + 2) * EZ
    grid_x = jnp.arange(NX, dtype=jnp.int32)[:, None, None]
    grid_y = jnp.arange(NY, dtype=jnp.int32)[None, :, None]
    local_x = grid_x % EX
    local_y = grid_y % EY

    def position(ext_a, ext_b, stored):
        return (ext_a * (EY + 2) + ext_b) * EZ + stored

    def lookup(slots, depth):
        return jnp.take_along_axis(slots, depth, axis=2)
    before_x = jnp.concatenate([slot_of[:1], slot_of[:-1]], axis=0)
    after_x = jnp.concatenate([slot_of[1:], slot_of[-1:]], axis=0)
    before_y = jnp.concatenate([slot_of[:, :1], slot_of[:, :-1]], axis=1)
    after_y = jnp.concatenate([slot_of[:, 1:], slot_of[:, -1:]], axis=1)
    lower_z = jnp.maximum(placed - 1, 0)
    upper_z = jnp.minimum(placed + 1, EZ - 1)
    by_face = [jnp.where(grid_x > 0, position(local_x, local_y + 1, lookup(before_x, placed)), empty_slot), jnp.where(grid_x < NX - 1, position(local_x + 2, local_y + 1, lookup(after_x, placed)), empty_slot), jnp.where(grid_y > 0, position(local_x + 1, local_y, lookup(before_y, placed)), empty_slot), jnp.where(grid_y < NY - 1, position(local_x + 1, local_y + 2, lookup(after_y, placed)), empty_slot), jnp.where(placed > 0, position(local_x + 1, local_y + 1, lookup(slot_of, lower_z)), empty_slot), jnp.where(placed < EZ - 1, position(local_x + 1, local_y + 1, lookup(slot_of, upper_z)), empty_slot)]
    return jnp.stack(by_face).astype(jnp.int32)


def draw_blocks(key, part):
    seeded = jax.random.fold_in(key, 3)
    first_key, second_key = jax.random.split(seeded)
    spread = jnp.exp(jax.random.uniform(first_key, (NX, NY, EZ, P_SIZE), jnp.float32, jnp.log(0.2), jnp.log(4.0)))
    random_part = jax.random.uniform(second_key, (NX, NY, EZ, P_SIZE, P_SIZE), jnp.float32, -1.0, 1.0) / P_SIZE
    symmetric = 0.5 * (random_part + jnp.swapaxes(random_part, -1, -2))
    rows_index = jnp.arange(P_SIZE, dtype=jnp.int32)[:, None]
    cols_index = jnp.arange(P_SIZE, dtype=jnp.int32)[None, :]
    on_diagonal = (rows_index == cols_index).astype(jnp.float32)
    matrices = symmetric * (1.0 - on_diagonal) + on_diagonal * (1.5 + spread)[..., None]
    return matrices.reshape(NX, NY, EZ, P_SIZE * P_SIZE)


def place_ends(drawn, stream_key, least, high):
    index_at = [jax.random.randint(jax.random.fold_in(stream_key, axis), (), 0, length) for axis, length in enumerate(drawn.shape)]
    widest = drawn.shape.index(max(drawn.shape))
    next_to = index_at[:widest] + [(index_at[widest] + 1) % drawn.shape[widest]] + index_at[widest + 1:]
    return drawn.at[tuple(index_at)].set(least).at[tuple(next_to)].set(high)


def levels(own_key, extent, cuts, least, top_value):
    loudness = 1.0
    for dim, shards_of in cuts:
        draws = jax.random.uniform(jax.random.fold_in(jax.random.fold_in(own_key, 6), dim), (shards_of,), jnp.float32, least / len(cuts), top_value / len(cuts))
        loudness = loudness * jnp.repeat(jnp.exp(draws), extent[dim] // shards_of).reshape((-1,) + (1,) * (len(extent) - 1 - dim))
    return loudness


def noise(key, extent, deviation, reach, cuts=(), held_as=jnp.bfloat16):
    entries = jax.random.normal(key, extent, jnp.float32) * deviation
    if len(cuts) > 0:
        entries = levels(key, extent, cuts, -0.22, 0.18) * entries
    return jnp.clip(entries, min=-reach, max=reach).astype(held_as)


def setup_inputs(seed: int = 0) -> dict:
    arg_keys = jax.random.split(jax.random.key(seed), 9)
    forcing = noise(arg_keys[0], (NX, NY, EZ, P_SIZE * R), 1.0, 6.0, ((0, 4), (1, 8)), jnp.float32)
    initial = noise(arg_keys[1], (NX, NY, EZ, P_SIZE * R), 1.0, 6.0, ((0, 4), (1, 8)), jnp.float32)
    blocks = draw_blocks(jax.random.fold_in(arg_keys[8], 71), 0)
    face_blocks = noise(arg_keys[3], (6, P_SIZE, P_SIZE), P_SIZE ** -0.5, 0.75, (), jnp.float32)
    strength = jnp.clip(jnp.exp(math.log(2.0) - 2.3025851 * jax.random.uniform(arg_keys[4], (6, NX, NY, EZ), jnp.float32) ** levels(arg_keys[4], (6, NX, NY, EZ), ((1, 4), (2, 8)), -0.2, 0.2)), 0.2, 2.0)
    strong = place_ends((jax.random.randint(arg_keys[5], (6, NX, NY, EZ), 0, 3) < 2).astype(jnp.int32), jax.random.fold_in(arg_keys[5], 1), 0, 1)
    colour = draw_colour(jax.random.fold_in(arg_keys[8], 71), 0)
    neighbours = draw_neighbours(jax.random.fold_in(arg_keys[8], 71), 0)
    return {"forcing": forcing, "initial": initial, "blocks": blocks, "face_blocks": face_blocks, "strength": strength, "strong": strong, "colour": colour, "neighbours": neighbours}


def global_rows(neighbours):
    whole_count = NX * NY * EZ
    empty_slot = (EX + 2) * (EY + 2) * EZ
    column_size = (EY + 2) * EZ
    ext_x = neighbours // column_size
    ext_y = neighbours // EZ % (EY + 2)
    ext_slot = neighbours % EZ
    grid_x = jnp.arange(NX, dtype=jnp.int32)[None, :, None, None]
    grid_y = jnp.arange(NY, dtype=jnp.int32)[None, None, :, None]
    target_x = grid_x // EX * EX + ext_x - 1
    target_y = grid_y // EY * EY + ext_y - 1
    flat_rows = (target_x * NY + target_y) * EZ + ext_slot
    return jnp.where(neighbours == empty_slot, whole_count, flat_rows).astype(jnp.int32)

def block_inverses(matrices):
    lower_factor = jnp.linalg.cholesky(matrices)
    identity = jnp.broadcast_to(jnp.eye(P_SIZE, dtype=matrices.dtype), matrices.shape)
    solved = jax.scipy.linalg.solve_triangular(lower_factor, identity, lower=True)
    return jnp.einsum('eqp,eqr->epr', solved, solved, precision=lax.Precision.HIGHEST)

def reference(forcing, initial, blocks, face_blocks, strength, strong, colour, neighbours):
    count = NX * NY * EZ
    inverse = block_inverses(blocks.reshape(count, P_SIZE, P_SIZE)).reshape(NX, NY * EZ, P_SIZE, P_SIZE)
    weight = (strength * strong.astype(strength.dtype)).reshape(6, NX, NY * EZ)
    weight_slabs = jnp.moveaxis(weight, 0, 1)
    row_slabs = jnp.moveaxis(global_rows(neighbours).reshape(6, NX, NY * EZ), 0, 1)
    target = forcing.reshape(NX, NY * EZ, P_SIZE, R)
    paint = colour.reshape(NX, NY * EZ)
    state = initial.reshape(count, P_SIZE, R)
    blank = jnp.zeros((1, P_SIZE, R), state.dtype)
    for sweep_index in range(SWEEPS):
        for paint_now in (0, 1):
            padded = jnp.concatenate([state, blank], axis=0)

            def one_slab(packed):
                rows_slab, weight_slab, target_slab, inverse_slab = packed
                coupled = jnp.zeros_like(target_slab)
                for face_index in range(6):
                    nearby = padded[rows_slab[face_index]]
                    product = jnp.einsum('pq,eqr->epr', face_blocks[face_index], nearby, precision=lax.Precision.HIGHEST)
                    coupled = coupled + weight_slab[face_index][:, None, None] * product
                return jnp.einsum('epq,eqr->epr', inverse_slab, target_slab - coupled, precision=lax.Precision.HIGHEST)
            update = lax.map(one_slab, (row_slabs, weight_slabs, target, inverse))
            current = state.reshape(NX, NY * EZ, P_SIZE, R)
            state = jnp.where((paint == paint_now)[..., None, None], update, current).reshape(count, P_SIZE, R)
    return state.reshape(NX, NY, EZ, P_SIZE * R)
```

```python
import functools

import jax
import jax.numpy as jnp
from jax import lax
from jax.experimental import pallas as pl
from jax.experimental.pallas import tpu as pltpu
from jax.sharding import PartitionSpec as P

P_SIZE = 64
R = 64
SWEEPS = 4


def padded(block, sides, width):
    for axis, dim in sides:
        count = lax.axis_size(axis)
        forward = [(i, i + 1) for i in range(count - 1)]
        backward = [(target, source) for source, target in forward]
        low = lax.ppermute(
            lax.slice_in_dim(block, block.shape[dim] - width, None, axis=dim), axis, forward
        )
        high = lax.ppermute(lax.slice_in_dim(block, 0, width, axis=dim), axis, backward)
        block = jnp.concatenate([low, block, high], axis=dim)
    return block


def _gauss_jordan_kernel(a_ref, o_ref, *, n, nb):
    lanes = n * nb
    tiles = lanes // 128
    o_ref[...] = a_ref[...]
    lane_t = lax.broadcasted_iota(jnp.int32, (n, 128), 1)
    lane_r = lax.broadcasted_iota(jnp.int32, (1, 128), 1)
    row_i = lax.broadcasted_iota(jnp.int32, (n, 128), 0)

    def spread(x):
        shift = nb
        while shift < 128:
            x = x + pltpu.roll(x, shift, 1)
            shift *= 2
        return x

    def step(k, carry):
        start = k * nb
        tile = start // 128
        off = start % 128
        tile_start = pl.multiple_of(tile * 128, 128)
        column = spread(
            jnp.where((lane_t >= off) & (lane_t < off + nb), o_ref[:, pl.ds(tile_start, 128)], 0.0)
        )
        pivot = jnp.sum(jnp.where(row_i == k, column, 0.0), axis=0, keepdims=True)
        base = pl.multiple_of((k // 8) * 8, 8)
        band = o_ref[pl.ds(base, 8), :]
        band_i = lax.broadcasted_iota(jnp.int32, band.shape, 0)
        row = jnp.sum(jnp.where(band_i == k - base, band, 0.0), axis=0, keepdims=True)
        for t in range(tiles):
            in_col = (t == tile) & (lane_r >= off) & (lane_r < off + nb)
            scaled = jnp.where(in_col, 1.0 / pivot, row[:, t * 128:(t + 1) * 128] / pivot)
            kept = jnp.where(in_col, 0.0, o_ref[:, t * 128:(t + 1) * 128])
            o_ref[:, t * 128:(t + 1) * 128] = jnp.where(row_i == k, scaled, kept - column * scaled)
        return carry

    lax.fori_loop(0, n, step, 0)


def block_inverses(matrices):
    nb, n, _ = matrices.shape
    if 128 % nb or (n * nb) % 128:
        lower_factor = jnp.linalg.cholesky(matrices)
        identity = jnp.broadcast_to(jnp.eye(n, dtype=matrices.dtype), matrices.shape)
        solved = jax.scipy.linalg.solve_triangular(lower_factor, identity, lower=True)
        return jnp.einsum("eqp,eqr->epr", solved, solved, precision=lax.Precision.HIGHEST)
    packed = jnp.transpose(matrices, (1, 2, 0)).reshape(n, n * nb)
    inverted = pl.pallas_call(
        functools.partial(_gauss_jordan_kernel, n=n, nb=nb),
        out_shape=jax.ShapeDtypeStruct((n, n * nb), jnp.float32),
        in_specs=[pl.BlockSpec(memory_space=pltpu.VMEM)],
        out_specs=pl.BlockSpec(memory_space=pltpu.VMEM),
    )(packed)
    return jnp.transpose(inverted.reshape(n, n, nb), (2, 0, 1))


def extended(layer):
    merged = padded(layer, (("gx", 0), ("gy", 1)), 1)
    return merged


def body(forcing, initial, blocks, face_blocks, strength, strong, colour, neighbours):
    span_x, span_y, span_z, width = forcing.shape
    count = span_x * span_y * span_z
    half_depth = span_z // 2
    half_count = count // 2
    inverse = block_inverses(blocks.reshape(count, P_SIZE, P_SIZE))
    weight = (strength * strong.astype(jnp.float32)).reshape(6, count, 1)
    links = neighbours.reshape(6, count)
    target = forcing.reshape(count, P_SIZE, R)
    index_x = jnp.arange(span_x, dtype=jnp.int32)[:, None, None]
    index_y = jnp.arange(span_y, dtype=jnp.int32)[None, :, None]
    column_base = (index_x * span_y + index_y) * span_z
    orders = []
    for needed in (1, 0):
        own_match = (colour == needed).astype(jnp.int32)
        orders.append(jnp.argsort(1 - own_match, axis=2, stable=True)[..., :half_depth])
    members = [(column_base + orders[1 - paint_now]).reshape(half_count) for paint_now in (0, 1)]
    member_inverse = [inverse[members[paint_now]] for paint_now in (0, 1)]
    member_target = [target[members[paint_now]] for paint_now in (0, 1)]
    member_weight = [weight[:, members[paint_now]] for paint_now in (0, 1)]
    member_links = [links[:, members[paint_now]] for paint_now in (0, 1)]
    state = initial
    for sweep_index in range(SWEEPS):
        for paint_now in (0, 1):
            table = extended(state).reshape(-1, width)
            table = jnp.concatenate([table, jnp.zeros((1, width), table.dtype)], axis=0)
            nearby = (table[member_links[paint_now]] * member_weight[paint_now]).reshape(
                6, half_count, P_SIZE, R
            )
            coupled = jnp.einsum(
                "fpq,feqr->epr", face_blocks, nearby, precision=lax.Precision.HIGHEST
            )
            update = jnp.einsum(
                "epq,eqr->epr",
                member_inverse[paint_now],
                member_target[paint_now] - coupled,
                precision=lax.Precision.HIGHEST,
            )
            flat_state = (
                state.reshape(count, width)
                .at[members[paint_now]]
                .set(update.reshape(half_count, width))
            )
            state = flat_state.reshape(span_x, span_y, span_z, width)
    return state


def solution(mesh):
    in_specs = (
        P("gx", "gy", None, None),
        P("gx", "gy", None, None),
        P("gx", "gy", None, None),
        P(),
        P(None, "gx", "gy", None),
        P(None, "gx", "gy", None),
        P("gx", "gy", None),
        P(None, "gx", "gy", None),
    )
    out_specs = P("gx", "gy", None, None)
    return jax.shard_map(body, mesh=mesh, in_specs=in_specs, out_specs=out_specs, check_vma=False)
```

```python
import functools

import jax
import jax.numpy as jnp
from jax import lax
from jax.experimental import pallas as pl
from jax.experimental.pallas import tpu as pltpu
from jax.sharding import PartitionSpec as P

P_SIZE = 64
R = 64
SWEEPS = 4


def padded(block, sides, width):
    for axis, dim in sides:
        count = lax.axis_size(axis)
        forward = [(i, i + 1) for i in range(count - 1)]
        backward = [(target, source) for source, target in forward]
        low = lax.ppermute(
            lax.slice_in_dim(block, block.shape[dim] - width, None, axis=dim), axis, forward
        )
        high = lax.ppermute(lax.slice_in_dim(block, 0, width, axis=dim), axis, backward)
        block = jnp.concatenate([low, block, high], axis=dim)
    return block


def _gauss_jordan_kernel(a_ref, o_ref, *, n, nb):
    lanes = n * nb
    tiles = lanes // 128
    o_ref[...] = a_ref[...]
    lane_t = lax.broadcasted_iota(jnp.int32, (n, 128), 1)
    lane_r = lax.broadcasted_iota(jnp.int32, (1, 128), 1)
    row_i = lax.broadcasted_iota(jnp.int32, (n, 128), 0)

    def spread(x):
        shift = nb
        while shift < 128:
            x = x + pltpu.roll(x, shift, 1)
            shift *= 2
        return x

    def step(k, carry):
        start = k * nb
        tile = start // 128
        off = start % 128
        tile_start = pl.multiple_of(tile * 128, 128)
        column = spread(
            jnp.where((lane_t >= off) & (lane_t < off + nb), o_ref[:, pl.ds(tile_start, 128)], 0.0)
        )
        pivot = jnp.sum(jnp.where(row_i == k, column, 0.0), axis=0, keepdims=True)
        base = pl.multiple_of((k // 8) * 8, 8)
        band = o_ref[pl.ds(base, 8), :]
        band_i = lax.broadcasted_iota(jnp.int32, band.shape, 0)
        row = jnp.sum(jnp.where(band_i == k - base, band, 0.0), axis=0, keepdims=True)
        for t in range(tiles):
            in_col = (t == tile) & (lane_r >= off) & (lane_r < off + nb)
            scaled = jnp.where(in_col, 1.0 / pivot, row[:, t * 128:(t + 1) * 128] / pivot)
            kept = jnp.where(in_col, 0.0, o_ref[:, t * 128:(t + 1) * 128])
            o_ref[:, t * 128:(t + 1) * 128] = jnp.where(row_i == k, scaled, kept - column * scaled)
        return carry

    lax.fori_loop(0, n, step, 0)


def block_inverses(matrices):
    nb, n, _ = matrices.shape
    if 128 % nb or (n * nb) % 128:
        lower_factor = jnp.linalg.cholesky(matrices)
        identity = jnp.broadcast_to(jnp.eye(n, dtype=matrices.dtype), matrices.shape)
        solved = jax.scipy.linalg.solve_triangular(lower_factor, identity, lower=True)
        return jnp.einsum("eqp,eqr->epr", solved, solved, precision=lax.Precision.HIGHEST)
    packed = jnp.transpose(matrices, (1, 2, 0)).reshape(n, n * nb)
    inverted = pl.pallas_call(
        functools.partial(_gauss_jordan_kernel, n=n, nb=nb),
        out_shape=jax.ShapeDtypeStruct((n, n * nb), jnp.float32),
        in_specs=[pl.BlockSpec(memory_space=pltpu.VMEM)],
        out_specs=pl.BlockSpec(memory_space=pltpu.VMEM),
    )(packed)
    return jnp.transpose(inverted.reshape(n, n, nb), (2, 0, 1))


def shifted(values, halo, dim, lower):
    width = values.shape[dim]
    if lower:
        return jnp.concatenate([halo, lax.slice_in_dim(values, 0, width - 1, axis=dim)], axis=dim)
    return jnp.concatenate([lax.slice_in_dim(values, 1, width, axis=dim), halo], axis=dim)


def exchange(values, axis, dim):
    count = lax.axis_size(axis)
    forward = [(i, i + 1) for i in range(count - 1)]
    backward = [(target, source) for source, target in forward]
    width = values.shape[dim]
    from_lower = lax.ppermute(lax.slice_in_dim(values, width - 1, width, axis=dim), axis, forward)
    from_upper = lax.ppermute(lax.slice_in_dim(values, 0, 1, axis=dim), axis, backward)
    return from_lower, from_upper


def body(forcing, initial, blocks, face_blocks, strength, strong, colour, neighbours):
    span_x, span_y, span_z, width = forcing.shape
    count = span_x * span_y * span_z
    columns = span_x * span_y
    empty_slot = (span_x + 2) * (span_y + 2) * span_z
    inverse = block_inverses(blocks.reshape(count, P_SIZE, P_SIZE)).reshape(
        span_x, span_y, span_z, P_SIZE, P_SIZE
    )
    weight = jnp.where(neighbours == empty_slot, 0.0, strength * strong.astype(jnp.float32))
    first_is = [colour[:, :, 0] == paint for paint in (0, 1)]

    def pick(values, paint, axis=2):
        lead = (1,) * (axis - 2)
        mask = first_is[paint].reshape(lead + first_is[paint].shape + (1,) * (values.ndim - axis - 1))
        low = lax.index_in_dim(values, 0, axis=axis, keepdims=False)
        high = lax.index_in_dim(values, 1, axis=axis, keepdims=False)
        return jnp.where(mask, low, high)

    member_inverse = [pick(inverse, paint).reshape(columns, P_SIZE, P_SIZE) for paint in (0, 1)]
    member_target = [pick(forcing, paint).reshape(columns, P_SIZE, R) for paint in (0, 1)]
    member_weight = [pick(weight, paint, axis=3)[..., None] for paint in (0, 1)]
    state = [pick(initial, 0), pick(initial, 1)]
    for sweep_index in range(SWEEPS):
        for paint_now in (0, 1):
            other = state[1 - paint_now]
            low_x, high_x = exchange(other, "gx", 0)
            low_y, high_y = exchange(other, "gy", 1)
            nearby = jnp.stack(
                [
                    shifted(other, low_x, 0, True),
                    shifted(other, high_x, 0, False),
                    shifted(other, low_y, 1, True),
                    shifted(other, high_y, 1, False),
                    other,
                    other,
                ]
            )
            nearby = (nearby * member_weight[paint_now]).reshape(6, columns, P_SIZE, R)
            coupled = jnp.einsum(
                "fpq,feqr->epr", face_blocks, nearby, precision=lax.Precision.HIGHEST
            )
            update = jnp.einsum(
                "epq,eqr->epr",
                member_inverse[paint_now],
                member_target[paint_now] - coupled,
                precision=lax.Precision.HIGHEST,
            )
            state[paint_now] = update.reshape(span_x, span_y, width)
    first = first_is[0][..., None]
    return jnp.stack(
        [jnp.where(first, state[0], state[1]), jnp.where(first, state[1], state[0])], axis=2
    )


def solution(mesh):
    in_specs = (
        P("gx", "gy", None, None),
        P("gx", "gy", None, None),
        P("gx", "gy", None, None),
        P(),
        P(None, "gx", "gy", None),
        P(None, "gx", "gy", None),
        P("gx", "gy", None),
        P(None, "gx", "gy", None),
    )
    out_specs = P("gx", "gy", None, None)
    return jax.shard_map(body, mesh=mesh, in_specs=in_specs, out_specs=out_specs, check_vma=False)
```

```python
import functools

import jax
import jax.numpy as jnp
from jax import lax
from jax.experimental import pallas as pl
from jax.experimental.pallas import tpu as pltpu
from jax.sharding import PartitionSpec as P

P_SIZE = 64
R = 64
SWEEPS = 4


def padded(block, sides, width):
    for axis, dim in sides:
        count = lax.axis_size(axis)
        forward = [(i, i + 1) for i in range(count - 1)]
        backward = [(target, source) for source, target in forward]
        low = lax.ppermute(
            lax.slice_in_dim(block, block.shape[dim] - width, None, axis=dim), axis, forward
        )
        high = lax.ppermute(lax.slice_in_dim(block, 0, width, axis=dim), axis, backward)
        block = jnp.concatenate([low, block, high], axis=dim)
    return block


def _gauss_jordan_kernel(a_ref, o_ref, *, n, nb):
    lanes = n * nb
    tiles = lanes // 128
    o_ref[...] = a_ref[...]
    lane_t = lax.broadcasted_iota(jnp.int32, (n, 128), 1)
    lane_r = lax.broadcasted_iota(jnp.int32, (1, 128), 1)
    row_i = lax.broadcasted_iota(jnp.int32, (n, 128), 0)

    def spread(x):
        shift = nb
        while shift < 128:
            x = x + pltpu.roll(x, shift, 1)
            shift *= 2
        return x

    def step(k, carry):
        start = k * nb
        tile = start // 128
        off = start % 128
        tile_start = pl.multiple_of(tile * 128, 128)
        column = spread(
            jnp.where((lane_t >= off) & (lane_t < off + nb), o_ref[:, pl.ds(tile_start, 128)], 0.0)
        )
        pivot = jnp.sum(jnp.where(row_i == k, column, 0.0), axis=0, keepdims=True)
        base = pl.multiple_of((k // 8) * 8, 8)
        band = o_ref[pl.ds(base, 8), :]
        band_i = lax.broadcasted_iota(jnp.int32, band.shape, 0)
        row = jnp.sum(jnp.where(band_i == k - base, band, 0.0), axis=0, keepdims=True)
        for t in range(tiles):
            in_col = (t == tile) & (lane_r >= off) & (lane_r < off + nb)
            scaled = jnp.where(in_col, 1.0 / pivot, row[:, t * 128:(t + 1) * 128] / pivot)
            kept = jnp.where(in_col, 0.0, o_ref[:, t * 128:(t + 1) * 128])
            o_ref[:, t * 128:(t + 1) * 128] = jnp.where(row_i == k, scaled, kept - column * scaled)
        return carry

    lax.fori_loop(0, n, step, 0)


def block_inverses(matrices):
    nb, n, _ = matrices.shape
    if 128 % nb or (n * nb) % 128:
        lower_factor = jnp.linalg.cholesky(matrices)
        identity = jnp.broadcast_to(jnp.eye(n, dtype=matrices.dtype), matrices.shape)
        solved = jax.scipy.linalg.solve_triangular(lower_factor, identity, lower=True)
        return jnp.einsum("eqp,eqr->epr", solved, solved, precision=lax.Precision.HIGHEST)
    packed = jnp.transpose(matrices, (1, 2, 0)).reshape(n, n * nb)
    inverted = pl.pallas_call(
        functools.partial(_gauss_jordan_kernel, n=n, nb=nb),
        out_shape=jax.ShapeDtypeStruct((n, n * nb), jnp.float32),
        in_specs=[pl.BlockSpec(memory_space=pltpu.VMEM)],
        out_specs=pl.BlockSpec(memory_space=pltpu.VMEM),
    )(packed)
    return jnp.transpose(inverted.reshape(n, n, nb), (2, 0, 1))


def shifted(values, halo, dim, lower):
    width = values.shape[dim]
    if lower:
        return jnp.concatenate([halo, lax.slice_in_dim(values, 0, width - 1, axis=dim)], axis=dim)
    return jnp.concatenate([lax.slice_in_dim(values, 1, width, axis=dim), halo], axis=dim)


def exchange(values, axis, dim):
    count = lax.axis_size(axis)
    forward = [(i, i + 1) for i in range(count - 1)]
    backward = [(target, source) for source, target in forward]
    width = values.shape[dim]
    from_lower = lax.ppermute(lax.slice_in_dim(values, width - 1, width, axis=dim), axis, forward)
    from_upper = lax.ppermute(lax.slice_in_dim(values, 0, 1, axis=dim), axis, backward)
    return from_lower, from_upper


def body(forcing, initial, blocks, face_blocks, strength, strong, colour, neighbours):
    span_x, span_y, span_z, width = forcing.shape
    count = span_x * span_y * span_z
    columns = span_x * span_y
    empty_slot = (span_x + 2) * (span_y + 2) * span_z
    inverse = block_inverses(blocks.reshape(count, P_SIZE, P_SIZE)).reshape(
        span_x, span_y, span_z, P_SIZE, P_SIZE
    )
    weight = jnp.where(neighbours == empty_slot, 0.0, strength * strong.astype(jnp.float32))
    first_is = [colour[:, :, 0] == paint for paint in (0, 1)]

    def pick(values, paint, axis=2):
        lead = (1,) * (axis - 2)
        mask = first_is[paint].reshape(lead + first_is[paint].shape + (1,) * (values.ndim - axis - 1))
        low = lax.index_in_dim(values, 0, axis=axis, keepdims=False)
        high = lax.index_in_dim(values, 1, axis=axis, keepdims=False)
        return jnp.where(mask, low, high)

    member_inverse = [pick(inverse, paint).reshape(columns, P_SIZE, P_SIZE) for paint in (0, 1)]
    member_target = [pick(forcing, paint).reshape(columns, P_SIZE, R) for paint in (0, 1)]
    member_weight = [pick(weight, paint, axis=3)[..., None] for paint in (0, 1)]
    state = [pick(initial, 0), pick(initial, 1)]
    for sweep_index in range(SWEEPS):
        for paint_now in (0, 1):
            other = state[1 - paint_now]
            low_x, high_x = exchange(other, "gx", 0)
            low_y, high_y = exchange(other, "gy", 1)
            nearby = jnp.stack(
                [
                    shifted(other, low_x, 0, True),
                    shifted(other, high_x, 0, False),
                    shifted(other, low_y, 1, True),
                    shifted(other, high_y, 1, False),
                    other,
                    other,
                ]
            )
            nearby = (nearby * member_weight[paint_now]).reshape(6, columns, P_SIZE, R)
            coupled = jnp.einsum(
                "fpq,feqr->epr", face_blocks, nearby, precision=lax.Precision.HIGHEST
            )
            update = jnp.einsum(
                "epq,eqr->epr",
                member_inverse[paint_now],
                member_target[paint_now] - coupled,
                precision=lax.Precision.HIGHEST,
            )
            state[paint_now] = update.reshape(span_x, span_y, width)
    first = first_is[0][..., None]
    return jnp.stack(
        [jnp.where(first, state[0], state[1]), jnp.where(first, state[1], state[0])], axis=2
    )


def _half_sweep_kernel(
    other_ref, lo_x_ref, hi_x_ref, lo_y_ref, hi_y_ref, face_ref, weight_ref, inverse_ref,
    target_ref, out_ref, send_lo_x_ref, send_hi_x_ref, send_lo_y_ref, send_hi_y_ref, *, span_x
):
    tile = 2 * R
    highest = lax.Precision.HIGHEST
    other = other_ref[...]
    lanes = other.shape[1]
    lane = lax.broadcasted_iota(jnp.int32, (P_SIZE, tile), 1)
    low_half = lane < R
    tiles = [other[:, t * tile:(t + 1) * tile] for t in range(span_x)]
    lo_y = lo_y_ref[...]
    hi_y = hi_y_ref[...]

    def y_block(packed, x):
        held = packed[:, (x // 2) * tile:(x // 2 + 1) * tile]
        return held if x % 2 == 0 else pltpu.roll(held, R, 1)

    below, above = [], []
    for x in range(span_x):
        rolled = pltpu.roll(tiles[x], R, 1)
        below.append(jnp.where(low_half, y_block(lo_y, x), rolled))
        above.append(jnp.where(low_half, rolled, pltpu.roll(y_block(hi_y, x), R, 1)))
    nearby = [
        jnp.concatenate([lo_x_ref[...], other[:, :lanes - tile]], axis=1),
        jnp.concatenate([other[:, tile:], hi_x_ref[...]], axis=1),
        jnp.concatenate(below, axis=1),
        jnp.concatenate(above, axis=1),
        other,
        other,
    ]
    coupled = jnp.zeros_like(other)
    for face in range(6):
        product = jnp.dot(
            face_ref[face], nearby[face], precision=highest, preferred_element_type=jnp.float32
        )
        coupled = coupled + weight_ref[face] * product
    rhs = target_ref[...] - coupled
    outs = []
    for x in range(span_x):
        part = rhs[:, x * tile:(x + 1) * tile]
        first = jnp.dot(inverse_ref[2 * x], part, precision=highest, preferred_element_type=jnp.float32)
        second = jnp.dot(
            inverse_ref[2 * x + 1], part, precision=highest, preferred_element_type=jnp.float32
        )
        outs.append(jnp.where(low_half, first, second))
    out_ref[...] = jnp.concatenate(outs, axis=1)
    send_lo_x_ref[...] = outs[-1]
    send_hi_x_ref[...] = outs[0]
    for t in range(span_x // 2):
        even, odd = outs[2 * t], outs[2 * t + 1]
        send_lo_y_ref[:, t * tile:(t + 1) * tile] = jnp.where(low_half, pltpu.roll(even, R, 1), odd)
        send_hi_y_ref[:, t * tile:(t + 1) * tile] = jnp.where(low_half, even, pltpu.roll(odd, R, 1))


def half_sweep(other, halos, face_blocks, weight, inverse, target, span_x):
    lanes = other.shape[1]
    x_shape = jax.ShapeDtypeStruct((P_SIZE, 2 * R), jnp.float32)
    y_shape = jax.ShapeDtypeStruct((P_SIZE, span_x * R), jnp.float32)
    vmem = pl.BlockSpec(memory_space=pltpu.VMEM)
    return pl.pallas_call(
        functools.partial(_half_sweep_kernel, span_x=span_x),
        out_shape=(jax.ShapeDtypeStruct((P_SIZE, lanes), jnp.float32), x_shape, x_shape, y_shape, y_shape),
        in_specs=[vmem] * 9,
        out_specs=(vmem,) * 5,
    )(other, *halos, face_blocks, weight, inverse, target)


def send_buffers(state, span_x):
    blocks = state.reshape(P_SIZE, span_x, 2, R)
    return (
        blocks[:, -1].reshape(P_SIZE, 2 * R),
        blocks[:, 0].reshape(P_SIZE, 2 * R),
        blocks[:, :, 1].reshape(P_SIZE, span_x * R),
        blocks[:, :, 0].reshape(P_SIZE, span_x * R),
    )


def trade(sends):
    lo_x, hi_x = (
        lax.ppermute(sends[0], "gx", shift_pairs("gx", 1)),
        lax.ppermute(sends[1], "gx", shift_pairs("gx", -1)),
    )
    lo_y, hi_y = (
        lax.ppermute(sends[2], "gy", shift_pairs("gy", 1)),
        lax.ppermute(sends[3], "gy", shift_pairs("gy", -1)),
    )
    return lo_x, hi_x, lo_y, hi_y


def shift_pairs(axis, step):
    count = lax.axis_size(axis)
    return [(i, i + step) for i in range(count) if 0 <= i + step < count]


def lane_body(forcing, initial, blocks, face_blocks, strength, strong, colour, neighbours):
    span_x, span_y, span_z, width = forcing.shape
    count = span_x * span_y * span_z
    columns = span_x * span_y
    empty_slot = (span_x + 2) * (span_y + 2) * span_z
    inverse = block_inverses(blocks.reshape(count, P_SIZE, P_SIZE)).reshape(
        span_x, span_y, span_z, P_SIZE, P_SIZE
    )
    weight = jnp.where(neighbours == empty_slot, 0.0, strength * strong.astype(jnp.float32))
    first_is = [colour[:, :, 0] == paint for paint in (0, 1)]

    def pick(values, paint, axis=2):
        lead = (1,) * (axis - 2)
        mask = first_is[paint].reshape(lead + first_is[paint].shape + (1,) * (values.ndim - axis - 1))
        low = lax.index_in_dim(values, 0, axis=axis, keepdims=False)
        high = lax.index_in_dim(values, 1, axis=axis, keepdims=False)
        return jnp.where(mask, low, high)

    def to_lanes(values):
        return jnp.transpose(values.reshape(columns, P_SIZE, R), (1, 0, 2)).reshape(P_SIZE, columns * R)

    member_inverse = [pick(inverse, paint).reshape(columns, P_SIZE, P_SIZE) for paint in (0, 1)]
    member_target = [to_lanes(pick(forcing, paint)) for paint in (0, 1)]
    member_weight = [
        jnp.repeat(pick(weight, paint, axis=3).reshape(6, columns), R, axis=1).reshape(6, 1, columns * R)
        for paint in (0, 1)
    ]
    state = [None, to_lanes(pick(initial, 1))]
    sends = send_buffers(state[1], span_x)
    for sweep_index in range(SWEEPS):
        for paint_now in (0, 1):
            halos = trade(sends)
            state[paint_now], *sends = half_sweep(
                state[1 - paint_now],
                halos,
                face_blocks,
                member_weight[paint_now],
                member_inverse[paint_now],
                member_target[paint_now],
                span_x,
            )
    first = first_is[0][..., None]
    whole = [
        jnp.transpose(part.reshape(P_SIZE, columns, R), (1, 0, 2)).reshape(span_x, span_y, width)
        for part in state
    ]
    return jnp.stack(
        [jnp.where(first, whole[0], whole[1]), jnp.where(first, whole[1], whole[0])], axis=2
    )


def dispatch(forcing, *rest):
    span_x, span_y, span_z, width = forcing.shape
    if span_y == 2 and span_z == 2 and span_x % 2 == 0 and width == P_SIZE * R:
        return lane_body(forcing, *rest)
    return body(forcing, *rest)


def solution(mesh):
    in_specs = (
        P("gx", "gy", None, None),
        P("gx", "gy", None, None),
        P("gx", "gy", None, None),
        P(),
        P(None, "gx", "gy", None),
        P(None, "gx", "gy", None),
        P("gx", "gy", None),
        P(None, "gx", "gy", None),
    )
    out_specs = P("gx", "gy", None, None)
    return jax.shard_map(dispatch, mesh=mesh, in_specs=in_specs, out_specs=out_specs, check_vma=False)
```

```python
import functools

import jax
import jax.numpy as jnp
from jax import lax
from jax.experimental import pallas as pl
from jax.experimental.pallas import tpu as pltpu
from jax.sharding import PartitionSpec as P

P_SIZE = 64
R = 64
SWEEPS = 4


def padded(block, sides, width):
    for axis, dim in sides:
        count = lax.axis_size(axis)
        forward = [(i, i + 1) for i in range(count - 1)]
        backward = [(target, source) for source, target in forward]
        low = lax.ppermute(
            lax.slice_in_dim(block, block.shape[dim] - width, None, axis=dim), axis, forward
        )
        high = lax.ppermute(lax.slice_in_dim(block, 0, width, axis=dim), axis, backward)
        block = jnp.concatenate([low, block, high], axis=dim)
    return block


def _gauss_jordan_kernel(a_ref, o_ref, *, n, nb):
    lanes = n * nb
    tiles = lanes // 128
    o_ref[...] = a_ref[...]
    lane_t = lax.broadcasted_iota(jnp.int32, (n, 128), 1)
    lane_r = lax.broadcasted_iota(jnp.int32, (1, 128), 1)
    row_i = lax.broadcasted_iota(jnp.int32, (n, 128), 0)

    def spread(x):
        shift = nb
        while shift < 128:
            x = x + pltpu.roll(x, shift, 1)
            shift *= 2
        return x

    def step(k, carry):
        start = k * nb
        tile = start // 128
        off = start % 128
        tile_start = pl.multiple_of(tile * 128, 128)
        column = spread(
            jnp.where((lane_t >= off) & (lane_t < off + nb), o_ref[:, pl.ds(tile_start, 128)], 0.0)
        )
        pivot = jnp.sum(jnp.where(row_i == k, column, 0.0), axis=0, keepdims=True)
        base = pl.multiple_of((k // 8) * 8, 8)
        band = o_ref[pl.ds(base, 8), :]
        band_i = lax.broadcasted_iota(jnp.int32, band.shape, 0)
        row = jnp.sum(jnp.where(band_i == k - base, band, 0.0), axis=0, keepdims=True)
        for t in range(tiles):
            in_col = (t == tile) & (lane_r >= off) & (lane_r < off + nb)
            scaled = jnp.where(in_col, 1.0 / pivot, row[:, t * 128:(t + 1) * 128] / pivot)
            kept = jnp.where(in_col, 0.0, o_ref[:, t * 128:(t + 1) * 128])
            o_ref[:, t * 128:(t + 1) * 128] = jnp.where(row_i == k, scaled, kept - column * scaled)
        return carry

    lax.fori_loop(0, n, step, 0)


def block_inverses(matrices):
    nb, n, _ = matrices.shape
    if 128 % nb or (n * nb) % 128:
        lower_factor = jnp.linalg.cholesky(matrices)
        identity = jnp.broadcast_to(jnp.eye(n, dtype=matrices.dtype), matrices.shape)
        solved = jax.scipy.linalg.solve_triangular(lower_factor, identity, lower=True)
        return jnp.einsum("eqp,eqr->epr", solved, solved, precision=lax.Precision.HIGHEST)
    packed = jnp.transpose(matrices, (1, 2, 0)).reshape(n, n * nb)
    inverted = pl.pallas_call(
        functools.partial(_gauss_jordan_kernel, n=n, nb=nb),
        out_shape=jax.ShapeDtypeStruct((n, n * nb), jnp.float32),
        in_specs=[pl.BlockSpec(memory_space=pltpu.VMEM)],
        out_specs=pl.BlockSpec(memory_space=pltpu.VMEM),
        cost_estimate=pl.CostEstimate(
            flops=2000 * n ** 3 * nb, transcendentals=0, bytes_accessed=8 * n * n * nb
        ),
    )(packed)
    return jnp.transpose(inverted.reshape(n, n, nb), (2, 0, 1))


def shifted(values, halo, dim, lower):
    width = values.shape[dim]
    if lower:
        return jnp.concatenate([halo, lax.slice_in_dim(values, 0, width - 1, axis=dim)], axis=dim)
    return jnp.concatenate([lax.slice_in_dim(values, 1, width, axis=dim), halo], axis=dim)


def exchange(values, axis, dim):
    count = lax.axis_size(axis)
    forward = [(i, i + 1) for i in range(count - 1)]
    backward = [(target, source) for source, target in forward]
    width = values.shape[dim]
    from_lower = lax.ppermute(lax.slice_in_dim(values, width - 1, width, axis=dim), axis, forward)
    from_upper = lax.ppermute(lax.slice_in_dim(values, 0, 1, axis=dim), axis, backward)
    return from_lower, from_upper


def body(forcing, initial, blocks, face_blocks, strength, strong, colour, neighbours):
    span_x, span_y, span_z, width = forcing.shape
    count = span_x * span_y * span_z
    columns = span_x * span_y
    empty_slot = (span_x + 2) * (span_y + 2) * span_z
    inverse = block_inverses(blocks.reshape(count, P_SIZE, P_SIZE)).reshape(
        span_x, span_y, span_z, P_SIZE, P_SIZE
    )
    weight = jnp.where(neighbours == empty_slot, 0.0, strength * strong.astype(jnp.float32))
    first_is = [colour[:, :, 0] == paint for paint in (0, 1)]

    def pick(values, paint, axis=2):
        lead = (1,) * (axis - 2)
        mask = first_is[paint].reshape(lead + first_is[paint].shape + (1,) * (values.ndim - axis - 1))
        low = lax.index_in_dim(values, 0, axis=axis, keepdims=False)
        high = lax.index_in_dim(values, 1, axis=axis, keepdims=False)
        return jnp.where(mask, low, high)

    member_inverse = [pick(inverse, paint).reshape(columns, P_SIZE, P_SIZE) for paint in (0, 1)]
    member_target = [pick(forcing, paint).reshape(columns, P_SIZE, R) for paint in (0, 1)]
    member_weight = [pick(weight, paint, axis=3)[..., None] for paint in (0, 1)]
    state = [pick(initial, 0), pick(initial, 1)]
    for sweep_index in range(SWEEPS):
        for paint_now in (0, 1):
            other = state[1 - paint_now]
            low_x, high_x = exchange(other, "gx", 0)
            low_y, high_y = exchange(other, "gy", 1)
            nearby = jnp.stack(
                [
                    shifted(other, low_x, 0, True),
                    shifted(other, high_x, 0, False),
                    shifted(other, low_y, 1, True),
                    shifted(other, high_y, 1, False),
                    other,
                    other,
                ]
            )
            nearby = (nearby * member_weight[paint_now]).reshape(6, columns, P_SIZE, R)
            coupled = jnp.einsum(
                "fpq,feqr->epr", face_blocks, nearby, precision=lax.Precision.HIGHEST
            )
            update = jnp.einsum(
                "epq,eqr->epr",
                member_inverse[paint_now],
                member_target[paint_now] - coupled,
                precision=lax.Precision.HIGHEST,
            )
            state[paint_now] = update.reshape(span_x, span_y, width)
    first = first_is[0][..., None]
    return jnp.stack(
        [jnp.where(first, state[0], state[1]), jnp.where(first, state[1], state[0])], axis=2
    )


def _half_sweep_kernel(
    other_ref, lo_x_ref, hi_x_ref, lo_y_ref, hi_y_ref, face_ref, weight_ref, inverse_ref,
    target_ref, out_ref, send_lo_x_ref, send_hi_x_ref, send_lo_y_ref, send_hi_y_ref, *, span_x
):
    tile = 2 * R
    highest = lax.Precision.HIGHEST
    other = other_ref[...]
    lanes = other.shape[1]
    lane = lax.broadcasted_iota(jnp.int32, (P_SIZE, tile), 1)
    low_half = lane < R
    tiles = [other[:, t * tile:(t + 1) * tile] for t in range(span_x)]
    lo_y = lo_y_ref[...]
    hi_y = hi_y_ref[...]

    def y_block(packed, x):
        held = packed[:, (x // 2) * tile:(x // 2 + 1) * tile]
        return held if x % 2 == 0 else pltpu.roll(held, R, 1)

    below, above = [], []
    for x in range(span_x):
        rolled = pltpu.roll(tiles[x], R, 1)
        below.append(jnp.where(low_half, y_block(lo_y, x), rolled))
        above.append(jnp.where(low_half, rolled, pltpu.roll(y_block(hi_y, x), R, 1)))
    nearby = [
        jnp.concatenate([lo_x_ref[...], other[:, :lanes - tile]], axis=1),
        jnp.concatenate([other[:, tile:], hi_x_ref[...]], axis=1),
        jnp.concatenate(below, axis=1),
        jnp.concatenate(above, axis=1),
        other,
        other,
    ]
    coupled = jnp.zeros_like(other)
    for face in range(6):
        product = jnp.dot(
            face_ref[face], nearby[face], precision=highest, preferred_element_type=jnp.float32
        )
        coupled = coupled + weight_ref[face] * product
    rhs = target_ref[...] - coupled
    outs = []
    for x in range(span_x):
        part = rhs[:, x * tile:(x + 1) * tile]
        first = jnp.dot(inverse_ref[2 * x], part, precision=highest, preferred_element_type=jnp.float32)
        second = jnp.dot(
            inverse_ref[2 * x + 1], part, precision=highest, preferred_element_type=jnp.float32
        )
        outs.append(jnp.where(low_half, first, second))
    out_ref[...] = jnp.concatenate(outs, axis=1)
    send_lo_x_ref[...] = outs[-1]
    send_hi_x_ref[...] = outs[0]
    for t in range(span_x // 2):
        even, odd = outs[2 * t], outs[2 * t + 1]
        send_lo_y_ref[:, t * tile:(t + 1) * tile] = jnp.where(low_half, pltpu.roll(even, R, 1), odd)
        send_hi_y_ref[:, t * tile:(t + 1) * tile] = jnp.where(low_half, even, pltpu.roll(odd, R, 1))


def half_sweep(other, halos, face_blocks, weight, inverse, target, span_x):
    lanes = other.shape[1]
    x_shape = jax.ShapeDtypeStruct((P_SIZE, 2 * R), jnp.float32)
    y_shape = jax.ShapeDtypeStruct((P_SIZE, span_x * R), jnp.float32)
    vmem = pl.BlockSpec(memory_space=pltpu.VMEM)
    return pl.pallas_call(
        functools.partial(_half_sweep_kernel, span_x=span_x),
        out_shape=(jax.ShapeDtypeStruct((P_SIZE, lanes), jnp.float32), x_shape, x_shape, y_shape, y_shape),
        in_specs=[vmem] * 9,
        out_specs=(vmem,) * 5,
    )(other, *halos, face_blocks, weight, inverse, target)


def send_buffers(state, span_x):
    blocks = state.reshape(P_SIZE, span_x, 2, R)
    return (
        blocks[:, -1].reshape(P_SIZE, 2 * R),
        blocks[:, 0].reshape(P_SIZE, 2 * R),
        blocks[:, :, 1].reshape(P_SIZE, span_x * R),
        blocks[:, :, 0].reshape(P_SIZE, span_x * R),
    )


def trade(sends):
    lo_x, hi_x = (
        lax.ppermute(sends[0], "gx", shift_pairs("gx", 1)),
        lax.ppermute(sends[1], "gx", shift_pairs("gx", -1)),
    )
    lo_y, hi_y = (
        lax.ppermute(sends[2], "gy", shift_pairs("gy", 1)),
        lax.ppermute(sends[3], "gy", shift_pairs("gy", -1)),
    )
    return lo_x, hi_x, lo_y, hi_y


def shift_pairs(axis, step):
    count = lax.axis_size(axis)
    return [(i, (i + step) % count) for i in range(count)]


def lane_body(forcing, initial, blocks, face_blocks, strength, strong, colour, neighbours):
    span_x, span_y, span_z, width = forcing.shape
    count = span_x * span_y * span_z
    columns = span_x * span_y
    empty_slot = (span_x + 2) * (span_y + 2) * span_z
    first_is = [colour[:, :, 0] == paint for paint in (0, 1)]

    def pick(values, paint, axis=2):
        lead = (1,) * (axis - 2)
        mask = first_is[paint].reshape(lead + first_is[paint].shape + (1,) * (values.ndim - axis - 1))
        low = lax.index_in_dim(values, 0, axis=axis, keepdims=False)
        high = lax.index_in_dim(values, 1, axis=axis, keepdims=False)
        return jnp.where(mask, low, high)

    def to_lanes(values):
        return jnp.transpose(values.reshape(columns, P_SIZE, R), (1, 0, 2)).reshape(P_SIZE, columns * R)

    start_state = to_lanes(pick(initial, 1))
    first_halos = trade(send_buffers(start_state, span_x))
    inverse = block_inverses(blocks.reshape(count, P_SIZE, P_SIZE)).reshape(
        span_x, span_y, span_z, P_SIZE, P_SIZE
    )
    weight = jnp.where(neighbours == empty_slot, 0.0, strength * strong.astype(jnp.float32))
    member_inverse = [pick(inverse, paint).reshape(columns, P_SIZE, P_SIZE) for paint in (0, 1)]
    member_target = [to_lanes(pick(forcing, paint)) for paint in (0, 1)]
    member_weight = [
        jnp.repeat(pick(weight, paint, axis=3).reshape(6, columns), R, axis=1).reshape(6, 1, columns * R)
        for paint in (0, 1)
    ]
    state = [None, start_state]
    sends = None
    for sweep_index in range(SWEEPS):
        for paint_now in (0, 1):
            halos = first_halos if sends is None else trade(sends)
            state[paint_now], *sends = half_sweep(
                state[1 - paint_now],
                halos,
                face_blocks,
                member_weight[paint_now],
                member_inverse[paint_now],
                member_target[paint_now],
                span_x,
            )
    first = first_is[0][..., None]
    whole = [
        jnp.transpose(part.reshape(P_SIZE, columns, R), (1, 0, 2)).reshape(span_x, span_y, width)
        for part in state
    ]
    return jnp.stack(
        [jnp.where(first, whole[0], whole[1]), jnp.where(first, whole[1], whole[0])], axis=2
    )


def dispatch(forcing, *rest):
    span_x, span_y, span_z, width = forcing.shape
    if span_y == 2 and span_z == 2 and span_x % 2 == 0 and width == P_SIZE * R:
        return lane_body(forcing, *rest)
    return body(forcing, *rest)


def solution(mesh):
    in_specs = (
        P("gx", "gy", None, None),
        P("gx", "gy", None, None),
        P("gx", "gy", None, None),
        P(),
        P(None, "gx", "gy", None),
        P(None, "gx", "gy", None),
        P("gx", "gy", None),
        P(None, "gx", "gy", None),
    )
    out_specs = P("gx", "gy", None, None)
    return jax.shard_map(dispatch, mesh=mesh, in_specs=in_specs, out_specs=out_specs, check_vma=False)
```

```python
import functools

import jax
import jax.numpy as jnp
from jax import lax
from jax.experimental import pallas as pl
from jax.experimental.pallas import tpu as pltpu
from jax.sharding import PartitionSpec as P

P_SIZE = 64
R = 64
SWEEPS = 4


def padded(block, sides, width):
    for axis, dim in sides:
        count = lax.axis_size(axis)
        forward = [(i, i + 1) for i in range(count - 1)]
        backward = [(target, source) for source, target in forward]
        low = lax.ppermute(
            lax.slice_in_dim(block, block.shape[dim] - width, None, axis=dim), axis, forward
        )
        high = lax.ppermute(lax.slice_in_dim(block, 0, width, axis=dim), axis, backward)
        block = jnp.concatenate([low, block, high], axis=dim)
    return block


def _gauss_jordan_kernel(a_ref, o_ref, *, n, nb):
    lanes = n * nb
    tiles = lanes // 128
    o_ref[...] = a_ref[...]
    lane_t = lax.broadcasted_iota(jnp.int32, (n, 128), 1)
    lane_r = lax.broadcasted_iota(jnp.int32, (1, 128), 1)
    row_i = lax.broadcasted_iota(jnp.int32, (n, 128), 0)

    def spread(x):
        shift = nb
        while shift < 128:
            x = x + pltpu.roll(x, shift, 1)
            shift *= 2
        return x

    def step(k, carry):
        start = k * nb
        tile = start // 128
        off = start % 128
        tile_start = pl.multiple_of(tile * 128, 128)
        column = spread(
            jnp.where((lane_t >= off) & (lane_t < off + nb), o_ref[:, pl.ds(tile_start, 128)], 0.0)
        )
        pivot = jnp.sum(jnp.where(row_i == k, column, 0.0), axis=0, keepdims=True)
        base = pl.multiple_of((k // 8) * 8, 8)
        band = o_ref[pl.ds(base, 8), :]
        band_i = lax.broadcasted_iota(jnp.int32, band.shape, 0)
        row = jnp.sum(jnp.where(band_i == k - base, band, 0.0), axis=0, keepdims=True)
        for t in range(tiles):
            in_col = (t == tile) & (lane_r >= off) & (lane_r < off + nb)
            scaled = jnp.where(in_col, 1.0 / pivot, row[:, t * 128:(t + 1) * 128] / pivot)
            kept = jnp.where(in_col, 0.0, o_ref[:, t * 128:(t + 1) * 128])
            o_ref[:, t * 128:(t + 1) * 128] = jnp.where(row_i == k, scaled, kept - column * scaled)
        return carry

    lax.fori_loop(0, n, step, 0)


def block_inverses(matrices, lanes_out=False):
    nb, n, _ = matrices.shape
    if 128 % nb or (n * nb) % 128:
        assert not lanes_out
        lower_factor = jnp.linalg.cholesky(matrices)
        identity = jnp.broadcast_to(jnp.eye(n, dtype=matrices.dtype), matrices.shape)
        solved = jax.scipy.linalg.solve_triangular(lower_factor, identity, lower=True)
        return jnp.einsum("eqp,eqr->epr", solved, solved, precision=lax.Precision.HIGHEST)
    packed = jnp.transpose(matrices, (1, 2, 0)).reshape(n, n * nb)
    inverted = pl.pallas_call(
        functools.partial(_gauss_jordan_kernel, n=n, nb=nb),
        out_shape=jax.ShapeDtypeStruct((n, n * nb), jnp.float32),
        in_specs=[pl.BlockSpec(memory_space=pltpu.VMEM)],
        out_specs=pl.BlockSpec(memory_space=pltpu.VMEM),
        cost_estimate=pl.CostEstimate(
            flops=2000 * n ** 3 * nb, transcendentals=0, bytes_accessed=8 * n * n * nb
        ),
    )(packed)
    if lanes_out:
        return jnp.transpose(inverted.reshape(n, n, nb), (0, 2, 1)).reshape(n, nb * n)
    return jnp.transpose(inverted.reshape(n, n, nb), (2, 0, 1))


def shifted(values, halo, dim, lower):
    width = values.shape[dim]
    if lower:
        return jnp.concatenate([halo, lax.slice_in_dim(values, 0, width - 1, axis=dim)], axis=dim)
    return jnp.concatenate([lax.slice_in_dim(values, 1, width, axis=dim), halo], axis=dim)


def exchange(values, axis, dim):
    count = lax.axis_size(axis)
    forward = [(i, i + 1) for i in range(count - 1)]
    backward = [(target, source) for source, target in forward]
    width = values.shape[dim]
    from_lower = lax.ppermute(lax.slice_in_dim(values, width - 1, width, axis=dim), axis, forward)
    from_upper = lax.ppermute(lax.slice_in_dim(values, 0, 1, axis=dim), axis, backward)
    return from_lower, from_upper


def body(forcing, initial, blocks, face_blocks, strength, strong, colour, neighbours):
    span_x, span_y, span_z, width = forcing.shape
    count = span_x * span_y * span_z
    columns = span_x * span_y
    empty_slot = (span_x + 2) * (span_y + 2) * span_z
    inverse = block_inverses(blocks.reshape(count, P_SIZE, P_SIZE)).reshape(
        span_x, span_y, span_z, P_SIZE, P_SIZE
    )
    weight = jnp.where(neighbours == empty_slot, 0.0, strength * strong.astype(jnp.float32))
    first_is = [colour[:, :, 0] == paint for paint in (0, 1)]

    def pick(values, paint, axis=2):
        lead = (1,) * (axis - 2)
        mask = first_is[paint].reshape(lead + first_is[paint].shape + (1,) * (values.ndim - axis - 1))
        low = lax.index_in_dim(values, 0, axis=axis, keepdims=False)
        high = lax.index_in_dim(values, 1, axis=axis, keepdims=False)
        return jnp.where(mask, low, high)

    member_inverse = [inverse[:, paint * columns * P_SIZE:(paint + 1) * columns * P_SIZE] for paint in (0, 1)]
    face_row = jnp.transpose(face_blocks, (1, 0, 2)).reshape(P_SIZE, 6 * P_SIZE)
    member_target = [pick(forcing, paint).reshape(columns, P_SIZE, R) for paint in (0, 1)]
    member_weight = [pick(weight, paint, axis=3)[..., None] for paint in (0, 1)]
    state = [pick(initial, 0), pick(initial, 1)]
    for sweep_index in range(SWEEPS):
        for paint_now in (0, 1):
            other = state[1 - paint_now]
            low_x, high_x = exchange(other, "gx", 0)
            low_y, high_y = exchange(other, "gy", 1)
            nearby = jnp.stack(
                [
                    shifted(other, low_x, 0, True),
                    shifted(other, high_x, 0, False),
                    shifted(other, low_y, 1, True),
                    shifted(other, high_y, 1, False),
                    other,
                    other,
                ]
            )
            nearby = (nearby * member_weight[paint_now]).reshape(6, columns, P_SIZE, R)
            coupled = jnp.einsum(
                "fpq,feqr->epr", face_blocks, nearby, precision=lax.Precision.HIGHEST
            )
            update = jnp.einsum(
                "epq,eqr->epr",
                member_inverse[paint_now],
                member_target[paint_now] - coupled,
                precision=lax.Precision.HIGHEST,
            )
            state[paint_now] = update.reshape(span_x, span_y, width)
    first = first_is[0][..., None]
    return jnp.stack(
        [jnp.where(first, state[0], state[1]), jnp.where(first, state[1], state[0])], axis=2
    )


def _half_sweep_kernel(
    other_ref, lo_x_ref, hi_x_ref, lo_y_ref, hi_y_ref, face_ref, weight_ref, inverse_ref,
    target_ref, out_ref, send_lo_x_ref, send_hi_x_ref, send_lo_y_ref, send_hi_y_ref, *, span_x
):
    tile = 2 * R
    highest = lax.Precision.HIGHEST
    other = other_ref[...]
    lanes = other.shape[1]
    lane = lax.broadcasted_iota(jnp.int32, (P_SIZE, tile), 1)
    low_half = lane < R
    tiles = [other[:, t * tile:(t + 1) * tile] for t in range(span_x)]
    lo_y = lo_y_ref[...]
    hi_y = hi_y_ref[...]

    def y_block(packed, x):
        held = packed[:, (x // 2) * tile:(x // 2 + 1) * tile]
        return held if x % 2 == 0 else pltpu.roll(held, R, 1)

    below, above = [], []
    for x in range(span_x):
        rolled = pltpu.roll(tiles[x], R, 1)
        below.append(jnp.where(low_half, y_block(lo_y, x), rolled))
        above.append(jnp.where(low_half, rolled, pltpu.roll(y_block(hi_y, x), R, 1)))
    nearby = [
        jnp.concatenate([lo_x_ref[...], other[:, :lanes - tile]], axis=1),
        jnp.concatenate([other[:, tile:], hi_x_ref[...]], axis=1),
        jnp.concatenate(below, axis=1),
        jnp.concatenate(above, axis=1),
        other,
        other,
    ]
    stacked = jnp.concatenate([weight_ref[face] * nearby[face] for face in range(6)], axis=0)
    coupled = jnp.dot(face_ref[...], stacked, precision=highest, preferred_element_type=jnp.float32)
    rhs = target_ref[...] - coupled
    outs = []
    for x in range(span_x):
        part = rhs[:, x * tile:(x + 1) * tile]
        split = jnp.concatenate([jnp.where(low_half, part, 0.0), jnp.where(low_half, 0.0, part)], axis=0)
        outs.append(
            jnp.dot(
                inverse_ref[:, x * tile:(x + 1) * tile], split, precision=highest,
                preferred_element_type=jnp.float32,
            )
        )
    out_ref[...] = jnp.concatenate(outs, axis=1)
    send_lo_x_ref[...] = outs[-1]
    send_hi_x_ref[...] = outs[0]
    for t in range(span_x // 2):
        even, odd = outs[2 * t], outs[2 * t + 1]
        send_lo_y_ref[:, t * tile:(t + 1) * tile] = jnp.where(low_half, pltpu.roll(even, R, 1), odd)
        send_hi_y_ref[:, t * tile:(t + 1) * tile] = jnp.where(low_half, even, pltpu.roll(odd, R, 1))


def half_sweep(other, halos, face_blocks, weight, inverse, target, span_x):
    lanes = other.shape[1]
    x_shape = jax.ShapeDtypeStruct((P_SIZE, 2 * R), jnp.float32)
    y_shape = jax.ShapeDtypeStruct((P_SIZE, span_x * R), jnp.float32)
    vmem = pl.BlockSpec(memory_space=pltpu.VMEM)
    return pl.pallas_call(
        functools.partial(_half_sweep_kernel, span_x=span_x),
        out_shape=(jax.ShapeDtypeStruct((P_SIZE, lanes), jnp.float32), x_shape, x_shape, y_shape, y_shape),
        in_specs=[vmem] * 9,
        out_specs=(vmem,) * 5,
    )(other, *halos, face_blocks, weight, inverse, target)


def send_buffers(state, span_x):
    blocks = state.reshape(P_SIZE, span_x, 2, R)
    return (
        blocks[:, -1].reshape(P_SIZE, 2 * R),
        blocks[:, 0].reshape(P_SIZE, 2 * R),
        blocks[:, :, 1].reshape(P_SIZE, span_x * R),
        blocks[:, :, 0].reshape(P_SIZE, span_x * R),
    )


def trade(sends):
    lo_x, hi_x = (
        lax.ppermute(sends[0], "gx", shift_pairs("gx", 1)),
        lax.ppermute(sends[1], "gx", shift_pairs("gx", -1)),
    )
    lo_y, hi_y = (
        lax.ppermute(sends[2], "gy", shift_pairs("gy", 1)),
        lax.ppermute(sends[3], "gy", shift_pairs("gy", -1)),
    )
    return lo_x, hi_x, lo_y, hi_y


def shift_pairs(axis, step):
    count = lax.axis_size(axis)
    return [(i, (i + step) % count) for i in range(count)]


def lane_body(forcing, initial, blocks, face_blocks, strength, strong, colour, neighbours):
    span_x, span_y, span_z, width = forcing.shape
    count = span_x * span_y * span_z
    columns = span_x * span_y
    empty_slot = (span_x + 2) * (span_y + 2) * span_z
    first_is = [colour[:, :, 0] == paint for paint in (0, 1)]

    def pick(values, paint, axis=2):
        lead = (1,) * (axis - 2)
        mask = first_is[paint].reshape(lead + first_is[paint].shape + (1,) * (values.ndim - axis - 1))
        low = lax.index_in_dim(values, 0, axis=axis, keepdims=False)
        high = lax.index_in_dim(values, 1, axis=axis, keepdims=False)
        return jnp.where(mask, low, high)

    def to_lanes(values):
        return jnp.transpose(values.reshape(columns, P_SIZE, R), (1, 0, 2)).reshape(P_SIZE, columns * R)

    start_state = to_lanes(pick(initial, 1))
    first_halos = trade(send_buffers(start_state, span_x))
    by_colour = jnp.stack([pick(blocks, paint) for paint in (0, 1)]).reshape(count, P_SIZE, P_SIZE)
    inverse = block_inverses(by_colour, lanes_out=True)
    weight = jnp.where(neighbours == empty_slot, 0.0, strength * strong.astype(jnp.float32))
    member_inverse = [inverse[:, paint * columns * P_SIZE:(paint + 1) * columns * P_SIZE] for paint in (0, 1)]
    face_row = jnp.transpose(face_blocks, (1, 0, 2)).reshape(P_SIZE, 6 * P_SIZE)
    member_target = [to_lanes(pick(forcing, paint)) for paint in (0, 1)]
    member_weight = [
        jnp.repeat(pick(weight, paint, axis=3).reshape(6, columns), R, axis=1).reshape(6, 1, columns * R)
        for paint in (0, 1)
    ]
    state = [None, start_state]
    sends = None
    for sweep_index in range(SWEEPS):
        for paint_now in (0, 1):
            halos = first_halos if sends is None else trade(sends)
            state[paint_now], *sends = half_sweep(
                state[1 - paint_now],
                halos,
                face_row,
                member_weight[paint_now],
                member_inverse[paint_now],
                member_target[paint_now],
                span_x,
            )
    first = first_is[0][..., None]
    whole = [
        jnp.transpose(part.reshape(P_SIZE, columns, R), (1, 0, 2)).reshape(span_x, span_y, width)
        for part in state
    ]
    return jnp.stack(
        [jnp.where(first, whole[0], whole[1]), jnp.where(first, whole[1], whole[0])], axis=2
    )


def dispatch(forcing, *rest):
    span_x, span_y, span_z, width = forcing.shape
    if span_y == 2 and span_z == 2 and span_x % 2 == 0 and width == P_SIZE * R:
        return lane_body(forcing, *rest)
    return body(forcing, *rest)


def solution(mesh):
    in_specs = (
        P("gx", "gy", None, None),
        P("gx", "gy", None, None),
        P("gx", "gy", None, None),
        P(),
        P(None, "gx", "gy", None),
        P(None, "gx", "gy", None),
        P("gx", "gy", None),
        P(None, "gx", "gy", None),
    )
    out_specs = P("gx", "gy", None, None)
    return jax.shard_map(dispatch, mesh=mesh, in_specs=in_specs, out_specs=out_specs, check_vma=False)
```

```python
import functools

import jax
import jax.numpy as jnp
from jax import lax
from jax.experimental import pallas as pl
from jax.experimental.pallas import tpu as pltpu
from jax.sharding import PartitionSpec as P

P_SIZE = 64
R = 64
SWEEPS = 4


def padded(block, sides, width):
    for axis, dim in sides:
        count = lax.axis_size(axis)
        forward = [(i, i + 1) for i in range(count - 1)]
        backward = [(target, source) for source, target in forward]
        low = lax.ppermute(
            lax.slice_in_dim(block, block.shape[dim] - width, None, axis=dim), axis, forward
        )
        high = lax.ppermute(lax.slice_in_dim(block, 0, width, axis=dim), axis, backward)
        block = jnp.concatenate([low, block, high], axis=dim)
    return block


def _gauss_jordan_kernel(a_ref, o_ref, *, n, nb):
    lanes = n * nb
    tiles = lanes // 128
    o_ref[...] = a_ref[...]
    lane_t = lax.broadcasted_iota(jnp.int32, (n, 128), 1)
    lane_r = lax.broadcasted_iota(jnp.int32, (1, 128), 1)
    row_i = lax.broadcasted_iota(jnp.int32, (n, 128), 0)

    def spread(x):
        shift = nb
        while shift < 128:
            x = x + pltpu.roll(x, shift, 1)
            shift *= 2
        return x

    def step(k, carry):
        start = k * nb
        tile = start // 128
        off = start % 128
        tile_start = pl.multiple_of(tile * 128, 128)
        column = spread(
            jnp.where((lane_t >= off) & (lane_t < off + nb), o_ref[:, pl.ds(tile_start, 128)], 0.0)
        )
        pivot = jnp.sum(jnp.where(row_i == k, column, 0.0), axis=0, keepdims=True)
        base = pl.multiple_of((k // 8) * 8, 8)
        band = o_ref[pl.ds(base, 8), :]
        band_i = lax.broadcasted_iota(jnp.int32, band.shape, 0)
        row = jnp.sum(jnp.where(band_i == k - base, band, 0.0), axis=0, keepdims=True)
        for t in range(tiles):
            in_col = (t == tile) & (lane_r >= off) & (lane_r < off + nb)
            scaled = jnp.where(in_col, 1.0 / pivot, row[:, t * 128:(t + 1) * 128] / pivot)
            kept = jnp.where(in_col, 0.0, o_ref[:, t * 128:(t + 1) * 128])
            o_ref[:, t * 128:(t + 1) * 128] = jnp.where(row_i == k, scaled, kept - column * scaled)
        return carry

    lax.fori_loop(0, n, step, 0)


def block_inverses(matrices, lanes_out=False):
    nb, n, _ = matrices.shape
    if 128 % nb or (n * nb) % 128:
        assert not lanes_out
        lower_factor = jnp.linalg.cholesky(matrices)
        identity = jnp.broadcast_to(jnp.eye(n, dtype=matrices.dtype), matrices.shape)
        solved = jax.scipy.linalg.solve_triangular(lower_factor, identity, lower=True)
        return jnp.einsum("eqp,eqr->epr", solved, solved, precision=lax.Precision.HIGHEST)
    packed = jnp.transpose(matrices, (1, 2, 0)).reshape(n, n * nb)
    inverted = pl.pallas_call(
        functools.partial(_gauss_jordan_kernel, n=n, nb=nb),
        out_shape=jax.ShapeDtypeStruct((n, n * nb), jnp.float32),
        in_specs=[pl.BlockSpec(memory_space=pltpu.VMEM)],
        out_specs=pl.BlockSpec(memory_space=pltpu.VMEM),
        cost_estimate=pl.CostEstimate(
            flops=2000 * n ** 3 * nb, transcendentals=0, bytes_accessed=8 * n * n * nb
        ),
    )(packed)
    if lanes_out:
        return jnp.transpose(inverted.reshape(n, n, nb), (0, 2, 1)).reshape(n, nb * n)
    return jnp.transpose(inverted.reshape(n, n, nb), (2, 0, 1))


def shifted(values, halo, dim, lower):
    width = values.shape[dim]
    if lower:
        return jnp.concatenate([halo, lax.slice_in_dim(values, 0, width - 1, axis=dim)], axis=dim)
    return jnp.concatenate([lax.slice_in_dim(values, 1, width, axis=dim), halo], axis=dim)


def exchange(values, axis, dim):
    count = lax.axis_size(axis)
    forward = [(i, i + 1) for i in range(count - 1)]
    backward = [(target, source) for source, target in forward]
    width = values.shape[dim]
    from_lower = lax.ppermute(lax.slice_in_dim(values, width - 1, width, axis=dim), axis, forward)
    from_upper = lax.ppermute(lax.slice_in_dim(values, 0, 1, axis=dim), axis, backward)
    return from_lower, from_upper


def body(forcing, initial, blocks, face_blocks, strength, strong, colour, neighbours):
    span_x, span_y, span_z, width = forcing.shape
    count = span_x * span_y * span_z
    columns = span_x * span_y
    empty_slot = (span_x + 2) * (span_y + 2) * span_z
    inverse = block_inverses(blocks.reshape(count, P_SIZE, P_SIZE)).reshape(
        span_x, span_y, span_z, P_SIZE, P_SIZE
    )
    weight = jnp.where(neighbours == empty_slot, 0.0, strength * strong.astype(jnp.float32))
    first_is = [colour[:, :, 0] == paint for paint in (0, 1)]

    def pick(values, paint, axis=2):
        lead = (1,) * (axis - 2)
        mask = first_is[paint].reshape(lead + first_is[paint].shape + (1,) * (values.ndim - axis - 1))
        low = lax.index_in_dim(values, 0, axis=axis, keepdims=False)
        high = lax.index_in_dim(values, 1, axis=axis, keepdims=False)
        return jnp.where(mask, low, high)

    member_inverse = [inverse[:, paint * columns * P_SIZE:(paint + 1) * columns * P_SIZE] for paint in (0, 1)]
    face_row = jnp.transpose(face_blocks, (1, 0, 2)).reshape(P_SIZE, 6 * P_SIZE)
    member_target = [pick(forcing, paint).reshape(columns, P_SIZE, R) for paint in (0, 1)]
    member_weight = [pick(weight, paint, axis=3)[..., None] for paint in (0, 1)]
    state = [pick(initial, 0), pick(initial, 1)]
    for sweep_index in range(SWEEPS):
        for paint_now in (0, 1):
            other = state[1 - paint_now]
            low_x, high_x = exchange(other, "gx", 0)
            low_y, high_y = exchange(other, "gy", 1)
            nearby = jnp.stack(
                [
                    shifted(other, low_x, 0, True),
                    shifted(other, high_x, 0, False),
                    shifted(other, low_y, 1, True),
                    shifted(other, high_y, 1, False),
                    other,
                    other,
                ]
            )
            nearby = (nearby * member_weight[paint_now]).reshape(6, columns, P_SIZE, R)
            coupled = jnp.einsum(
                "fpq,feqr->epr", face_blocks, nearby, precision=lax.Precision.HIGHEST
            )
            update = jnp.einsum(
                "epq,eqr->epr",
                member_inverse[paint_now],
                member_target[paint_now] - coupled,
                precision=lax.Precision.HIGHEST,
            )
            state[paint_now] = update.reshape(span_x, span_y, width)
    first = first_is[0][..., None]
    return jnp.stack(
        [jnp.where(first, state[0], state[1]), jnp.where(first, state[1], state[0])], axis=2
    )


def _half_sweep_kernel(
    other_ref, lo_x_ref, hi_x_ref, lo_y_ref, hi_y_ref, face_ref, weight_ref, inverse_ref,
    target_ref, out_ref, send_lo_x_ref, send_hi_x_ref, send_lo_y_ref, send_hi_y_ref, *, span_x
):
    tile = 2 * R
    highest = lax.Precision.HIGHEST
    other = other_ref[...]
    lanes = other.shape[1]
    lane = lax.broadcasted_iota(jnp.int32, (P_SIZE, tile), 1)
    low_half = lane < R
    tiles = [other[:, t * tile:(t + 1) * tile] for t in range(span_x)]
    lo_y = lo_y_ref[...]
    hi_y = hi_y_ref[...]

    def y_block(packed, x):
        held = packed[:, (x // 2) * tile:(x // 2 + 1) * tile]
        return held if x % 2 == 0 else pltpu.roll(held, R, 1)

    below, above = [], []
    for x in range(span_x):
        rolled = pltpu.roll(tiles[x], R, 1)
        below.append(jnp.where(low_half, y_block(lo_y, x), rolled))
        above.append(jnp.where(low_half, rolled, pltpu.roll(y_block(hi_y, x), R, 1)))
    nearby = [
        jnp.concatenate([lo_x_ref[...], other[:, :lanes - tile]], axis=1),
        jnp.concatenate([other[:, tile:], hi_x_ref[...]], axis=1),
        jnp.concatenate(below, axis=1),
        jnp.concatenate(above, axis=1),
        other,
        other,
    ]
    stacked = jnp.concatenate(
        [weight_ref[face:face + 1, :] * nearby[face] for face in range(6)], axis=0
    )
    coupled = jnp.dot(face_ref[...], stacked, precision=highest, preferred_element_type=jnp.float32)
    rhs = target_ref[...] - coupled
    outs = []
    for x in range(span_x):
        part = rhs[:, x * tile:(x + 1) * tile]
        split = jnp.concatenate([jnp.where(low_half, part, 0.0), jnp.where(low_half, 0.0, part)], axis=0)
        outs.append(
            jnp.dot(
                inverse_ref[:, x * tile:(x + 1) * tile], split, precision=highest,
                preferred_element_type=jnp.float32,
            )
        )
    out_ref[...] = jnp.concatenate(outs, axis=1)
    send_lo_x_ref[...] = outs[-1]
    send_hi_x_ref[...] = outs[0]
    for t in range(span_x // 2):
        even, odd = outs[2 * t], outs[2 * t + 1]
        send_lo_y_ref[:, t * tile:(t + 1) * tile] = jnp.where(low_half, pltpu.roll(even, R, 1), odd)
        send_hi_y_ref[:, t * tile:(t + 1) * tile] = jnp.where(low_half, even, pltpu.roll(odd, R, 1))


def half_sweep(other, halos, face_blocks, weight, inverse, target, span_x):
    lanes = other.shape[1]
    x_shape = jax.ShapeDtypeStruct((P_SIZE, 2 * R), jnp.float32)
    y_shape = jax.ShapeDtypeStruct((P_SIZE, span_x * R), jnp.float32)
    vmem = pl.BlockSpec(memory_space=pltpu.VMEM)
    return pl.pallas_call(
        functools.partial(_half_sweep_kernel, span_x=span_x),
        out_shape=(jax.ShapeDtypeStruct((P_SIZE, lanes), jnp.float32), x_shape, x_shape, y_shape, y_shape),
        in_specs=[vmem] * 9,
        out_specs=(vmem,) * 5,
    )(other, *halos, face_blocks, weight, inverse, target)


def send_buffers(state, span_x):
    blocks = state.reshape(P_SIZE, span_x, 2, R)
    return (
        blocks[:, -1].reshape(P_SIZE, 2 * R),
        blocks[:, 0].reshape(P_SIZE, 2 * R),
        blocks[:, :, 1].reshape(P_SIZE, span_x * R),
        blocks[:, :, 0].reshape(P_SIZE, span_x * R),
    )


def trade(sends):
    lo_x, hi_x = (
        lax.ppermute(sends[0], "gx", shift_pairs("gx", 1)),
        lax.ppermute(sends[1], "gx", shift_pairs("gx", -1)),
    )
    lo_y, hi_y = (
        lax.ppermute(sends[2], "gy", shift_pairs("gy", 1)),
        lax.ppermute(sends[3], "gy", shift_pairs("gy", -1)),
    )
    return lo_x, hi_x, lo_y, hi_y


def shift_pairs(axis, step):
    count = lax.axis_size(axis)
    return [(i, (i + step) % count) for i in range(count)]


def lane_body(forcing, initial, blocks, face_blocks, strength, strong, colour, neighbours):
    span_x, span_y, span_z, width = forcing.shape
    count = span_x * span_y * span_z
    columns = span_x * span_y
    empty_slot = (span_x + 2) * (span_y + 2) * span_z
    first_is = [colour[:, :, 0] == paint for paint in (0, 1)]

    def pick(values, paint, axis=2):
        lead = (1,) * (axis - 2)
        mask = first_is[paint].reshape(lead + first_is[paint].shape + (1,) * (values.ndim - axis - 1))
        low = lax.index_in_dim(values, 0, axis=axis, keepdims=False)
        high = lax.index_in_dim(values, 1, axis=axis, keepdims=False)
        return jnp.where(mask, low, high)

    def to_lanes(values):
        return jnp.transpose(values.reshape(columns, P_SIZE, R), (1, 0, 2)).reshape(P_SIZE, columns * R)

    start_state = to_lanes(pick(initial, 1))
    first_halos = trade(send_buffers(start_state, span_x))
    by_colour = jnp.stack([pick(blocks, paint) for paint in (0, 1)]).reshape(count, P_SIZE, P_SIZE)
    inverse = block_inverses(by_colour, lanes_out=True)
    weight = jnp.where(neighbours == empty_slot, 0.0, strength * strong.astype(jnp.float32))
    member_inverse = [inverse[:, paint * columns * P_SIZE:(paint + 1) * columns * P_SIZE] for paint in (0, 1)]
    face_row = jnp.transpose(face_blocks, (1, 0, 2)).reshape(P_SIZE, 6 * P_SIZE)
    member_target = [to_lanes(pick(forcing, paint)) for paint in (0, 1)]
    member_weight = [
        jnp.pad(jnp.repeat(pick(weight, paint, axis=3).reshape(6, columns), R, axis=1), ((0, 2), (0, 0)))
        for paint in (0, 1)
    ]
    member_inverse, member_target, member_weight, face_row = lax.optimization_barrier(
        (member_inverse, member_target, member_weight, face_row)
    )
    state = [None, start_state]
    sends = None
    for sweep_index in range(SWEEPS):
        for paint_now in (0, 1):
            halos = first_halos if sends is None else trade(sends)
            state[paint_now], *sends = half_sweep(
                state[1 - paint_now],
                halos,
                face_row,
                member_weight[paint_now],
                member_inverse[paint_now],
                member_target[paint_now],
                span_x,
            )
    first = first_is[0][..., None]
    whole = [
        jnp.transpose(part.reshape(P_SIZE, columns, R), (1, 0, 2)).reshape(span_x, span_y, width)
        for part in state
    ]
    return jnp.stack(
        [jnp.where(first, whole[0], whole[1]), jnp.where(first, whole[1], whole[0])], axis=2
    )


def dispatch(forcing, *rest):
    span_x, span_y, span_z, width = forcing.shape
    if span_y == 2 and span_z == 2 and span_x % 2 == 0 and width == P_SIZE * R:
        return lane_body(forcing, *rest)
    return body(forcing, *rest)


def solution(mesh):
    in_specs = (
        P("gx", "gy", None, None),
        P("gx", "gy", None, None),
        P("gx", "gy", None, None),
        P(),
        P(None, "gx", "gy", None),
        P(None, "gx", "gy", None),
        P("gx", "gy", None),
        P(None, "gx", "gy", None),
    )
    out_specs = P("gx", "gy", None, None)
    return jax.shard_map(dispatch, mesh=mesh, in_specs=in_specs, out_specs=out_specs, check_vma=False)
```

```python
import functools

import jax
import jax.numpy as jnp
from jax import lax
from jax.experimental import pallas as pl
from jax.experimental.pallas import tpu as pltpu
from jax.sharding import PartitionSpec as P

P_SIZE = 64
R = 64
SWEEPS = 4


def padded(block, sides, width):
    for axis, dim in sides:
        count = lax.axis_size(axis)
        forward = [(i, i + 1) for i in range(count - 1)]
        backward = [(target, source) for source, target in forward]
        low = lax.ppermute(
            lax.slice_in_dim(block, block.shape[dim] - width, None, axis=dim), axis, forward
        )
        high = lax.ppermute(lax.slice_in_dim(block, 0, width, axis=dim), axis, backward)
        block = jnp.concatenate([low, block, high], axis=dim)
    return block


def _gauss_jordan_kernel(a_ref, o_ref, *, n, nb):
    lanes = n * nb
    tiles = lanes // 128
    o_ref[...] = a_ref[...]
    lane_t = lax.broadcasted_iota(jnp.int32, (n, 128), 1)
    lane_r = lax.broadcasted_iota(jnp.int32, (1, 128), 1)
    row_i = lax.broadcasted_iota(jnp.int32, (n, 128), 0)

    def spread(x):
        shift = nb
        while shift < 128:
            x = x + pltpu.roll(x, shift, 1)
            shift *= 2
        return x

    def step(k, carry):
        start = k * nb
        tile = start // 128
        off = start % 128
        tile_start = pl.multiple_of(tile * 128, 128)
        column = spread(
            jnp.where((lane_t >= off) & (lane_t < off + nb), o_ref[:, pl.ds(tile_start, 128)], 0.0)
        )
        pivot = jnp.sum(jnp.where(row_i == k, column, 0.0), axis=0, keepdims=True)
        base = pl.multiple_of((k // 8) * 8, 8)
        band = o_ref[pl.ds(base, 8), :]
        band_i = lax.broadcasted_iota(jnp.int32, band.shape, 0)
        row = jnp.sum(jnp.where(band_i == k - base, band, 0.0), axis=0, keepdims=True)
        for t in range(tiles):
            in_col = (t == tile) & (lane_r >= off) & (lane_r < off + nb)
            scaled = jnp.where(in_col, 1.0 / pivot, row[:, t * 128:(t + 1) * 128] / pivot)
            kept = jnp.where(in_col, 0.0, o_ref[:, t * 128:(t + 1) * 128])
            o_ref[:, t * 128:(t + 1) * 128] = jnp.where(row_i == k, scaled, kept - column * scaled)
        return carry

    lax.fori_loop(0, n, step, 0)


def block_inverses(matrices, lanes_out=False):
    nb, n, _ = matrices.shape
    if 128 % nb or (n * nb) % 128:
        assert not lanes_out
        lower_factor = jnp.linalg.cholesky(matrices)
        identity = jnp.broadcast_to(jnp.eye(n, dtype=matrices.dtype), matrices.shape)
        solved = jax.scipy.linalg.solve_triangular(lower_factor, identity, lower=True)
        return jnp.einsum("eqp,eqr->epr", solved, solved, precision=lax.Precision.HIGHEST)
    packed = jnp.transpose(matrices, (1, 2, 0)).reshape(n, n * nb)
    inverted = pl.pallas_call(
        functools.partial(_gauss_jordan_kernel, n=n, nb=nb),
        out_shape=jax.ShapeDtypeStruct((n, n * nb), jnp.float32),
        in_specs=[pl.BlockSpec(memory_space=pltpu.VMEM)],
        out_specs=pl.BlockSpec(memory_space=pltpu.VMEM),
        cost_estimate=pl.CostEstimate(
            flops=2000 * n ** 3 * nb, transcendentals=0, bytes_accessed=8 * n * n * nb
        ),
    )(packed)
    if lanes_out:
        return jnp.transpose(inverted.reshape(n, n, nb), (0, 2, 1)).reshape(n, nb * n)
    return jnp.transpose(inverted.reshape(n, n, nb), (2, 0, 1))


def shifted(values, halo, dim, lower):
    width = values.shape[dim]
    if lower:
        return jnp.concatenate([halo, lax.slice_in_dim(values, 0, width - 1, axis=dim)], axis=dim)
    return jnp.concatenate([lax.slice_in_dim(values, 1, width, axis=dim), halo], axis=dim)


def exchange(values, axis, dim):
    count = lax.axis_size(axis)
    forward = [(i, i + 1) for i in range(count - 1)]
    backward = [(target, source) for source, target in forward]
    width = values.shape[dim]
    from_lower = lax.ppermute(lax.slice_in_dim(values, width - 1, width, axis=dim), axis, forward)
    from_upper = lax.ppermute(lax.slice_in_dim(values, 0, 1, axis=dim), axis, backward)
    return from_lower, from_upper


def body(forcing, initial, blocks, face_blocks, strength, strong, colour, neighbours):
    span_x, span_y, span_z, width = forcing.shape
    count = span_x * span_y * span_z
    columns = span_x * span_y
    empty_slot = (span_x + 2) * (span_y + 2) * span_z
    inverse = block_inverses(blocks.reshape(count, P_SIZE, P_SIZE)).reshape(
        span_x, span_y, span_z, P_SIZE, P_SIZE
    )
    weight = jnp.where(neighbours == empty_slot, 0.0, strength * strong.astype(jnp.float32))
    first_is = [colour[:, :, 0] == paint for paint in (0, 1)]

    def pick(values, paint, axis=2):
        lead = (1,) * (axis - 2)
        mask = first_is[paint].reshape(lead + first_is[paint].shape + (1,) * (values.ndim - axis - 1))
        low = lax.index_in_dim(values, 0, axis=axis, keepdims=False)
        high = lax.index_in_dim(values, 1, axis=axis, keepdims=False)
        return jnp.where(mask, low, high)

    member_inverse = [inverse[:, paint * columns * P_SIZE:(paint + 1) * columns * P_SIZE] for paint in (0, 1)]
    face_row = jnp.transpose(face_blocks, (1, 0, 2)).reshape(P_SIZE, 6 * P_SIZE)
    member_target = [pick(forcing, paint).reshape(columns, P_SIZE, R) for paint in (0, 1)]
    member_weight = [pick(weight, paint, axis=3)[..., None] for paint in (0, 1)]
    state = [pick(initial, 0), pick(initial, 1)]
    for sweep_index in range(SWEEPS):
        for paint_now in (0, 1):
            other = state[1 - paint_now]
            low_x, high_x = exchange(other, "gx", 0)
            low_y, high_y = exchange(other, "gy", 1)
            nearby = jnp.stack(
                [
                    shifted(other, low_x, 0, True),
                    shifted(other, high_x, 0, False),
                    shifted(other, low_y, 1, True),
                    shifted(other, high_y, 1, False),
                    other,
                    other,
                ]
            )
            nearby = (nearby * member_weight[paint_now]).reshape(6, columns, P_SIZE, R)
            coupled = jnp.einsum(
                "fpq,feqr->epr", face_blocks, nearby, precision=lax.Precision.HIGHEST
            )
            update = jnp.einsum(
                "epq,eqr->epr",
                member_inverse[paint_now],
                member_target[paint_now] - coupled,
                precision=lax.Precision.HIGHEST,
            )
            state[paint_now] = update.reshape(span_x, span_y, width)
    first = first_is[0][..., None]
    return jnp.stack(
        [jnp.where(first, state[0], state[1]), jnp.where(first, state[1], state[0])], axis=2
    )


def _half_sweep_kernel(
    other_ref, lo_x_ref, hi_x_ref, lo_y_ref, hi_y_ref, face_ref, weight_ref, inverse_ref,
    target_ref, out_ref, send_lo_x_ref, send_hi_x_ref, send_lo_y_ref, send_hi_y_ref, *, span_x
):
    tile = 2 * R
    highest = lax.Precision.HIGHEST
    other = other_ref[...]
    lanes = other.shape[1]
    lane = lax.broadcasted_iota(jnp.int32, (P_SIZE, tile), 1)
    low_half = lane < R
    tiles = [other[:, t * tile:(t + 1) * tile] for t in range(span_x)]
    lo_y = lo_y_ref[...]
    hi_y = hi_y_ref[...]

    def y_block(packed, x):
        held = packed[:, (x // 2) * tile:(x // 2 + 1) * tile]
        return held if x % 2 == 0 else pltpu.roll(held, R, 1)

    below, above = [], []
    for x in range(span_x):
        rolled = pltpu.roll(tiles[x], R, 1)
        below.append(jnp.where(low_half, y_block(lo_y, x), rolled))
        above.append(jnp.where(low_half, rolled, pltpu.roll(y_block(hi_y, x), R, 1)))
    nearby = [
        jnp.concatenate([lo_x_ref[...], other[:, :lanes - tile]], axis=1),
        jnp.concatenate([other[:, tile:], hi_x_ref[...]], axis=1),
        jnp.concatenate(below, axis=1),
        jnp.concatenate(above, axis=1),
        other,
        other,
    ]
    stacked = jnp.concatenate(
        [weight_ref[face:face + 1, :] * nearby[face] for face in range(6)], axis=0
    )
    coupled = jnp.dot(face_ref[...], stacked, precision=highest, preferred_element_type=jnp.float32)
    rhs = target_ref[...] - coupled
    outs = []
    for x in range(span_x):
        part = rhs[:, x * tile:(x + 1) * tile]
        split = jnp.concatenate([jnp.where(low_half, part, 0.0), jnp.where(low_half, 0.0, part)], axis=0)
        outs.append(
            jnp.dot(
                inverse_ref[:, x * tile:(x + 1) * tile], split, precision=highest,
                preferred_element_type=jnp.float32,
            )
        )
    out_ref[...] = jnp.concatenate(outs, axis=1)
    send_lo_x_ref[...] = outs[-1]
    send_hi_x_ref[...] = outs[0]
    for t in range(span_x // 2):
        even, odd = outs[2 * t], outs[2 * t + 1]
        send_lo_y_ref[:, t * tile:(t + 1) * tile] = jnp.where(low_half, pltpu.roll(even, R, 1), odd)
        send_hi_y_ref[:, t * tile:(t + 1) * tile] = jnp.where(low_half, even, pltpu.roll(odd, R, 1))


def half_sweep(other, halos, face_blocks, weight, inverse, target, span_x):
    lanes = other.shape[1]
    x_shape = jax.ShapeDtypeStruct((P_SIZE, 2 * R), jnp.float32)
    y_shape = jax.ShapeDtypeStruct((P_SIZE, span_x * R), jnp.float32)
    vmem = pl.BlockSpec(memory_space=pltpu.VMEM)
    return pl.pallas_call(
        functools.partial(_half_sweep_kernel, span_x=span_x),
        out_shape=(jax.ShapeDtypeStruct((P_SIZE, lanes), jnp.float32), x_shape, x_shape, y_shape, y_shape),
        in_specs=[vmem] * 9,
        out_specs=(vmem,) * 5,
    )(*[
        pltpu.with_memory_space_constraint(value, pltpu.VMEM)
        for value in (other, *halos, face_blocks, weight, inverse, target)
    ])


def send_buffers(state, span_x):
    blocks = state.reshape(P_SIZE, span_x, 2, R)
    return (
        blocks[:, -1].reshape(P_SIZE, 2 * R),
        blocks[:, 0].reshape(P_SIZE, 2 * R),
        blocks[:, :, 1].reshape(P_SIZE, span_x * R),
        blocks[:, :, 0].reshape(P_SIZE, span_x * R),
    )


def trade(sends):
    lo_x, hi_x = (
        lax.ppermute(sends[0], "gx", shift_pairs("gx", 1)),
        lax.ppermute(sends[1], "gx", shift_pairs("gx", -1)),
    )
    lo_y, hi_y = (
        lax.ppermute(sends[2], "gy", shift_pairs("gy", 1)),
        lax.ppermute(sends[3], "gy", shift_pairs("gy", -1)),
    )
    return lo_x, hi_x, lo_y, hi_y


def shift_pairs(axis, step):
    count = lax.axis_size(axis)
    return [(i, (i + step) % count) for i in range(count)]


def lane_body(forcing, initial, blocks, face_blocks, strength, strong, colour, neighbours):
    span_x, span_y, span_z, width = forcing.shape
    count = span_x * span_y * span_z
    columns = span_x * span_y
    empty_slot = (span_x + 2) * (span_y + 2) * span_z
    first_is = [colour[:, :, 0] == paint for paint in (0, 1)]

    def pick(values, paint, axis=2):
        lead = (1,) * (axis - 2)
        mask = first_is[paint].reshape(lead + first_is[paint].shape + (1,) * (values.ndim - axis - 1))
        low = lax.index_in_dim(values, 0, axis=axis, keepdims=False)
        high = lax.index_in_dim(values, 1, axis=axis, keepdims=False)
        return jnp.where(mask, low, high)

    def to_lanes(values):
        return jnp.transpose(values.reshape(columns, P_SIZE, R), (1, 0, 2)).reshape(P_SIZE, columns * R)

    start_state = to_lanes(pick(initial, 1))
    first_halos = trade(send_buffers(start_state, span_x))
    by_colour = jnp.stack([pick(blocks, paint) for paint in (0, 1)]).reshape(count, P_SIZE, P_SIZE)
    inverse = block_inverses(by_colour, lanes_out=True)
    weight = jnp.where(neighbours == empty_slot, 0.0, strength * strong.astype(jnp.float32))
    member_inverse = [inverse[:, paint * columns * P_SIZE:(paint + 1) * columns * P_SIZE] for paint in (0, 1)]
    face_row = jnp.transpose(face_blocks, (1, 0, 2)).reshape(P_SIZE, 6 * P_SIZE)
    member_target = [to_lanes(pick(forcing, paint)) for paint in (0, 1)]
    member_weight = [
        jnp.pad(jnp.repeat(pick(weight, paint, axis=3).reshape(6, columns), R, axis=1), ((0, 2), (0, 0)))
        for paint in (0, 1)
    ]
    member_inverse, member_target, member_weight, face_row = lax.optimization_barrier(
        (member_inverse, member_target, member_weight, face_row)
    )
    state = [None, start_state]
    sends = None
    for sweep_index in range(SWEEPS):
        for paint_now in (0, 1):
            halos = first_halos if sends is None else trade(sends)
            state[paint_now], *sends = half_sweep(
                state[1 - paint_now],
                halos,
                face_row,
                member_weight[paint_now],
                member_inverse[paint_now],
                member_target[paint_now],
                span_x,
            )
    first = first_is[0][..., None]
    whole = [
        jnp.transpose(part.reshape(P_SIZE, columns, R), (1, 0, 2)).reshape(span_x, span_y, width)
        for part in state
    ]
    return jnp.stack(
        [jnp.where(first, whole[0], whole[1]), jnp.where(first, whole[1], whole[0])], axis=2
    )


def dispatch(forcing, *rest):
    span_x, span_y, span_z, width = forcing.shape
    if span_y == 2 and span_z == 2 and span_x % 2 == 0 and width == P_SIZE * R:
        return lane_body(forcing, *rest)
    return body(forcing, *rest)


def solution(mesh):
    in_specs = (
        P("gx", "gy", None, None),
        P("gx", "gy", None, None),
        P("gx", "gy", None, None),
        P(),
        P(None, "gx", "gy", None),
        P(None, "gx", "gy", None),
        P("gx", "gy", None),
        P(None, "gx", "gy", None),
    )
    out_specs = P("gx", "gy", None, None)
    return jax.shard_map(dispatch, mesh=mesh, in_specs=in_specs, out_specs=out_specs, check_vma=False)
```

```python
import functools

import jax
import jax.numpy as jnp
from jax import lax
from jax.experimental import pallas as pl
from jax.experimental.pallas import tpu as pltpu
from jax.sharding import PartitionSpec as P

P_SIZE = 64
R = 64
SWEEPS = 4


def padded(block, sides, width):
    for axis, dim in sides:
        count = lax.axis_size(axis)
        forward = [(i, i + 1) for i in range(count - 1)]
        backward = [(target, source) for source, target in forward]
        low = lax.ppermute(
            lax.slice_in_dim(block, block.shape[dim] - width, None, axis=dim), axis, forward
        )
        high = lax.ppermute(lax.slice_in_dim(block, 0, width, axis=dim), axis, backward)
        block = jnp.concatenate([low, block, high], axis=dim)
    return block


def _gauss_jordan_kernel(a_ref, o_ref, *, n, nb):
    lanes = n * nb
    tiles = lanes // 128
    o_ref[...] = a_ref[...]
    lane_t = lax.broadcasted_iota(jnp.int32, (n, 128), 1)
    lane_r = lax.broadcasted_iota(jnp.int32, (1, 128), 1)
    row_i = lax.broadcasted_iota(jnp.int32, (n, 128), 0)

    def spread(x):
        shift = nb
        while shift < 128:
            x = x + pltpu.roll(x, shift, 1)
            shift *= 2
        return x

    def step(k, carry):
        start = k * nb
        tile = start // 128
        off = start % 128
        tile_start = pl.multiple_of(tile * 128, 128)
        column = spread(
            jnp.where((lane_t >= off) & (lane_t < off + nb), o_ref[:, pl.ds(tile_start, 128)], 0.0)
        )
        pivot = jnp.sum(jnp.where(row_i == k, column, 0.0), axis=0, keepdims=True)
        base = pl.multiple_of((k // 8) * 8, 8)
        band = o_ref[pl.ds(base, 8), :]
        band_i = lax.broadcasted_iota(jnp.int32, band.shape, 0)
        row = jnp.sum(jnp.where(band_i == k - base, band, 0.0), axis=0, keepdims=True)
        for t in range(tiles):
            in_col = (t == tile) & (lane_r >= off) & (lane_r < off + nb)
            scaled = jnp.where(in_col, 1.0 / pivot, row[:, t * 128:(t + 1) * 128] / pivot)
            kept = jnp.where(in_col, 0.0, o_ref[:, t * 128:(t + 1) * 128])
            o_ref[:, t * 128:(t + 1) * 128] = jnp.where(row_i == k, scaled, kept - column * scaled)
        return carry

    lax.fori_loop(0, n, step, 0)


def block_inverses(matrices, lanes_out=False):
    nb, n, _ = matrices.shape
    if 128 % nb or (n * nb) % 128:
        assert not lanes_out
        lower_factor = jnp.linalg.cholesky(matrices)
        identity = jnp.broadcast_to(jnp.eye(n, dtype=matrices.dtype), matrices.shape)
        solved = jax.scipy.linalg.solve_triangular(lower_factor, identity, lower=True)
        return jnp.einsum("eqp,eqr->epr", solved, solved, precision=lax.Precision.HIGHEST)
    packed = jnp.transpose(matrices, (1, 2, 0)).reshape(n, n * nb)
    inverted = pl.pallas_call(
        functools.partial(_gauss_jordan_kernel, n=n, nb=nb),
        out_shape=jax.ShapeDtypeStruct((n, n * nb), jnp.float32),
        in_specs=[pl.BlockSpec(memory_space=pltpu.VMEM)],
        out_specs=pl.BlockSpec(memory_space=pltpu.VMEM),
        cost_estimate=pl.CostEstimate(
            flops=2000 * n ** 3 * nb, transcendentals=0, bytes_accessed=8 * n * n * nb
        ),
    )(packed)
    if lanes_out:
        return jnp.transpose(inverted.reshape(n, n, nb), (0, 2, 1)).reshape(n, nb * n)
    return jnp.transpose(inverted.reshape(n, n, nb), (2, 0, 1))


def shifted(values, halo, dim, lower):
    width = values.shape[dim]
    if lower:
        return jnp.concatenate([halo, lax.slice_in_dim(values, 0, width - 1, axis=dim)], axis=dim)
    return jnp.concatenate([lax.slice_in_dim(values, 1, width, axis=dim), halo], axis=dim)


def exchange(values, axis, dim):
    count = lax.axis_size(axis)
    forward = [(i, i + 1) for i in range(count - 1)]
    backward = [(target, source) for source, target in forward]
    width = values.shape[dim]
    from_lower = lax.ppermute(lax.slice_in_dim(values, width - 1, width, axis=dim), axis, forward)
    from_upper = lax.ppermute(lax.slice_in_dim(values, 0, 1, axis=dim), axis, backward)
    return from_lower, from_upper


def body(forcing, initial, blocks, face_blocks, strength, strong, colour, neighbours):
    span_x, span_y, span_z, width = forcing.shape
    count = span_x * span_y * span_z
    columns = span_x * span_y
    empty_slot = (span_x + 2) * (span_y + 2) * span_z
    inverse = block_inverses(blocks.reshape(count, P_SIZE, P_SIZE)).reshape(
        span_x, span_y, span_z, P_SIZE, P_SIZE
    )
    weight = jnp.where(neighbours == empty_slot, 0.0, strength * strong.astype(jnp.float32))
    first_is = [colour[:, :, 0] == paint for paint in (0, 1)]

    def pick(values, paint, axis=2):
        lead = (1,) * (axis - 2)
        mask = first_is[paint].reshape(lead + first_is[paint].shape + (1,) * (values.ndim - axis - 1))
        low = lax.index_in_dim(values, 0, axis=axis, keepdims=False)
        high = lax.index_in_dim(values, 1, axis=axis, keepdims=False)
        return jnp.where(mask, low, high)

    member_inverse = [inverse[:, paint * columns * P_SIZE:(paint + 1) * columns * P_SIZE] for paint in (0, 1)]
    face_row = jnp.transpose(face_blocks, (1, 0, 2)).reshape(P_SIZE, 6 * P_SIZE)
    member_target = [pick(forcing, paint).reshape(columns, P_SIZE, R) for paint in (0, 1)]
    member_weight = [pick(weight, paint, axis=3)[..., None] for paint in (0, 1)]
    state = [pick(initial, 0), pick(initial, 1)]
    for sweep_index in range(SWEEPS):
        for paint_now in (0, 1):
            other = state[1 - paint_now]
            low_x, high_x = exchange(other, "gx", 0)
            low_y, high_y = exchange(other, "gy", 1)
            nearby = jnp.stack(
                [
                    shifted(other, low_x, 0, True),
                    shifted(other, high_x, 0, False),
                    shifted(other, low_y, 1, True),
                    shifted(other, high_y, 1, False),
                    other,
                    other,
                ]
            )
            nearby = (nearby * member_weight[paint_now]).reshape(6, columns, P_SIZE, R)
            coupled = jnp.einsum(
                "fpq,feqr->epr", face_blocks, nearby, precision=lax.Precision.HIGHEST
            )
            update = jnp.einsum(
                "epq,eqr->epr",
                member_inverse[paint_now],
                member_target[paint_now] - coupled,
                precision=lax.Precision.HIGHEST,
            )
            state[paint_now] = update.reshape(span_x, span_y, width)
    first = first_is[0][..., None]
    return jnp.stack(
        [jnp.where(first, state[0], state[1]), jnp.where(first, state[1], state[0])], axis=2
    )


def _half_sweep_kernel(
    other_ref, lo_x_ref, hi_x_ref, lo_y_ref, hi_y_ref, face_ref, weight_ref, inverse_ref,
    target_ref, out_ref, send_lo_x_ref, send_hi_x_ref, send_lo_y_ref, send_hi_y_ref, *, span_x
):
    tile = 2 * R
    highest = lax.Precision.HIGHEST
    other = other_ref[...]
    lanes = other.shape[1]
    lane = lax.broadcasted_iota(jnp.int32, (P_SIZE, tile), 1)
    low_half = lane < R
    tiles = [other[:, t * tile:(t + 1) * tile] for t in range(span_x)]
    lo_y = lo_y_ref[...]
    hi_y = hi_y_ref[...]

    def y_block(packed, x):
        held = packed[:, (x // 2) * tile:(x // 2 + 1) * tile]
        return held if x % 2 == 0 else pltpu.roll(held, R, 1)

    below, above = [], []
    for x in range(span_x):
        rolled = pltpu.roll(tiles[x], R, 1)
        below.append(jnp.where(low_half, y_block(lo_y, x), rolled))
        above.append(jnp.where(low_half, rolled, pltpu.roll(y_block(hi_y, x), R, 1)))
    nearby = [
        jnp.concatenate([lo_x_ref[...], other[:, :lanes - tile]], axis=1),
        jnp.concatenate([other[:, tile:], hi_x_ref[...]], axis=1),
        jnp.concatenate(below, axis=1),
        jnp.concatenate(above, axis=1),
        other,
        other,
    ]
    stacked = jnp.concatenate(
        [weight_ref[face:face + 1, :] * nearby[face] for face in range(6)], axis=0
    )
    coupled = jnp.dot(face_ref[...], stacked, precision=highest, preferred_element_type=jnp.float32)
    rhs = target_ref[...] - coupled
    outs = []
    for x in range(span_x):
        part = rhs[:, x * tile:(x + 1) * tile]
        split = jnp.concatenate([jnp.where(low_half, part, 0.0), jnp.where(low_half, 0.0, part)], axis=0)
        outs.append(
            jnp.dot(
                inverse_ref[:, x * tile:(x + 1) * tile], split, precision=highest,
                preferred_element_type=jnp.float32,
            )
        )
    out_ref[...] = jnp.concatenate(outs, axis=1)
    send_lo_x_ref[...] = outs[-1]
    send_hi_x_ref[...] = outs[0]
    for t in range(span_x // 2):
        even, odd = outs[2 * t], outs[2 * t + 1]
        send_lo_y_ref[:, t * tile:(t + 1) * tile] = jnp.where(low_half, pltpu.roll(even, R, 1), odd)
        send_hi_y_ref[:, t * tile:(t + 1) * tile] = jnp.where(low_half, even, pltpu.roll(odd, R, 1))


def half_sweep(other, halos, face_blocks, weight, inverse, target, span_x):
    lanes = other.shape[1]
    x_shape = jax.ShapeDtypeStruct((P_SIZE, 2 * R), jnp.float32)
    y_shape = jax.ShapeDtypeStruct((P_SIZE, span_x * R), jnp.float32)
    vmem = pl.BlockSpec(memory_space=pltpu.VMEM)
    return pl.pallas_call(
        functools.partial(_half_sweep_kernel, span_x=span_x),
        out_shape=(jax.ShapeDtypeStruct((P_SIZE, lanes), jnp.float32), x_shape, x_shape, y_shape, y_shape),
        in_specs=[vmem] * 9,
        out_specs=(vmem,) * 5,
    )(other, *[
        pltpu.with_memory_space_constraint(value, pltpu.VMEM)
        for value in (*halos, face_blocks, weight, inverse, target)
    ])


def send_buffers(state, span_x):
    blocks = state.reshape(P_SIZE, span_x, 2, R)
    return (
        blocks[:, -1].reshape(P_SIZE, 2 * R),
        blocks[:, 0].reshape(P_SIZE, 2 * R),
        blocks[:, :, 1].reshape(P_SIZE, span_x * R),
        blocks[:, :, 0].reshape(P_SIZE, span_x * R),
    )


def trade(sends):
    lo_x, hi_x = (
        lax.ppermute(sends[0], "gx", shift_pairs("gx", 1)),
        lax.ppermute(sends[1], "gx", shift_pairs("gx", -1)),
    )
    lo_y, hi_y = (
        lax.ppermute(sends[2], "gy", shift_pairs("gy", 1)),
        lax.ppermute(sends[3], "gy", shift_pairs("gy", -1)),
    )
    return lo_x, hi_x, lo_y, hi_y


def shift_pairs(axis, step):
    count = lax.axis_size(axis)
    return [(i, (i + step) % count) for i in range(count)]


def lane_body(forcing, initial, blocks, face_blocks, strength, strong, colour, neighbours):
    span_x, span_y, span_z, width = forcing.shape
    count = span_x * span_y * span_z
    columns = span_x * span_y
    empty_slot = (span_x + 2) * (span_y + 2) * span_z
    first_is = [colour[:, :, 0] == paint for paint in (0, 1)]

    def pick(values, paint, axis=2):
        lead = (1,) * (axis - 2)
        mask = first_is[paint].reshape(lead + first_is[paint].shape + (1,) * (values.ndim - axis - 1))
        low = lax.index_in_dim(values, 0, axis=axis, keepdims=False)
        high = lax.index_in_dim(values, 1, axis=axis, keepdims=False)
        return jnp.where(mask, low, high)

    def to_lanes(values):
        return jnp.transpose(values.reshape(columns, P_SIZE, R), (1, 0, 2)).reshape(P_SIZE, columns * R)

    start_state = to_lanes(pick(initial, 1))
    first_halos = trade(send_buffers(start_state, span_x))
    by_colour = jnp.stack([pick(blocks, paint) for paint in (0, 1)]).reshape(count, P_SIZE, P_SIZE)
    inverse = block_inverses(by_colour, lanes_out=True)
    weight = jnp.where(neighbours == empty_slot, 0.0, strength * strong.astype(jnp.float32))
    member_inverse = [inverse[:, paint * columns * P_SIZE:(paint + 1) * columns * P_SIZE] for paint in (0, 1)]
    face_row = jnp.transpose(face_blocks, (1, 0, 2)).reshape(P_SIZE, 6 * P_SIZE)
    member_target = [to_lanes(pick(forcing, paint)) for paint in (0, 1)]
    member_weight = [
        jnp.pad(jnp.repeat(pick(weight, paint, axis=3).reshape(6, columns), R, axis=1), ((0, 2), (0, 0)))
        for paint in (0, 1)
    ]
    member_inverse, member_target, member_weight, face_row = lax.optimization_barrier(
        (member_inverse, member_target, member_weight, face_row)
    )
    state = [None, start_state]
    sends = None
    for sweep_index in range(SWEEPS):
        for paint_now in (0, 1):
            halos = first_halos if sends is None else trade(sends)
            state[paint_now], *sends = half_sweep(
                state[1 - paint_now],
                halos,
                face_row,
                member_weight[paint_now],
                member_inverse[paint_now],
                member_target[paint_now],
                span_x,
            )
    first = first_is[0][..., None]
    whole = [
        jnp.transpose(part.reshape(P_SIZE, columns, R), (1, 0, 2)).reshape(span_x, span_y, width)
        for part in state
    ]
    return jnp.stack(
        [jnp.where(first, whole[0], whole[1]), jnp.where(first, whole[1], whole[0])], axis=2
    )


def dispatch(forcing, *rest):
    span_x, span_y, span_z, width = forcing.shape
    if span_y == 2 and span_z == 2 and span_x % 2 == 0 and width == P_SIZE * R:
        return lane_body(forcing, *rest)
    return body(forcing, *rest)


def solution(mesh):
    in_specs = (
        P("gx", "gy", None, None),
        P("gx", "gy", None, None),
        P("gx", "gy", None, None),
        P(),
        P(None, "gx", "gy", None),
        P(None, "gx", "gy", None),
        P("gx", "gy", None),
        P(None, "gx", "gy", None),
    )
    out_specs = P("gx", "gy", None, None)
    return jax.shard_map(dispatch, mesh=mesh, in_specs=in_specs, out_specs=out_specs, check_vma=False)
```

```python
import functools

import jax
import jax.numpy as jnp
from jax import lax
from jax.experimental import pallas as pl
from jax.experimental.pallas import tpu as pltpu
from jax.sharding import PartitionSpec as P

P_SIZE = 64
R = 64
SWEEPS = 4


def padded(block, sides, width):
    for axis, dim in sides:
        count = lax.axis_size(axis)
        forward = [(i, i + 1) for i in range(count - 1)]
        backward = [(target, source) for source, target in forward]
        low = lax.ppermute(
            lax.slice_in_dim(block, block.shape[dim] - width, None, axis=dim), axis, forward
        )
        high = lax.ppermute(lax.slice_in_dim(block, 0, width, axis=dim), axis, backward)
        block = jnp.concatenate([low, block, high], axis=dim)
    return block


def _gauss_jordan_kernel(a_ref, o_ref, *, n, nb):
    lanes = n * nb
    tiles = lanes // 128
    o_ref[...] = a_ref[...]
    lane_t = lax.broadcasted_iota(jnp.int32, (n, 128), 1)
    lane_r = lax.broadcasted_iota(jnp.int32, (1, 128), 1)
    row_i = lax.broadcasted_iota(jnp.int32, (n, 128), 0)

    def spread(x):
        shift = nb
        while shift < 128:
            x = x + pltpu.roll(x, shift, 1)
            shift *= 2
        return x

    def step(k, carry):
        start = k * nb
        tile = start // 128
        off = start % 128
        tile_start = pl.multiple_of(tile * 128, 128)
        column = spread(
            jnp.where((lane_t >= off) & (lane_t < off + nb), o_ref[:, pl.ds(tile_start, 128)], 0.0)
        )
        pivot = jnp.sum(jnp.where(row_i == k, column, 0.0), axis=0, keepdims=True)
        base = pl.multiple_of((k // 8) * 8, 8)
        band = o_ref[pl.ds(base, 8), :]
        band_i = lax.broadcasted_iota(jnp.int32, band.shape, 0)
        row = jnp.sum(jnp.where(band_i == k - base, band, 0.0), axis=0, keepdims=True)
        for t in range(tiles):
            in_col = (t == tile) & (lane_r >= off) & (lane_r < off + nb)
            scaled = jnp.where(in_col, 1.0 / pivot, row[:, t * 128:(t + 1) * 128] / pivot)
            kept = jnp.where(in_col, 0.0, o_ref[:, t * 128:(t + 1) * 128])
            o_ref[:, t * 128:(t + 1) * 128] = jnp.where(row_i == k, scaled, kept - column * scaled)
        return carry

    lax.fori_loop(0, n, step, 0)


def block_inverses(matrices, lanes_out=False):
    nb, n, _ = matrices.shape
    if 128 % nb or (n * nb) % 128:
        assert not lanes_out
        lower_factor = jnp.linalg.cholesky(matrices)
        identity = jnp.broadcast_to(jnp.eye(n, dtype=matrices.dtype), matrices.shape)
        solved = jax.scipy.linalg.solve_triangular(lower_factor, identity, lower=True)
        return jnp.einsum("eqp,eqr->epr", solved, solved, precision=lax.Precision.HIGHEST)
    packed = jnp.transpose(matrices, (1, 2, 0)).reshape(n, n * nb)
    inverted = pl.pallas_call(
        functools.partial(_gauss_jordan_kernel, n=n, nb=nb),
        out_shape=jax.ShapeDtypeStruct((n, n * nb), jnp.float32),
        in_specs=[pl.BlockSpec(memory_space=pltpu.VMEM)],
        out_specs=pl.BlockSpec(memory_space=pltpu.VMEM),
        cost_estimate=pl.CostEstimate(
            flops=2000 * n ** 3 * nb, transcendentals=0, bytes_accessed=8 * n * n * nb
        ),
    )(packed)
    if lanes_out:
        return jnp.transpose(inverted.reshape(n, n, nb), (0, 2, 1)).reshape(n, nb * n)
    return jnp.transpose(inverted.reshape(n, n, nb), (2, 0, 1))


def shifted(values, halo, dim, lower):
    width = values.shape[dim]
    if lower:
        return jnp.concatenate([halo, lax.slice_in_dim(values, 0, width - 1, axis=dim)], axis=dim)
    return jnp.concatenate([lax.slice_in_dim(values, 1, width, axis=dim), halo], axis=dim)


def exchange(values, axis, dim):
    count = lax.axis_size(axis)
    forward = [(i, i + 1) for i in range(count - 1)]
    backward = [(target, source) for source, target in forward]
    width = values.shape[dim]
    from_lower = lax.ppermute(lax.slice_in_dim(values, width - 1, width, axis=dim), axis, forward)
    from_upper = lax.ppermute(lax.slice_in_dim(values, 0, 1, axis=dim), axis, backward)
    return from_lower, from_upper


def body(forcing, initial, blocks, face_blocks, strength, strong, colour, neighbours):
    span_x, span_y, span_z, width = forcing.shape
    count = span_x * span_y * span_z
    columns = span_x * span_y
    empty_slot = (span_x + 2) * (span_y + 2) * span_z
    inverse = block_inverses(blocks.reshape(count, P_SIZE, P_SIZE)).reshape(
        span_x, span_y, span_z, P_SIZE, P_SIZE
    )
    weight = jnp.where(neighbours == empty_slot, 0.0, strength * strong.astype(jnp.float32))
    first_is = [colour[:, :, 0] == paint for paint in (0, 1)]

    def pick(values, paint, axis=2):
        lead = (1,) * (axis - 2)
        mask = first_is[paint].reshape(lead + first_is[paint].shape + (1,) * (values.ndim - axis - 1))
        low = lax.index_in_dim(values, 0, axis=axis, keepdims=False)
        high = lax.index_in_dim(values, 1, axis=axis, keepdims=False)
        return jnp.where(mask, low, high)

    member_inverse = [inverse[:, paint * columns * P_SIZE:(paint + 1) * columns * P_SIZE] for paint in (0, 1)]
    face_row = jnp.transpose(face_blocks, (1, 0, 2)).reshape(P_SIZE, 6 * P_SIZE)
    member_target = [pick(forcing, paint).reshape(columns, P_SIZE, R) for paint in (0, 1)]
    member_weight = [pick(weight, paint, axis=3)[..., None] for paint in (0, 1)]
    state = [pick(initial, 0), pick(initial, 1)]
    for sweep_index in range(SWEEPS):
        for paint_now in (0, 1):
            other = state[1 - paint_now]
            low_x, high_x = exchange(other, "gx", 0)
            low_y, high_y = exchange(other, "gy", 1)
            nearby = jnp.stack(
                [
                    shifted(other, low_x, 0, True),
                    shifted(other, high_x, 0, False),
                    shifted(other, low_y, 1, True),
                    shifted(other, high_y, 1, False),
                    other,
                    other,
                ]
            )
            nearby = (nearby * member_weight[paint_now]).reshape(6, columns, P_SIZE, R)
            coupled = jnp.einsum(
                "fpq,feqr->epr", face_blocks, nearby, precision=lax.Precision.HIGHEST
            )
            update = jnp.einsum(
                "epq,eqr->epr",
                member_inverse[paint_now],
                member_target[paint_now] - coupled,
                precision=lax.Precision.HIGHEST,
            )
            state[paint_now] = update.reshape(span_x, span_y, width)
    first = first_is[0][..., None]
    return jnp.stack(
        [jnp.where(first, state[0], state[1]), jnp.where(first, state[1], state[0])], axis=2
    )


def _half_sweep_kernel(
    other_ref, lo_x_ref, hi_x_ref, lo_y_ref, hi_y_ref, face_ref, weight_ref, inverse_ref,
    target_ref, previous_ref, out_ref, send_lo_x_ref, send_hi_x_ref, send_lo_y_ref, send_hi_y_ref, *, span_x
):
    tile = 2 * R
    highest = lax.Precision.HIGHEST
    other = other_ref[...]
    lanes = other.shape[1]
    lane = lax.broadcasted_iota(jnp.int32, (P_SIZE, tile), 1)
    low_half = lane < R
    tiles = [other[:, t * tile:(t + 1) * tile] for t in range(span_x)]
    lo_y = lo_y_ref[...]
    hi_y = hi_y_ref[...]

    def y_block(packed, x):
        held = packed[:, (x // 2) * tile:(x // 2 + 1) * tile]
        return held if x % 2 == 0 else pltpu.roll(held, R, 1)

    below, above = [], []
    for x in range(span_x):
        rolled = pltpu.roll(tiles[x], R, 1)
        below.append(jnp.where(low_half, y_block(lo_y, x), rolled))
        above.append(jnp.where(low_half, rolled, pltpu.roll(y_block(hi_y, x), R, 1)))
    nearby = [
        jnp.concatenate([lo_x_ref[...], other[:, :lanes - tile]], axis=1),
        jnp.concatenate([other[:, tile:], hi_x_ref[...]], axis=1),
        jnp.concatenate(below, axis=1),
        jnp.concatenate(above, axis=1),
        other,
        other,
    ]
    stacked = jnp.concatenate(
        [weight_ref[face:face + 1, :] * nearby[face] for face in range(6)], axis=0
    )
    coupled = jnp.dot(face_ref[...], stacked, precision=highest, preferred_element_type=jnp.float32)
    rhs = target_ref[...] - coupled
    outs = []
    for x in range(span_x):
        part = rhs[:, x * tile:(x + 1) * tile]
        split = jnp.concatenate([jnp.where(low_half, part, 0.0), jnp.where(low_half, 0.0, part)], axis=0)
        outs.append(
            jnp.dot(
                inverse_ref[:, x * tile:(x + 1) * tile], split, precision=highest,
                preferred_element_type=jnp.float32,
            )
        )
    out_ref[...] = jnp.concatenate(outs, axis=1)
    send_lo_x_ref[...] = outs[-1]
    send_hi_x_ref[...] = outs[0]
    for t in range(span_x // 2):
        even, odd = outs[2 * t], outs[2 * t + 1]
        send_lo_y_ref[:, t * tile:(t + 1) * tile] = jnp.where(low_half, pltpu.roll(even, R, 1), odd)
        send_hi_y_ref[:, t * tile:(t + 1) * tile] = jnp.where(low_half, even, pltpu.roll(odd, R, 1))


def half_sweep(other, halos, face_blocks, weight, inverse, target, previous, span_x):
    lanes = other.shape[1]
    x_shape = jax.ShapeDtypeStruct((P_SIZE, 2 * R), jnp.float32)
    y_shape = jax.ShapeDtypeStruct((P_SIZE, span_x * R), jnp.float32)
    vmem = pl.BlockSpec(memory_space=pltpu.VMEM)
    return pl.pallas_call(
        functools.partial(_half_sweep_kernel, span_x=span_x),
        out_shape=(jax.ShapeDtypeStruct((P_SIZE, lanes), jnp.float32), x_shape, x_shape, y_shape, y_shape),
        in_specs=[vmem] * 10,
        out_specs=(vmem,) * 5,
        input_output_aliases={9: 0},
    )(*[
        pltpu.with_memory_space_constraint(value, pltpu.VMEM)
        for value in (other, *halos, face_blocks, weight, inverse, target, previous)
    ])


def send_buffers(state, span_x):
    blocks = state.reshape(P_SIZE, span_x, 2, R)
    return (
        blocks[:, -1].reshape(P_SIZE, 2 * R),
        blocks[:, 0].reshape(P_SIZE, 2 * R),
        blocks[:, :, 1].reshape(P_SIZE, span_x * R),
        blocks[:, :, 0].reshape(P_SIZE, span_x * R),
    )


def trade(sends):
    lo_x, hi_x = (
        lax.ppermute(sends[0], "gx", shift_pairs("gx", 1)),
        lax.ppermute(sends[1], "gx", shift_pairs("gx", -1)),
    )
    lo_y, hi_y = (
        lax.ppermute(sends[2], "gy", shift_pairs("gy", 1)),
        lax.ppermute(sends[3], "gy", shift_pairs("gy", -1)),
    )
    return lo_x, hi_x, lo_y, hi_y


def shift_pairs(axis, step):
    count = lax.axis_size(axis)
    return [(i, (i + step) % count) for i in range(count)]


def lane_body(forcing, initial, blocks, face_blocks, strength, strong, colour, neighbours):
    span_x, span_y, span_z, width = forcing.shape
    count = span_x * span_y * span_z
    columns = span_x * span_y
    empty_slot = (span_x + 2) * (span_y + 2) * span_z
    first_is = [colour[:, :, 0] == paint for paint in (0, 1)]

    def pick(values, paint, axis=2):
        lead = (1,) * (axis - 2)
        mask = first_is[paint].reshape(lead + first_is[paint].shape + (1,) * (values.ndim - axis - 1))
        low = lax.index_in_dim(values, 0, axis=axis, keepdims=False)
        high = lax.index_in_dim(values, 1, axis=axis, keepdims=False)
        return jnp.where(mask, low, high)

    def to_lanes(values):
        return jnp.transpose(values.reshape(columns, P_SIZE, R), (1, 0, 2)).reshape(P_SIZE, columns * R)

    start_state = to_lanes(pick(initial, 1))
    first_halos = trade(send_buffers(start_state, span_x))
    by_colour = jnp.stack([pick(blocks, paint) for paint in (0, 1)]).reshape(count, P_SIZE, P_SIZE)
    inverse = block_inverses(by_colour, lanes_out=True)
    weight = jnp.where(neighbours == empty_slot, 0.0, strength * strong.astype(jnp.float32))
    member_inverse = [inverse[:, paint * columns * P_SIZE:(paint + 1) * columns * P_SIZE] for paint in (0, 1)]
    face_row = jnp.transpose(face_blocks, (1, 0, 2)).reshape(P_SIZE, 6 * P_SIZE)
    member_target = [to_lanes(pick(forcing, paint)) for paint in (0, 1)]
    member_weight = [
        jnp.pad(jnp.repeat(pick(weight, paint, axis=3).reshape(6, columns), R, axis=1), ((0, 2), (0, 0)))
        for paint in (0, 1)
    ]
    member_inverse, member_target, member_weight, face_row = lax.optimization_barrier(
        (member_inverse, member_target, member_weight, face_row)
    )
    state = [jnp.zeros_like(start_state), start_state]
    sends = None
    for sweep_index in range(SWEEPS):
        for paint_now in (0, 1):
            halos = first_halos if sends is None else trade(sends)
            state[paint_now], *sends = half_sweep(
                state[1 - paint_now],
                halos,
                face_row,
                member_weight[paint_now],
                member_inverse[paint_now],
                member_target[paint_now],
                state[paint_now],
                span_x,
            )
    first = first_is[0][..., None]
    whole = [
        jnp.transpose(part.reshape(P_SIZE, columns, R), (1, 0, 2)).reshape(span_x, span_y, width)
        for part in state
    ]
    return jnp.stack(
        [jnp.where(first, whole[0], whole[1]), jnp.where(first, whole[1], whole[0])], axis=2
    )


def dispatch(forcing, *rest):
    span_x, span_y, span_z, width = forcing.shape
    if span_y == 2 and span_z == 2 and span_x % 2 == 0 and width == P_SIZE * R:
        return lane_body(forcing, *rest)
    return body(forcing, *rest)


def solution(mesh):
    in_specs = (
        P("gx", "gy", None, None),
        P("gx", "gy", None, None),
        P("gx", "gy", None, None),
        P(),
        P(None, "gx", "gy", None),
        P(None, "gx", "gy", None),
        P("gx", "gy", None),
        P(None, "gx", "gy", None),
    )
    out_specs = P("gx", "gy", None, None)
    return jax.shard_map(dispatch, mesh=mesh, in_specs=in_specs, out_specs=out_specs, check_vma=False)
```

```python
import functools

import jax
import jax.numpy as jnp
from jax import lax
from jax.experimental import pallas as pl
from jax.experimental.pallas import tpu as pltpu
from jax.sharding import PartitionSpec as P

P_SIZE = 64
R = 64
SWEEPS = 4


def padded(block, sides, width):
    for axis, dim in sides:
        count = lax.axis_size(axis)
        forward = [(i, i + 1) for i in range(count - 1)]
        backward = [(target, source) for source, target in forward]
        low = lax.ppermute(
            lax.slice_in_dim(block, block.shape[dim] - width, None, axis=dim), axis, forward
        )
        high = lax.ppermute(lax.slice_in_dim(block, 0, width, axis=dim), axis, backward)
        block = jnp.concatenate([low, block, high], axis=dim)
    return block


def _gauss_jordan_kernel(a_ref, o_ref, *, n, nb):
    lanes = n * nb
    tiles = lanes // 128
    o_ref[...] = a_ref[...]
    lane_t = lax.broadcasted_iota(jnp.int32, (n, 128), 1)
    lane_r = lax.broadcasted_iota(jnp.int32, (1, 128), 1)
    row_i = lax.broadcasted_iota(jnp.int32, (n, 128), 0)

    def spread(x):
        shift = nb
        while shift < 128:
            x = x + pltpu.roll(x, shift, 1)
            shift *= 2
        return x

    def step(k, carry):
        start = k * nb
        tile = start // 128
        off = start % 128
        tile_start = pl.multiple_of(tile * 128, 128)
        column = spread(
            jnp.where((lane_t >= off) & (lane_t < off + nb), o_ref[:, pl.ds(tile_start, 128)], 0.0)
        )
        pivot = jnp.sum(jnp.where(row_i == k, column, 0.0), axis=0, keepdims=True)
        base = pl.multiple_of((k // 8) * 8, 8)
        band = o_ref[pl.ds(base, 8), :]
        band_i = lax.broadcasted_iota(jnp.int32, band.shape, 0)
        row = jnp.sum(jnp.where(band_i == k - base, band, 0.0), axis=0, keepdims=True)
        for t in range(tiles):
            in_col = (t == tile) & (lane_r >= off) & (lane_r < off + nb)
            scaled = jnp.where(in_col, 1.0 / pivot, row[:, t * 128:(t + 1) * 128] / pivot)
            kept = jnp.where(in_col, 0.0, o_ref[:, t * 128:(t + 1) * 128])
            o_ref[:, t * 128:(t + 1) * 128] = jnp.where(row_i == k, scaled, kept - column * scaled)
        return carry

    lax.fori_loop(0, n, step, 0)


def block_inverses(matrices, lanes_out=False):
    nb, n, _ = matrices.shape
    if 128 % nb or (n * nb) % 128:
        assert not lanes_out
        lower_factor = jnp.linalg.cholesky(matrices)
        identity = jnp.broadcast_to(jnp.eye(n, dtype=matrices.dtype), matrices.shape)
        solved = jax.scipy.linalg.solve_triangular(lower_factor, identity, lower=True)
        return jnp.einsum("eqp,eqr->epr", solved, solved, precision=lax.Precision.HIGHEST)
    packed = jnp.transpose(matrices, (1, 2, 0)).reshape(n, n * nb)
    inverted = pl.pallas_call(
        functools.partial(_gauss_jordan_kernel, n=n, nb=nb),
        out_shape=jax.ShapeDtypeStruct((n, n * nb), jnp.float32),
        in_specs=[pl.BlockSpec(memory_space=pltpu.VMEM)],
        out_specs=pl.BlockSpec(memory_space=pltpu.VMEM),
        cost_estimate=pl.CostEstimate(
            flops=2000 * n ** 3 * nb, transcendentals=0, bytes_accessed=8 * n * n * nb
        ),
    )(packed)
    if lanes_out:
        return jnp.transpose(inverted.reshape(n, n, nb), (0, 2, 1)).reshape(n, nb * n)
    return jnp.transpose(inverted.reshape(n, n, nb), (2, 0, 1))


def shifted(values, halo, dim, lower):
    width = values.shape[dim]
    if lower:
        return jnp.concatenate([halo, lax.slice_in_dim(values, 0, width - 1, axis=dim)], axis=dim)
    return jnp.concatenate([lax.slice_in_dim(values, 1, width, axis=dim), halo], axis=dim)


def exchange(values, axis, dim):
    count = lax.axis_size(axis)
    forward = [(i, i + 1) for i in range(count - 1)]
    backward = [(target, source) for source, target in forward]
    width = values.shape[dim]
    from_lower = lax.ppermute(lax.slice_in_dim(values, width - 1, width, axis=dim), axis, forward)
    from_upper = lax.ppermute(lax.slice_in_dim(values, 0, 1, axis=dim), axis, backward)
    return from_lower, from_upper


def body(forcing, initial, blocks, face_blocks, strength, strong, colour, neighbours):
    span_x, span_y, span_z, width = forcing.shape
    count = span_x * span_y * span_z
    columns = span_x * span_y
    empty_slot = (span_x + 2) * (span_y + 2) * span_z
    inverse = block_inverses(blocks.reshape(count, P_SIZE, P_SIZE)).reshape(
        span_x, span_y, span_z, P_SIZE, P_SIZE
    )
    weight = jnp.where(neighbours == empty_slot, 0.0, strength * strong.astype(jnp.float32))
    first_is = [colour[:, :, 0] == paint for paint in (0, 1)]

    def pick(values, paint, axis=2):
        lead = (1,) * (axis - 2)
        mask = first_is[paint].reshape(lead + first_is[paint].shape + (1,) * (values.ndim - axis - 1))
        low = lax.index_in_dim(values, 0, axis=axis, keepdims=False)
        high = lax.index_in_dim(values, 1, axis=axis, keepdims=False)
        return jnp.where(mask, low, high)

    member_inverse = [inverse[:, paint * columns * P_SIZE:(paint + 1) * columns * P_SIZE] for paint in (0, 1)]
    face_row = jnp.transpose(face_blocks, (1, 0, 2)).reshape(P_SIZE, 6 * P_SIZE)
    member_target = [pick(forcing, paint).reshape(columns, P_SIZE, R) for paint in (0, 1)]
    member_weight = [pick(weight, paint, axis=3)[..., None] for paint in (0, 1)]
    state = [pick(initial, 0), pick(initial, 1)]
    for sweep_index in range(SWEEPS):
        for paint_now in (0, 1):
            other = state[1 - paint_now]
            low_x, high_x = exchange(other, "gx", 0)
            low_y, high_y = exchange(other, "gy", 1)
            nearby = jnp.stack(
                [
                    shifted(other, low_x, 0, True),
                    shifted(other, high_x, 0, False),
                    shifted(other, low_y, 1, True),
                    shifted(other, high_y, 1, False),
                    other,
                    other,
                ]
            )
            nearby = (nearby * member_weight[paint_now]).reshape(6, columns, P_SIZE, R)
            coupled = jnp.einsum(
                "fpq,feqr->epr", face_blocks, nearby, precision=lax.Precision.HIGHEST
            )
            update = jnp.einsum(
                "epq,eqr->epr",
                member_inverse[paint_now],
                member_target[paint_now] - coupled,
                precision=lax.Precision.HIGHEST,
            )
            state[paint_now] = update.reshape(span_x, span_y, width)
    first = first_is[0][..., None]
    return jnp.stack(
        [jnp.where(first, state[0], state[1]), jnp.where(first, state[1], state[0])], axis=2
    )


def _half_sweep_kernel(
    other_ref, lo_x_ref, hi_x_ref, lo_y_ref, hi_y_ref, face_ref, weight_ref, inverse_ref,
    target_ref, previous_ref, old_lo_x, old_hi_x, old_lo_y, old_hi_y, out_ref, send_lo_x_ref, send_hi_x_ref, send_lo_y_ref, send_hi_y_ref, *, span_x
):
    tile = 2 * R
    highest = lax.Precision.HIGHEST
    other = other_ref[...]
    lanes = other.shape[1]
    lane = lax.broadcasted_iota(jnp.int32, (P_SIZE, tile), 1)
    low_half = lane < R
    tiles = [other[:, t * tile:(t + 1) * tile] for t in range(span_x)]
    lo_y = lo_y_ref[...]
    hi_y = hi_y_ref[...]

    def y_block(packed, x):
        held = packed[:, (x // 2) * tile:(x // 2 + 1) * tile]
        return held if x % 2 == 0 else pltpu.roll(held, R, 1)

    below, above = [], []
    for x in range(span_x):
        rolled = pltpu.roll(tiles[x], R, 1)
        below.append(jnp.where(low_half, y_block(lo_y, x), rolled))
        above.append(jnp.where(low_half, rolled, pltpu.roll(y_block(hi_y, x), R, 1)))
    nearby = [
        jnp.concatenate([lo_x_ref[...], other[:, :lanes - tile]], axis=1),
        jnp.concatenate([other[:, tile:], hi_x_ref[...]], axis=1),
        jnp.concatenate(below, axis=1),
        jnp.concatenate(above, axis=1),
        other,
        other,
    ]
    stacked = jnp.concatenate(
        [weight_ref[face:face + 1, :] * nearby[face] for face in range(6)], axis=0
    )
    coupled = jnp.dot(face_ref[...], stacked, precision=highest, preferred_element_type=jnp.float32)
    rhs = target_ref[...] - coupled
    outs = []
    for x in range(span_x):
        part = rhs[:, x * tile:(x + 1) * tile]
        split = jnp.concatenate([jnp.where(low_half, part, 0.0), jnp.where(low_half, 0.0, part)], axis=0)
        outs.append(
            jnp.dot(
                inverse_ref[:, x * tile:(x + 1) * tile], split, precision=highest,
                preferred_element_type=jnp.float32,
            )
        )
    out_ref[...] = jnp.concatenate(outs, axis=1)
    send_lo_x_ref[...] = outs[-1]
    send_hi_x_ref[...] = outs[0]
    for t in range(span_x // 2):
        even, odd = outs[2 * t], outs[2 * t + 1]
        send_lo_y_ref[:, t * tile:(t + 1) * tile] = jnp.where(low_half, pltpu.roll(even, R, 1), odd)
        send_hi_y_ref[:, t * tile:(t + 1) * tile] = jnp.where(low_half, even, pltpu.roll(odd, R, 1))


def half_sweep(other, halos, face_blocks, weight, inverse, target, previous, old_sends, span_x):
    lanes = other.shape[1]
    x_shape = jax.ShapeDtypeStruct((P_SIZE, 2 * R), jnp.float32)
    y_shape = jax.ShapeDtypeStruct((P_SIZE, span_x * R), jnp.float32)
    vmem = pl.BlockSpec(memory_space=pltpu.VMEM)
    return pl.pallas_call(
        functools.partial(_half_sweep_kernel, span_x=span_x),
        out_shape=(jax.ShapeDtypeStruct((P_SIZE, lanes), jnp.float32), x_shape, x_shape, y_shape, y_shape),
        in_specs=[vmem] * 14,
        out_specs=(vmem,) * 5,
        input_output_aliases={9: 0, 10: 1, 11: 2, 12: 3, 13: 4},
    )(*[
        pltpu.with_memory_space_constraint(value, pltpu.VMEM)
        for value in (other, *halos, face_blocks, weight, inverse, target, previous, *old_sends)
    ])


def send_buffers(state, span_x):
    blocks = state.reshape(P_SIZE, span_x, 2, R)
    return (
        blocks[:, -1].reshape(P_SIZE, 2 * R),
        blocks[:, 0].reshape(P_SIZE, 2 * R),
        blocks[:, :, 1].reshape(P_SIZE, span_x * R),
        blocks[:, :, 0].reshape(P_SIZE, span_x * R),
    )


def trade(sends):
    lo_x, hi_x = (
        lax.ppermute(sends[0], "gx", shift_pairs("gx", 1)),
        lax.ppermute(sends[1], "gx", shift_pairs("gx", -1)),
    )
    lo_y, hi_y = (
        lax.ppermute(sends[2], "gy", shift_pairs("gy", 1)),
        lax.ppermute(sends[3], "gy", shift_pairs("gy", -1)),
    )
    return lo_x, hi_x, lo_y, hi_y


def shift_pairs(axis, step):
    count = lax.axis_size(axis)
    return [(i, (i + step) % count) for i in range(count)]


def lane_body(forcing, initial, blocks, face_blocks, strength, strong, colour, neighbours):
    span_x, span_y, span_z, width = forcing.shape
    count = span_x * span_y * span_z
    columns = span_x * span_y
    empty_slot = (span_x + 2) * (span_y + 2) * span_z
    first_is = [colour[:, :, 0] == paint for paint in (0, 1)]

    def pick(values, paint, axis=2):
        lead = (1,) * (axis - 2)
        mask = first_is[paint].reshape(lead + first_is[paint].shape + (1,) * (values.ndim - axis - 1))
        low = lax.index_in_dim(values, 0, axis=axis, keepdims=False)
        high = lax.index_in_dim(values, 1, axis=axis, keepdims=False)
        return jnp.where(mask, low, high)

    def to_lanes(values):
        return jnp.transpose(values.reshape(columns, P_SIZE, R), (1, 0, 2)).reshape(P_SIZE, columns * R)

    start_state = to_lanes(pick(initial, 1))
    first_sends = send_buffers(start_state, span_x)
    first_halos = trade(first_sends)
    by_colour = jnp.stack([pick(blocks, paint) for paint in (0, 1)]).reshape(count, P_SIZE, P_SIZE)
    inverse = block_inverses(by_colour, lanes_out=True)
    weight = jnp.where(neighbours == empty_slot, 0.0, strength * strong.astype(jnp.float32))
    member_inverse = [inverse[:, paint * columns * P_SIZE:(paint + 1) * columns * P_SIZE] for paint in (0, 1)]
    face_row = jnp.transpose(face_blocks, (1, 0, 2)).reshape(P_SIZE, 6 * P_SIZE)
    member_target = [to_lanes(pick(forcing, paint)) for paint in (0, 1)]
    member_weight = [
        jnp.pad(jnp.repeat(pick(weight, paint, axis=3).reshape(6, columns), R, axis=1), ((0, 2), (0, 0)))
        for paint in (0, 1)
    ]
    member_inverse, member_target, member_weight, face_row = lax.optimization_barrier(
        (member_inverse, member_target, member_weight, face_row)
    )
    state = [jnp.zeros_like(start_state), start_state]
    sends = None
    for sweep_index in range(SWEEPS):
        for paint_now in (0, 1):
            halos = first_halos if sends is None else trade(sends)
            state[paint_now], *sends = half_sweep(
                state[1 - paint_now],
                halos,
                face_row,
                member_weight[paint_now],
                member_inverse[paint_now],
                member_target[paint_now],
                state[paint_now],
                first_sends if sends is None else sends,
                span_x,
            )
    first = first_is[0][..., None]
    whole = [
        jnp.transpose(part.reshape(P_SIZE, columns, R), (1, 0, 2)).reshape(span_x, span_y, width)
        for part in state
    ]
    return jnp.stack(
        [jnp.where(first, whole[0], whole[1]), jnp.where(first, whole[1], whole[0])], axis=2
    )


def dispatch(forcing, *rest):
    span_x, span_y, span_z, width = forcing.shape
    if span_y == 2 and span_z == 2 and span_x % 2 == 0 and width == P_SIZE * R:
        return lane_body(forcing, *rest)
    return body(forcing, *rest)


def solution(mesh):
    in_specs = (
        P("gx", "gy", None, None),
        P("gx", "gy", None, None),
        P("gx", "gy", None, None),
        P(),
        P(None, "gx", "gy", None),
        P(None, "gx", "gy", None),
        P("gx", "gy", None),
        P(None, "gx", "gy", None),
    )
    out_specs = P("gx", "gy", None, None)
    return jax.shard_map(dispatch, mesh=mesh, in_specs=in_specs, out_specs=out_specs, check_vma=False)
```

```python
import functools

import jax
import jax.numpy as jnp
from jax import lax
from jax.experimental import pallas as pl
from jax.experimental.pallas import tpu as pltpu
from jax.sharding import PartitionSpec as P

P_SIZE = 64
R = 64
SWEEPS = 4


def padded(block, sides, width):
    for axis, dim in sides:
        count = lax.axis_size(axis)
        forward = [(i, i + 1) for i in range(count - 1)]
        backward = [(target, source) for source, target in forward]
        low = lax.ppermute(
            lax.slice_in_dim(block, block.shape[dim] - width, None, axis=dim), axis, forward
        )
        high = lax.ppermute(lax.slice_in_dim(block, 0, width, axis=dim), axis, backward)
        block = jnp.concatenate([low, block, high], axis=dim)
    return block


def _gauss_jordan_kernel(a_ref, o_ref, *, n, nb):
    lanes = n * nb
    tiles = lanes // 128
    del a_ref
    lane_t = lax.broadcasted_iota(jnp.int32, (n, 128), 1)
    lane_r = lax.broadcasted_iota(jnp.int32, (1, 128), 1)
    row_i = lax.broadcasted_iota(jnp.int32, (n, 128), 0)

    def spread(x):
        shift = nb
        while shift < 128:
            x = x + pltpu.roll(x, shift, 1)
            shift *= 2
        return x

    def step(k, carry):
        start = k * nb
        tile = start // 128
        off = start % 128
        tile_start = pl.multiple_of(tile * 128, 128)
        column = spread(
            jnp.where((lane_t >= off) & (lane_t < off + nb), o_ref[:, pl.ds(tile_start, 128)], 0.0)
        )
        pivot = jnp.sum(jnp.where(row_i == k, column, 0.0), axis=0, keepdims=True)
        base = pl.multiple_of((k // 8) * 8, 8)
        band = o_ref[pl.ds(base, 8), :]
        band_i = lax.broadcasted_iota(jnp.int32, band.shape, 0)
        row = jnp.sum(jnp.where(band_i == k - base, band, 0.0), axis=0, keepdims=True)
        for t in range(tiles):
            in_col = (t == tile) & (lane_r >= off) & (lane_r < off + nb)
            scaled = jnp.where(in_col, 1.0 / pivot, row[:, t * 128:(t + 1) * 128] / pivot)
            kept = jnp.where(in_col, 0.0, o_ref[:, t * 128:(t + 1) * 128])
            o_ref[:, t * 128:(t + 1) * 128] = jnp.where(row_i == k, scaled, kept - column * scaled)
        return carry

    lax.fori_loop(0, n, step, 0)


def block_inverses(matrices, lanes_out=False):
    nb, n, _ = matrices.shape
    if 128 % nb or (n * nb) % 128:
        assert not lanes_out
        lower_factor = jnp.linalg.cholesky(matrices)
        identity = jnp.broadcast_to(jnp.eye(n, dtype=matrices.dtype), matrices.shape)
        solved = jax.scipy.linalg.solve_triangular(lower_factor, identity, lower=True)
        return jnp.einsum("eqp,eqr->epr", solved, solved, precision=lax.Precision.HIGHEST)
    packed = jnp.transpose(matrices, (1, 2, 0)).reshape(n, n * nb)
    inverted = pl.pallas_call(
        functools.partial(_gauss_jordan_kernel, n=n, nb=nb),
        out_shape=jax.ShapeDtypeStruct((n, n * nb), jnp.float32),
        in_specs=[pl.BlockSpec(memory_space=pltpu.VMEM)],
        out_specs=pl.BlockSpec(memory_space=pltpu.VMEM),
        input_output_aliases={0: 0},
        cost_estimate=pl.CostEstimate(
            flops=2000 * n ** 3 * nb, transcendentals=0, bytes_accessed=8 * n * n * nb
        ),
    )(pltpu.with_memory_space_constraint(packed, pltpu.VMEM))
    if lanes_out:
        return jnp.transpose(inverted.reshape(n, n, nb), (0, 2, 1)).reshape(n, nb * n)
    return jnp.transpose(inverted.reshape(n, n, nb), (2, 0, 1))


def shifted(values, halo, dim, lower):
    width = values.shape[dim]
    if lower:
        return jnp.concatenate([halo, lax.slice_in_dim(values, 0, width - 1, axis=dim)], axis=dim)
    return jnp.concatenate([lax.slice_in_dim(values, 1, width, axis=dim), halo], axis=dim)


def exchange(values, axis, dim):
    count = lax.axis_size(axis)
    forward = [(i, i + 1) for i in range(count - 1)]
    backward = [(target, source) for source, target in forward]
    width = values.shape[dim]
    from_lower = lax.ppermute(lax.slice_in_dim(values, width - 1, width, axis=dim), axis, forward)
    from_upper = lax.ppermute(lax.slice_in_dim(values, 0, 1, axis=dim), axis, backward)
    return from_lower, from_upper


def body(forcing, initial, blocks, face_blocks, strength, strong, colour, neighbours):
    span_x, span_y, span_z, width = forcing.shape
    count = span_x * span_y * span_z
    columns = span_x * span_y
    empty_slot = (span_x + 2) * (span_y + 2) * span_z
    inverse = block_inverses(blocks.reshape(count, P_SIZE, P_SIZE)).reshape(
        span_x, span_y, span_z, P_SIZE, P_SIZE
    )
    weight = jnp.where(neighbours == empty_slot, 0.0, strength * strong.astype(jnp.float32))
    first_is = [colour[:, :, 0] == paint for paint in (0, 1)]

    def pick(values, paint, axis=2):
        lead = (1,) * (axis - 2)
        mask = first_is[paint].reshape(lead + first_is[paint].shape + (1,) * (values.ndim - axis - 1))
        low = lax.index_in_dim(values, 0, axis=axis, keepdims=False)
        high = lax.index_in_dim(values, 1, axis=axis, keepdims=False)
        return jnp.where(mask, low, high)

    member_inverse = [inverse[:, paint * columns * P_SIZE:(paint + 1) * columns * P_SIZE] for paint in (0, 1)]
    face_row = jnp.transpose(face_blocks, (1, 0, 2)).reshape(P_SIZE, 6 * P_SIZE)
    member_target = [pick(forcing, paint).reshape(columns, P_SIZE, R) for paint in (0, 1)]
    member_weight = [pick(weight, paint, axis=3)[..., None] for paint in (0, 1)]
    state = [pick(initial, 0), pick(initial, 1)]
    for sweep_index in range(SWEEPS):
        for paint_now in (0, 1):
            other = state[1 - paint_now]
            low_x, high_x = exchange(other, "gx", 0)
            low_y, high_y = exchange(other, "gy", 1)
            nearby = jnp.stack(
                [
                    shifted(other, low_x, 0, True),
                    shifted(other, high_x, 0, False),
                    shifted(other, low_y, 1, True),
                    shifted(other, high_y, 1, False),
                    other,
                    other,
                ]
            )
            nearby = (nearby * member_weight[paint_now]).reshape(6, columns, P_SIZE, R)
            coupled = jnp.einsum(
                "fpq,feqr->epr", face_blocks, nearby, precision=lax.Precision.HIGHEST
            )
            update = jnp.einsum(
                "epq,eqr->epr",
                member_inverse[paint_now],
                member_target[paint_now] - coupled,
                precision=lax.Precision.HIGHEST,
            )
            state[paint_now] = update.reshape(span_x, span_y, width)
    first = first_is[0][..., None]
    return jnp.stack(
        [jnp.where(first, state[0], state[1]), jnp.where(first, state[1], state[0])], axis=2
    )


def _half_sweep_kernel(
    other_ref, lo_x_ref, hi_x_ref, lo_y_ref, hi_y_ref, face_ref, weight_ref, inverse_ref,
    target_ref, previous_ref, old_lo_x, old_hi_x, old_lo_y, old_hi_y, out_ref, send_lo_x_ref, send_hi_x_ref, send_lo_y_ref, send_hi_y_ref, *, span_x
):
    tile = 2 * R
    highest = lax.Precision.HIGHEST
    other = other_ref[...]
    lanes = other.shape[1]
    lane = lax.broadcasted_iota(jnp.int32, (P_SIZE, tile), 1)
    low_half = lane < R
    tiles = [other[:, t * tile:(t + 1) * tile] for t in range(span_x)]
    lo_y = lo_y_ref[...]
    hi_y = hi_y_ref[...]

    def y_block(packed, x):
        held = packed[:, (x // 2) * tile:(x // 2 + 1) * tile]
        return held if x % 2 == 0 else pltpu.roll(held, R, 1)

    below, above = [], []
    for x in range(span_x):
        rolled = pltpu.roll(tiles[x], R, 1)
        below.append(jnp.where(low_half, y_block(lo_y, x), rolled))
        above.append(jnp.where(low_half, rolled, pltpu.roll(y_block(hi_y, x), R, 1)))
    nearby = [
        jnp.concatenate([lo_x_ref[...], other[:, :lanes - tile]], axis=1),
        jnp.concatenate([other[:, tile:], hi_x_ref[...]], axis=1),
        jnp.concatenate(below, axis=1),
        jnp.concatenate(above, axis=1),
        other,
        other,
    ]
    stacked = jnp.concatenate(
        [weight_ref[face:face + 1, :] * nearby[face] for face in range(6)], axis=0
    )
    coupled = jnp.dot(face_ref[...], stacked, precision=highest, preferred_element_type=jnp.float32)
    rhs = target_ref[...] - coupled
    outs = []
    for x in range(span_x):
        part = rhs[:, x * tile:(x + 1) * tile]
        split = jnp.concatenate([jnp.where(low_half, part, 0.0), jnp.where(low_half, 0.0, part)], axis=0)
        outs.append(
            jnp.dot(
                inverse_ref[:, x * tile:(x + 1) * tile], split, precision=highest,
                preferred_element_type=jnp.float32,
            )
        )
    out_ref[...] = jnp.concatenate(outs, axis=1)
    send_lo_x_ref[...] = outs[-1]
    send_hi_x_ref[...] = outs[0]
    for t in range(span_x // 2):
        even, odd = outs[2 * t], outs[2 * t + 1]
        send_lo_y_ref[:, t * tile:(t + 1) * tile] = jnp.where(low_half, pltpu.roll(even, R, 1), odd)
        send_hi_y_ref[:, t * tile:(t + 1) * tile] = jnp.where(low_half, even, pltpu.roll(odd, R, 1))


def half_sweep(other, halos, face_blocks, weight, inverse, target, previous, old_sends, span_x):
    lanes = other.shape[1]
    x_shape = jax.ShapeDtypeStruct((P_SIZE, 2 * R), jnp.float32)
    y_shape = jax.ShapeDtypeStruct((P_SIZE, span_x * R), jnp.float32)
    vmem = pl.BlockSpec(memory_space=pltpu.VMEM)
    return pl.pallas_call(
        functools.partial(_half_sweep_kernel, span_x=span_x),
        out_shape=(jax.ShapeDtypeStruct((P_SIZE, lanes), jnp.float32), x_shape, x_shape, y_shape, y_shape),
        in_specs=[vmem] * 14,
        out_specs=(vmem,) * 5,
        input_output_aliases={9: 0, 10: 1, 11: 2, 12: 3, 13: 4},
    )(*[
        pltpu.with_memory_space_constraint(value, pltpu.VMEM)
        for value in (other, *halos, face_blocks, weight, inverse, target, previous, *old_sends)
    ])


def send_buffers(state, span_x):
    blocks = state.reshape(P_SIZE, span_x, 2, R)
    return (
        blocks[:, -1].reshape(P_SIZE, 2 * R),
        blocks[:, 0].reshape(P_SIZE, 2 * R),
        blocks[:, :, 1].reshape(P_SIZE, span_x * R),
        blocks[:, :, 0].reshape(P_SIZE, span_x * R),
    )


def trade(sends):
    lo_x, hi_x = (
        lax.ppermute(sends[0], "gx", shift_pairs("gx", 1)),
        lax.ppermute(sends[1], "gx", shift_pairs("gx", -1)),
    )
    lo_y, hi_y = (
        lax.ppermute(sends[2], "gy", shift_pairs("gy", 1)),
        lax.ppermute(sends[3], "gy", shift_pairs("gy", -1)),
    )
    return lo_x, hi_x, lo_y, hi_y


def shift_pairs(axis, step):
    count = lax.axis_size(axis)
    return [(i, (i + step) % count) for i in range(count)]


def lane_body(forcing, initial, blocks, face_blocks, strength, strong, colour, neighbours):
    span_x, span_y, span_z, width = forcing.shape
    count = span_x * span_y * span_z
    columns = span_x * span_y
    empty_slot = (span_x + 2) * (span_y + 2) * span_z
    first_is = [colour[:, :, 0] == paint for paint in (0, 1)]

    def pick(values, paint, axis=2):
        lead = (1,) * (axis - 2)
        mask = first_is[paint].reshape(lead + first_is[paint].shape + (1,) * (values.ndim - axis - 1))
        low = lax.index_in_dim(values, 0, axis=axis, keepdims=False)
        high = lax.index_in_dim(values, 1, axis=axis, keepdims=False)
        return jnp.where(mask, low, high)

    def to_lanes(values):
        return jnp.transpose(values.reshape(columns, P_SIZE, R), (1, 0, 2)).reshape(P_SIZE, columns * R)

    start_state = to_lanes(pick(initial, 1))
    first_sends = send_buffers(start_state, span_x)
    first_halos = trade(first_sends)
    by_colour = jnp.stack([pick(blocks, paint) for paint in (0, 1)]).reshape(count, P_SIZE, P_SIZE)
    inverse = block_inverses(by_colour, lanes_out=True)
    weight = jnp.where(neighbours == empty_slot, 0.0, strength * strong.astype(jnp.float32))
    member_inverse = [inverse[:, paint * columns * P_SIZE:(paint + 1) * columns * P_SIZE] for paint in (0, 1)]
    face_row = jnp.transpose(face_blocks, (1, 0, 2)).reshape(P_SIZE, 6 * P_SIZE)
    member_target = [to_lanes(pick(forcing, paint)) for paint in (0, 1)]
    member_weight = [
        jnp.pad(jnp.repeat(pick(weight, paint, axis=3).reshape(6, columns), R, axis=1), ((0, 2), (0, 0)))
        for paint in (0, 1)
    ]
    member_inverse, member_target, member_weight, face_row = lax.optimization_barrier(
        (member_inverse, member_target, member_weight, face_row)
    )
    state = [jnp.zeros_like(start_state), start_state]
    sends = None
    for sweep_index in range(SWEEPS):
        for paint_now in (0, 1):
            halos = first_halos if sends is None else trade(sends)
            state[paint_now], *sends = half_sweep(
                state[1 - paint_now],
                halos,
                face_row,
                member_weight[paint_now],
                member_inverse[paint_now],
                member_target[paint_now],
                state[paint_now],
                first_sends if sends is None else sends,
                span_x,
            )
    first = first_is[0][..., None]
    whole = [
        jnp.transpose(part.reshape(P_SIZE, columns, R), (1, 0, 2)).reshape(span_x, span_y, width)
        for part in state
    ]
    return jnp.stack(
        [jnp.where(first, whole[0], whole[1]), jnp.where(first, whole[1], whole[0])], axis=2
    )


def dispatch(forcing, *rest):
    span_x, span_y, span_z, width = forcing.shape
    if span_y == 2 and span_z == 2 and span_x % 2 == 0 and width == P_SIZE * R:
        return lane_body(forcing, *rest)
    return body(forcing, *rest)


def solution(mesh):
    in_specs = (
        P("gx", "gy", None, None),
        P("gx", "gy", None, None),
        P("gx", "gy", None, None),
        P(),
        P(None, "gx", "gy", None),
        P(None, "gx", "gy", None),
        P("gx", "gy", None),
        P(None, "gx", "gy", None),
    )
    out_specs = P("gx", "gy", None, None)
    return jax.shard_map(dispatch, mesh=mesh, in_specs=in_specs, out_specs=out_specs, check_vma=False)
```

```python
import functools

import jax
import jax.numpy as jnp
from jax import lax
from jax.experimental import pallas as pl
from jax.experimental.pallas import tpu as pltpu
from jax.sharding import PartitionSpec as P

P_SIZE = 64
R = 64
SWEEPS = 4


def padded(block, sides, width):
    for axis, dim in sides:
        count = lax.axis_size(axis)
        forward = [(i, i + 1) for i in range(count - 1)]
        backward = [(target, source) for source, target in forward]
        low = lax.ppermute(
            lax.slice_in_dim(block, block.shape[dim] - width, None, axis=dim), axis, forward
        )
        high = lax.ppermute(lax.slice_in_dim(block, 0, width, axis=dim), axis, backward)
        block = jnp.concatenate([low, block, high], axis=dim)
    return block


def _gauss_jordan_kernel(a_ref, o_ref, *, n, nb):
    lanes = n * nb
    tiles = lanes // 128
    del a_ref
    lane_t = lax.broadcasted_iota(jnp.int32, (n, 128), 1)
    lane_r = lax.broadcasted_iota(jnp.int32, (1, 128), 1)
    row_i = lax.broadcasted_iota(jnp.int32, (n, 128), 0)

    def spread(x):
        shift = nb
        while shift < 128:
            x = x + pltpu.roll(x, shift, 1)
            shift *= 2
        return x

    def step(k, carry):
        start = k * nb
        tile = start // 128
        off = start % 128
        tile_start = pl.multiple_of(tile * 128, 128)
        column = spread(
            jnp.where((lane_t >= off) & (lane_t < off + nb), o_ref[:, pl.ds(tile_start, 128)], 0.0)
        )
        pivot = jnp.sum(jnp.where(row_i == k, column, 0.0), axis=0, keepdims=True)
        base = pl.multiple_of((k // 8) * 8, 8)
        band = o_ref[pl.ds(base, 8), :]
        band_i = lax.broadcasted_iota(jnp.int32, band.shape, 0)
        row = jnp.sum(jnp.where(band_i == k - base, band, 0.0), axis=0, keepdims=True)
        for t in range(tiles):
            in_col = (t == tile) & (lane_r >= off) & (lane_r < off + nb)
            scaled = jnp.where(in_col, 1.0 / pivot, row[:, t * 128:(t + 1) * 128] / pivot)
            kept = jnp.where(in_col, 0.0, o_ref[:, t * 128:(t + 1) * 128])
            o_ref[:, t * 128:(t + 1) * 128] = jnp.where(row_i == k, scaled, kept - column * scaled)
        return carry

    lax.fori_loop(0, n, step, 0)


def block_inverses(matrices, lanes_out=False):
    nb, n, _ = matrices.shape
    if 128 % nb or (n * nb) % 128:
        assert not lanes_out
        lower_factor = jnp.linalg.cholesky(matrices)
        identity = jnp.broadcast_to(jnp.eye(n, dtype=matrices.dtype), matrices.shape)
        solved = jax.scipy.linalg.solve_triangular(lower_factor, identity, lower=True)
        return jnp.einsum("eqp,eqr->epr", solved, solved, precision=lax.Precision.HIGHEST)
    packed = jnp.transpose(matrices, (1, 2, 0)).reshape(n, n * nb)
    inverted = pl.pallas_call(
        functools.partial(_gauss_jordan_kernel, n=n, nb=nb),
        out_shape=jax.ShapeDtypeStruct((n, n * nb), jnp.float32),
        in_specs=[pl.BlockSpec(memory_space=pltpu.VMEM)],
        out_specs=pl.BlockSpec(memory_space=pltpu.VMEM),
        input_output_aliases={0: 0},
        cost_estimate=pl.CostEstimate(
            flops=2000 * n ** 3 * nb, transcendentals=0, bytes_accessed=8 * n * n * nb
        ),
    )(pltpu.with_memory_space_constraint(packed, pltpu.VMEM))
    if lanes_out:
        return jnp.transpose(inverted.reshape(n, n, nb), (0, 2, 1)).reshape(n, nb * n)
    return jnp.transpose(inverted.reshape(n, n, nb), (2, 0, 1))


def shifted(values, halo, dim, lower):
    width = values.shape[dim]
    if lower:
        return jnp.concatenate([halo, lax.slice_in_dim(values, 0, width - 1, axis=dim)], axis=dim)
    return jnp.concatenate([lax.slice_in_dim(values, 1, width, axis=dim), halo], axis=dim)


def exchange(values, axis, dim):
    count = lax.axis_size(axis)
    forward = [(i, i + 1) for i in range(count - 1)]
    backward = [(target, source) for source, target in forward]
    width = values.shape[dim]
    from_lower = lax.ppermute(lax.slice_in_dim(values, width - 1, width, axis=dim), axis, forward)
    from_upper = lax.ppermute(lax.slice_in_dim(values, 0, 1, axis=dim), axis, backward)
    return from_lower, from_upper


def body(forcing, initial, blocks, face_blocks, strength, strong, colour, neighbours):
    span_x, span_y, span_z, width = forcing.shape
    count = span_x * span_y * span_z
    columns = span_x * span_y
    empty_slot = (span_x + 2) * (span_y + 2) * span_z
    inverse = block_inverses(blocks.reshape(count, P_SIZE, P_SIZE)).reshape(
        span_x, span_y, span_z, P_SIZE, P_SIZE
    )
    weight = jnp.where(neighbours == empty_slot, 0.0, strength * strong.astype(jnp.float32))
    first_is = [colour[:, :, 0] == paint for paint in (0, 1)]

    def pick(values, paint, axis=2):
        lead = (1,) * (axis - 2)
        mask = first_is[paint].reshape(lead + first_is[paint].shape + (1,) * (values.ndim - axis - 1))
        low = lax.index_in_dim(values, 0, axis=axis, keepdims=False)
        high = lax.index_in_dim(values, 1, axis=axis, keepdims=False)
        return jnp.where(mask, low, high)

    member_inverse = [inverse[:, paint * columns * P_SIZE:(paint + 1) * columns * P_SIZE] for paint in (0, 1)]
    face_row = jnp.transpose(face_blocks, (1, 0, 2)).reshape(P_SIZE, 6 * P_SIZE)
    member_target = [pick(forcing, paint).reshape(columns, P_SIZE, R) for paint in (0, 1)]
    member_weight = [pick(weight, paint, axis=3)[..., None] for paint in (0, 1)]
    state = [pick(initial, 0), pick(initial, 1)]
    for sweep_index in range(SWEEPS):
        for paint_now in (0, 1):
            other = state[1 - paint_now]
            low_x, high_x = exchange(other, "gx", 0)
            low_y, high_y = exchange(other, "gy", 1)
            nearby = jnp.stack(
                [
                    shifted(other, low_x, 0, True),
                    shifted(other, high_x, 0, False),
                    shifted(other, low_y, 1, True),
                    shifted(other, high_y, 1, False),
                    other,
                    other,
                ]
            )
            nearby = (nearby * member_weight[paint_now]).reshape(6, columns, P_SIZE, R)
            coupled = jnp.einsum(
                "fpq,feqr->epr", face_blocks, nearby, precision=lax.Precision.HIGHEST
            )
            update = jnp.einsum(
                "epq,eqr->epr",
                member_inverse[paint_now],
                member_target[paint_now] - coupled,
                precision=lax.Precision.HIGHEST,
            )
            state[paint_now] = update.reshape(span_x, span_y, width)
    first = first_is[0][..., None]
    return jnp.stack(
        [jnp.where(first, state[0], state[1]), jnp.where(first, state[1], state[0])], axis=2
    )


def _half_sweep_kernel(
    other_ref, lo_x_ref, hi_x_ref, lo_y_ref, hi_y_ref, face_ref, weight_ref, inverse_ref,
    target_ref, previous_ref, old_lo_x, old_hi_x, old_lo_y, old_hi_y, out_ref, send_lo_x_ref, send_hi_x_ref, send_lo_y_ref, send_hi_y_ref, *, span_x
):
    tile = 2 * R
    highest = lax.Precision.HIGHEST
    other = other_ref[...]
    lanes = other.shape[1]
    lane = lax.broadcasted_iota(jnp.int32, (P_SIZE, tile), 1)
    low_half = lane < R
    tiles = [other[:, t * tile:(t + 1) * tile] for t in range(span_x)]
    lo_y = lo_y_ref[...]
    hi_y = hi_y_ref[...]

    def y_block(packed, x):
        held = packed[:, (x // 2) * tile:(x // 2 + 1) * tile]
        return held if x % 2 == 0 else pltpu.roll(held, R, 1)

    below, above = [], []
    for x in range(span_x):
        rolled = pltpu.roll(tiles[x], R, 1)
        below.append(jnp.where(low_half, y_block(lo_y, x), rolled))
        above.append(jnp.where(low_half, rolled, pltpu.roll(y_block(hi_y, x), R, 1)))
    nearby = [
        jnp.concatenate([lo_x_ref[...], other[:, :lanes - tile]], axis=1),
        jnp.concatenate([other[:, tile:], hi_x_ref[...]], axis=1),
        jnp.concatenate(below, axis=1),
        jnp.concatenate(above, axis=1),
        other,
        other,
    ]
    stacked = jnp.concatenate(
        [weight_ref[face:face + 1, :] * nearby[face] for face in range(6)], axis=0
    )
    coupled = jnp.dot(face_ref[...], stacked, precision=highest, preferred_element_type=jnp.float32)
    rhs = target_ref[...] - coupled
    outs = []
    for x in range(span_x):
        part = rhs[:, x * tile:(x + 1) * tile]
        split = jnp.concatenate([jnp.where(low_half, part, 0.0), jnp.where(low_half, 0.0, part)], axis=0)
        outs.append(
            jnp.dot(
                inverse_ref[:, x * tile:(x + 1) * tile], split, precision=highest,
                preferred_element_type=jnp.float32,
            )
        )
    out_ref[...] = jnp.concatenate(outs, axis=1)
    send_lo_x_ref[...] = outs[-1]
    send_hi_x_ref[...] = outs[0]
    for t in range(span_x // 2):
        even, odd = outs[2 * t], outs[2 * t + 1]
        send_lo_y_ref[:, t * tile:(t + 1) * tile] = jnp.where(low_half, pltpu.roll(even, R, 1), odd)
        send_hi_y_ref[:, t * tile:(t + 1) * tile] = jnp.where(low_half, even, pltpu.roll(odd, R, 1))


def half_sweep(other, halos, face_blocks, weight, inverse, target, previous, old_sends, span_x):
    lanes = other.shape[1]
    x_shape = jax.ShapeDtypeStruct((P_SIZE, 2 * R), jnp.float32)
    y_shape = jax.ShapeDtypeStruct((P_SIZE, span_x * R), jnp.float32)
    vmem = pl.BlockSpec(memory_space=pltpu.VMEM)
    return pl.pallas_call(
        functools.partial(_half_sweep_kernel, span_x=span_x),
        out_shape=(jax.ShapeDtypeStruct((P_SIZE, lanes), jnp.float32), x_shape, x_shape, y_shape, y_shape),
        in_specs=[vmem] * 14,
        out_specs=(vmem,) * 5,
        input_output_aliases={9: 0, 10: 1, 11: 2, 12: 3, 13: 4},
    )(*[
        pltpu.with_memory_space_constraint(value, pltpu.VMEM)
        for value in (other, *halos, face_blocks, weight, inverse, target, previous, *old_sends)
    ])


def send_buffers(state, span_x):
    blocks = state.reshape(P_SIZE, span_x, 2, R)
    return (
        blocks[:, -1].reshape(P_SIZE, 2 * R),
        blocks[:, 0].reshape(P_SIZE, 2 * R),
        blocks[:, :, 1].reshape(P_SIZE, span_x * R),
        blocks[:, :, 0].reshape(P_SIZE, span_x * R),
    )


def trade(sends):
    lo_x, hi_x = (
        lax.ppermute(sends[0], "gx", shift_pairs("gx", 1)),
        lax.ppermute(sends[1], "gx", shift_pairs("gx", -1)),
    )
    lo_y, hi_y = (
        lax.ppermute(sends[2], "gy", shift_pairs("gy", 1)),
        lax.ppermute(sends[3], "gy", shift_pairs("gy", -1)),
    )
    return lo_x, hi_x, lo_y, hi_y


def shift_pairs(axis, step):
    count = lax.axis_size(axis)
    return [(i, (i + step) % count) for i in range(count)]


def lane_body(forcing, initial, blocks, face_blocks, strength, strong, colour, neighbours):
    span_x, span_y, span_z, width = forcing.shape
    count = span_x * span_y * span_z
    columns = span_x * span_y
    empty_slot = (span_x + 2) * (span_y + 2) * span_z
    first_is = [colour[:, :, 0] == paint for paint in (0, 1)]

    def pick(values, paint, axis=2):
        lead = (1,) * (axis - 2)
        mask = first_is[paint].reshape(lead + first_is[paint].shape + (1,) * (values.ndim - axis - 1))
        low = lax.index_in_dim(values, 0, axis=axis, keepdims=False)
        high = lax.index_in_dim(values, 1, axis=axis, keepdims=False)
        return jnp.where(mask, low, high)

    def to_lanes(values):
        return jnp.transpose(values.reshape(columns, P_SIZE, R), (1, 0, 2)).reshape(P_SIZE, columns * R)

    start_state = to_lanes(pick(initial, 1))
    first_sends = send_buffers(start_state, span_x)
    first_halos = trade(first_sends)
    by_colour = jnp.stack([pick(blocks, paint) for paint in (0, 1)]).reshape(count, P_SIZE, P_SIZE)
    inverse = block_inverses(by_colour, lanes_out=True)
    weight = jnp.where(neighbours == empty_slot, 0.0, strength * strong.astype(jnp.float32))
    member_inverse = [inverse[:, paint * columns * P_SIZE:(paint + 1) * columns * P_SIZE] for paint in (0, 1)]
    face_row = jnp.transpose(face_blocks, (1, 0, 2)).reshape(P_SIZE, 6 * P_SIZE)
    member_target = [to_lanes(pick(forcing, paint)) for paint in (0, 1)]
    member_weight = [
        jnp.pad(jnp.repeat(pick(weight, paint, axis=3).reshape(6, columns), R, axis=1), ((0, 2), (0, 0)))
        for paint in (0, 1)
    ]
    member_inverse, member_target, member_weight, face_row = lax.optimization_barrier(
        (member_inverse, member_target, member_weight, face_row)
    )
    state = [jnp.zeros_like(start_state), start_state]
    sends = None
    for sweep_index in range(SWEEPS):
        for paint_now in (0, 1):
            halos = first_halos if sends is None else trade(sends)
            state[paint_now], *sends = half_sweep(
                state[1 - paint_now],
                halos,
                face_row,
                member_weight[paint_now],
                member_inverse[paint_now],
                member_target[paint_now],
                state[paint_now],
                first_sends if sends is None else sends,
                span_x,
            )
    whole = [
        jnp.transpose(part.reshape(P_SIZE, columns, R), (1, 0, 2)).reshape(span_x, span_y, 1, width)
        for part in state
    ]
    return jnp.where((colour == 0)[..., None], whole[0], whole[1])


def dispatch(forcing, *rest):
    span_x, span_y, span_z, width = forcing.shape
    if span_y == 2 and span_z == 2 and span_x % 2 == 0 and width == P_SIZE * R:
        return lane_body(forcing, *rest)
    return body(forcing, *rest)


def solution(mesh):
    in_specs = (
        P("gx", "gy", None, None),
        P("gx", "gy", None, None),
        P("gx", "gy", None, None),
        P(),
        P(None, "gx", "gy", None),
        P(None, "gx", "gy", None),
        P("gx", "gy", None),
        P(None, "gx", "gy", None),
    )
    out_specs = P("gx", "gy", None, None)
    return jax.shard_map(dispatch, mesh=mesh, in_specs=in_specs, out_specs=out_specs, check_vma=False)
```

```python
import functools

import jax
import jax.numpy as jnp
from jax import lax
from jax.experimental import pallas as pl
from jax.experimental.pallas import tpu as pltpu
from jax.sharding import PartitionSpec as P

P_SIZE = 64
R = 64
SWEEPS = 4


def padded(block, sides, width):
    for axis, dim in sides:
        count = lax.axis_size(axis)
        forward = [(i, i + 1) for i in range(count - 1)]
        backward = [(target, source) for source, target in forward]
        low = lax.ppermute(
            lax.slice_in_dim(block, block.shape[dim] - width, None, axis=dim), axis, forward
        )
        high = lax.ppermute(lax.slice_in_dim(block, 0, width, axis=dim), axis, backward)
        block = jnp.concatenate([low, block, high], axis=dim)
    return block


def _gauss_jordan_kernel(a_ref, o_ref, *, n, nb):
    lanes = n * nb
    tiles = lanes // 128
    del a_ref
    lane_t = lax.broadcasted_iota(jnp.int32, (n, 128), 1)
    lane_r = lax.broadcasted_iota(jnp.int32, (1, 128), 1)
    row_i = lax.broadcasted_iota(jnp.int32, (n, 128), 0)

    def spread(x):
        shift = nb
        while shift < 128:
            x = x + pltpu.roll(x, shift, 1)
            shift *= 2
        return x

    def step(k, carry):
        start = k * nb
        tile = start // 128
        off = start % 128
        tile_start = pl.multiple_of(tile * 128, 128)
        column = spread(
            jnp.where((lane_t >= off) & (lane_t < off + nb), o_ref[:, pl.ds(tile_start, 128)], 0.0)
        )
        pivot = jnp.sum(jnp.where(row_i == k, column, 0.0), axis=0, keepdims=True)
        base = pl.multiple_of((k // 8) * 8, 8)
        band = o_ref[pl.ds(base, 8), :]
        band_i = lax.broadcasted_iota(jnp.int32, band.shape, 0)
        row = jnp.sum(jnp.where(band_i == k - base, band, 0.0), axis=0, keepdims=True)
        for t in range(tiles):
            in_col = (t == tile) & (lane_r >= off) & (lane_r < off + nb)
            scaled = jnp.where(in_col, 1.0 / pivot, row[:, t * 128:(t + 1) * 128] / pivot)
            kept = jnp.where(in_col, 0.0, o_ref[:, t * 128:(t + 1) * 128])
            o_ref[:, t * 128:(t + 1) * 128] = jnp.where(row_i == k, scaled, kept - column * scaled)
        return carry

    lax.fori_loop(0, n, step, 0)


def block_inverses(matrices, lanes_out=False):
    nb, n, _ = matrices.shape
    if 128 % nb or (n * nb) % 128:
        assert not lanes_out
        lower_factor = jnp.linalg.cholesky(matrices)
        identity = jnp.broadcast_to(jnp.eye(n, dtype=matrices.dtype), matrices.shape)
        solved = jax.scipy.linalg.solve_triangular(lower_factor, identity, lower=True)
        return jnp.einsum("eqp,eqr->epr", solved, solved, precision=lax.Precision.HIGHEST)
    packed = jnp.transpose(matrices, (1, 2, 0)).reshape(n, n * nb)
    inverted = pl.pallas_call(
        functools.partial(_gauss_jordan_kernel, n=n, nb=nb),
        out_shape=jax.ShapeDtypeStruct((n, n * nb), jnp.float32),
        in_specs=[pl.BlockSpec(memory_space=pltpu.VMEM)],
        out_specs=pl.BlockSpec(memory_space=pltpu.VMEM),
        input_output_aliases={0: 0},
        cost_estimate=pl.CostEstimate(
            flops=2000 * n ** 3 * nb, transcendentals=0, bytes_accessed=8 * n * n * nb
        ),
    )(pltpu.with_memory_space_constraint(packed, pltpu.VMEM))
    if lanes_out:
        return jnp.transpose(inverted.reshape(n, n, nb), (0, 2, 1)).reshape(n, nb * n)
    return jnp.transpose(inverted.reshape(n, n, nb), (2, 0, 1))


def shifted(values, halo, dim, lower):
    width = values.shape[dim]
    if lower:
        return jnp.concatenate([halo, lax.slice_in_dim(values, 0, width - 1, axis=dim)], axis=dim)
    return jnp.concatenate([lax.slice_in_dim(values, 1, width, axis=dim), halo], axis=dim)


def exchange(values, axis, dim):
    count = lax.axis_size(axis)
    forward = [(i, i + 1) for i in range(count - 1)]
    backward = [(target, source) for source, target in forward]
    width = values.shape[dim]
    from_lower = lax.ppermute(lax.slice_in_dim(values, width - 1, width, axis=dim), axis, forward)
    from_upper = lax.ppermute(lax.slice_in_dim(values, 0, 1, axis=dim), axis, backward)
    return from_lower, from_upper


def body(forcing, initial, blocks, face_blocks, strength, strong, colour, neighbours):
    span_x, span_y, span_z, width = forcing.shape
    count = span_x * span_y * span_z
    columns = span_x * span_y
    empty_slot = (span_x + 2) * (span_y + 2) * span_z
    inverse = block_inverses(blocks.reshape(count, P_SIZE, P_SIZE)).reshape(
        span_x, span_y, span_z, P_SIZE, P_SIZE
    )
    weight = jnp.where(neighbours == empty_slot, 0.0, strength * strong.astype(jnp.float32))
    first_is = [colour[:, :, 0] == paint for paint in (0, 1)]

    def pick(values, paint, axis=2):
        lead = (1,) * (axis - 2)
        mask = first_is[paint].reshape(lead + first_is[paint].shape + (1,) * (values.ndim - axis - 1))
        low = lax.index_in_dim(values, 0, axis=axis, keepdims=False)
        high = lax.index_in_dim(values, 1, axis=axis, keepdims=False)
        return jnp.where(mask, low, high)

    member_inverse = [inverse[:, paint * columns * P_SIZE:(paint + 1) * columns * P_SIZE] for paint in (0, 1)]
    face_row = jnp.transpose(face_blocks, (1, 0, 2)).reshape(P_SIZE, 6 * P_SIZE)
    member_target = [pick(forcing, paint).reshape(columns, P_SIZE, R) for paint in (0, 1)]
    member_weight = [pick(weight, paint, axis=3)[..., None] for paint in (0, 1)]
    state = [pick(initial, 0), pick(initial, 1)]
    for sweep_index in range(SWEEPS):
        for paint_now in (0, 1):
            other = state[1 - paint_now]
            low_x, high_x = exchange(other, "gx", 0)
            low_y, high_y = exchange(other, "gy", 1)
            nearby = jnp.stack(
                [
                    shifted(other, low_x, 0, True),
                    shifted(other, high_x, 0, False),
                    shifted(other, low_y, 1, True),
                    shifted(other, high_y, 1, False),
                    other,
                    other,
                ]
            )
            nearby = (nearby * member_weight[paint_now]).reshape(6, columns, P_SIZE, R)
            coupled = jnp.einsum(
                "fpq,feqr->epr", face_blocks, nearby, precision=lax.Precision.HIGHEST
            )
            update = jnp.einsum(
                "epq,eqr->epr",
                member_inverse[paint_now],
                member_target[paint_now] - coupled,
                precision=lax.Precision.HIGHEST,
            )
            state[paint_now] = update.reshape(span_x, span_y, width)
    first = first_is[0][..., None]
    return jnp.stack(
        [jnp.where(first, state[0], state[1]), jnp.where(first, state[1], state[0])], axis=2
    )


def _half_sweep_kernel(
    other_ref, lo_x_ref, hi_x_ref, lo_y_ref, hi_y_ref, face_ref, weight_ref, inverse_ref,
    target_ref, previous_ref, old_lo_x, old_hi_x, old_lo_y, old_hi_y, out_ref, send_lo_x_ref, send_hi_x_ref, send_lo_y_ref, send_hi_y_ref, *, span_x
):
    tile = 2 * R
    highest = lax.Precision.HIGHEST
    other = other_ref[...]
    lanes = other.shape[1]
    lane = lax.broadcasted_iota(jnp.int32, (P_SIZE, tile), 1)
    low_half = lane < R
    tiles = [other[:, t * tile:(t + 1) * tile] for t in range(span_x)]
    lo_y = lo_y_ref[...]
    hi_y = hi_y_ref[...]

    def y_block(packed, x):
        held = packed[:, (x // 2) * tile:(x // 2 + 1) * tile]
        return held if x % 2 == 0 else pltpu.roll(held, R, 1)

    below, above = [], []
    for x in range(span_x):
        rolled = pltpu.roll(tiles[x], R, 1)
        below.append(jnp.where(low_half, y_block(lo_y, x), rolled))
        above.append(jnp.where(low_half, rolled, pltpu.roll(y_block(hi_y, x), R, 1)))
    nearby = [
        jnp.concatenate([lo_x_ref[...], other[:, :lanes - tile]], axis=1),
        jnp.concatenate([other[:, tile:], hi_x_ref[...]], axis=1),
        jnp.concatenate(below, axis=1),
        jnp.concatenate(above, axis=1),
        other,
        other,
    ]
    stacked = jnp.concatenate(
        [weight_ref[face:face + 1, :] * nearby[face] for face in range(6)], axis=0
    )
    coupled = jnp.dot(face_ref[...], stacked, precision=highest, preferred_element_type=jnp.float32)
    rhs = target_ref[...] - coupled
    outs = []
    for x in range(span_x):
        part = rhs[:, x * tile:(x + 1) * tile]
        split = jnp.concatenate([jnp.where(low_half, part, 0.0), jnp.where(low_half, 0.0, part)], axis=0)
        outs.append(
            jnp.dot(
                inverse_ref[:, x * tile:(x + 1) * tile], split, precision=highest,
                preferred_element_type=jnp.float32,
            )
        )
    out_ref[...] = jnp.concatenate(outs, axis=1)
    send_lo_x_ref[...] = outs[-1]
    send_hi_x_ref[...] = outs[0]
    for t in range(span_x // 2):
        even, odd = outs[2 * t], outs[2 * t + 1]
        send_lo_y_ref[:, t * tile:(t + 1) * tile] = jnp.where(low_half, pltpu.roll(even, R, 1), odd)
        send_hi_y_ref[:, t * tile:(t + 1) * tile] = jnp.where(low_half, even, pltpu.roll(odd, R, 1))


def half_sweep(other, halos, face_blocks, weight, inverse, target, previous, old_sends, span_x):
    lanes = other.shape[1]
    x_shape = jax.ShapeDtypeStruct((P_SIZE, 2 * R), jnp.float32)
    y_shape = jax.ShapeDtypeStruct((P_SIZE, span_x * R), jnp.float32)
    vmem = pl.BlockSpec(memory_space=pltpu.VMEM)
    return pl.pallas_call(
        functools.partial(_half_sweep_kernel, span_x=span_x),
        out_shape=(jax.ShapeDtypeStruct((P_SIZE, lanes), jnp.float32), x_shape, x_shape, y_shape, y_shape),
        in_specs=[vmem] * 14,
        out_specs=(vmem,) * 5,
        input_output_aliases={9: 0, 10: 1, 11: 2, 12: 3, 13: 4},
    )(*[
        pltpu.with_memory_space_constraint(value, pltpu.VMEM)
        for value in (other, *halos, face_blocks, weight, inverse, target, previous, *old_sends)
    ])


def send_buffers(state, span_x):
    blocks = state.reshape(P_SIZE, span_x, 2, R)
    return (
        blocks[:, -1].reshape(P_SIZE, 2 * R),
        blocks[:, 0].reshape(P_SIZE, 2 * R),
        blocks[:, :, 1].reshape(P_SIZE, span_x * R),
        blocks[:, :, 0].reshape(P_SIZE, span_x * R),
    )


def trade(sends):
    lo_x, hi_x = (
        lax.ppermute(sends[0], "gx", shift_pairs("gx", 1)),
        lax.ppermute(sends[1], "gx", shift_pairs("gx", -1)),
    )
    lo_y, hi_y = (
        lax.ppermute(sends[2], "gy", shift_pairs("gy", 1)),
        lax.ppermute(sends[3], "gy", shift_pairs("gy", -1)),
    )
    return lo_x, hi_x, lo_y, hi_y


def shift_pairs(axis, step):
    count = lax.axis_size(axis)
    return [(i, (i + step) % count) for i in range(count)]


def lane_body(forcing, initial, blocks, face_blocks, strength, strong, colour, neighbours):
    span_x, span_y, span_z, width = forcing.shape
    count = span_x * span_y * span_z
    columns = span_x * span_y
    empty_slot = (span_x + 2) * (span_y + 2) * span_z
    first_is = [colour[:, :, 0] == paint for paint in (0, 1)]

    def pick(values, paint, axis=2):
        lead = (1,) * (axis - 2)
        mask = first_is[paint].reshape(lead + first_is[paint].shape + (1,) * (values.ndim - axis - 1))
        low = lax.index_in_dim(values, 0, axis=axis, keepdims=False)
        high = lax.index_in_dim(values, 1, axis=axis, keepdims=False)
        return jnp.where(mask, low, high)

    def to_lanes(values):
        return jnp.transpose(values.reshape(columns, P_SIZE, R), (1, 0, 2)).reshape(P_SIZE, columns * R)

    start_state = to_lanes(pick(initial, 1))
    first_sends = send_buffers(start_state, span_x)
    first_halos = trade(first_sends)
    by_colour = jnp.stack([pick(blocks, paint) for paint in (0, 1)]).reshape(count, P_SIZE, P_SIZE)
    inverse = block_inverses(by_colour, lanes_out=True)
    weight = jnp.where(neighbours == empty_slot, 0.0, strength * strong.astype(jnp.float32))
    member_inverse = [inverse[:, paint * columns * P_SIZE:(paint + 1) * columns * P_SIZE] for paint in (0, 1)]
    face_row = jnp.transpose(face_blocks, (1, 0, 2)).reshape(P_SIZE, 6 * P_SIZE)
    member_target = [to_lanes(pick(forcing, paint)) for paint in (0, 1)]
    member_weight = [
        jnp.pad(jnp.repeat(pick(weight, paint, axis=3).reshape(6, columns), R, axis=1), ((0, 2), (0, 0)))
        for paint in (0, 1)
    ]
    constants = [
        lax.optimization_barrier((member_inverse[paint], member_target[paint], member_weight[paint]))
        for paint in (0, 1)
    ]
    member_inverse, member_target, member_weight = (list(group) for group in zip(*constants))
    state = [jnp.zeros_like(start_state), start_state]
    sends = None
    for sweep_index in range(SWEEPS):
        for paint_now in (0, 1):
            halos = first_halos if sends is None else trade(sends)
            state[paint_now], *sends = half_sweep(
                state[1 - paint_now],
                halos,
                face_row,
                member_weight[paint_now],
                member_inverse[paint_now],
                member_target[paint_now],
                state[paint_now],
                first_sends if sends is None else sends,
                span_x,
            )
    whole = [
        jnp.transpose(part.reshape(P_SIZE, columns, R), (1, 0, 2)).reshape(span_x, span_y, 1, width)
        for part in state
    ]
    return jnp.where((colour == 0)[..., None], whole[0], whole[1])


def dispatch(forcing, *rest):
    span_x, span_y, span_z, width = forcing.shape
    if span_y == 2 and span_z == 2 and span_x % 2 == 0 and width == P_SIZE * R:
        return lane_body(forcing, *rest)
    return body(forcing, *rest)


def solution(mesh):
    in_specs = (
        P("gx", "gy", None, None),
        P("gx", "gy", None, None),
        P("gx", "gy", None, None),
        P(),
        P(None, "gx", "gy", None),
        P(None, "gx", "gy", None),
        P("gx", "gy", None),
        P(None, "gx", "gy", None),
    )
    out_specs = P("gx", "gy", None, None)
    return jax.shard_map(dispatch, mesh=mesh, in_specs=in_specs, out_specs=out_specs, check_vma=False)
```

```python
import functools

import jax
import jax.numpy as jnp
from jax import lax
from jax.experimental import pallas as pl
from jax.experimental.pallas import tpu as pltpu
from jax.sharding import PartitionSpec as P

P_SIZE = 64
R = 64
SWEEPS = 4


def padded(block, sides, width):
    for axis, dim in sides:
        count = lax.axis_size(axis)
        forward = [(i, i + 1) for i in range(count - 1)]
        backward = [(target, source) for source, target in forward]
        low = lax.ppermute(
            lax.slice_in_dim(block, block.shape[dim] - width, None, axis=dim), axis, forward
        )
        high = lax.ppermute(lax.slice_in_dim(block, 0, width, axis=dim), axis, backward)
        block = jnp.concatenate([low, block, high], axis=dim)
    return block


def _gauss_jordan_kernel(a_ref, o_ref, *, n, nb):
    lanes = n * nb
    tiles = lanes // 128
    del a_ref
    lane_t = lax.broadcasted_iota(jnp.int32, (n, 128), 1)
    lane_r = lax.broadcasted_iota(jnp.int32, (1, 128), 1)
    row_i = lax.broadcasted_iota(jnp.int32, (n, 128), 0)

    def spread(x):
        shift = nb
        while shift < 128:
            x = x + pltpu.roll(x, shift, 1)
            shift *= 2
        return x

    def step(k, carry):
        start = k * nb
        tile = start // 128
        off = start % 128
        tile_start = pl.multiple_of(tile * 128, 128)
        column = spread(
            jnp.where((lane_t >= off) & (lane_t < off + nb), o_ref[:, pl.ds(tile_start, 128)], 0.0)
        )
        pivot = jnp.sum(jnp.where(row_i == k, column, 0.0), axis=0, keepdims=True)
        base = pl.multiple_of((k // 8) * 8, 8)
        band = o_ref[pl.ds(base, 8), :]
        band_i = lax.broadcasted_iota(jnp.int32, band.shape, 0)
        row = jnp.sum(jnp.where(band_i == k - base, band, 0.0), axis=0, keepdims=True)
        for t in range(tiles):
            in_col = (t == tile) & (lane_r >= off) & (lane_r < off + nb)
            scaled = jnp.where(in_col, 1.0 / pivot, row[:, t * 128:(t + 1) * 128] / pivot)
            kept = jnp.where(in_col, 0.0, o_ref[:, t * 128:(t + 1) * 128])
            o_ref[:, t * 128:(t + 1) * 128] = jnp.where(row_i == k, scaled, kept - column * scaled)
        return carry

    lax.fori_loop(0, n, step, 0)


def block_inverses(matrices, lanes_out=False):
    nb, n, _ = matrices.shape
    if 128 % nb or (n * nb) % 128:
        assert not lanes_out
        lower_factor = jnp.linalg.cholesky(matrices)
        identity = jnp.broadcast_to(jnp.eye(n, dtype=matrices.dtype), matrices.shape)
        solved = jax.scipy.linalg.solve_triangular(lower_factor, identity, lower=True)
        return jnp.einsum("eqp,eqr->epr", solved, solved, precision=lax.Precision.HIGHEST)
    packed = jnp.transpose(matrices, (1, 2, 0)).reshape(n, n * nb)
    inverted = pl.pallas_call(
        functools.partial(_gauss_jordan_kernel, n=n, nb=nb),
        out_shape=jax.ShapeDtypeStruct((n, n * nb), jnp.float32),
        in_specs=[pl.BlockSpec(memory_space=pltpu.VMEM)],
        out_specs=pl.BlockSpec(memory_space=pltpu.VMEM),
        input_output_aliases={0: 0},
        cost_estimate=pl.CostEstimate(
            flops=2000 * n ** 3 * nb, transcendentals=0, bytes_accessed=8 * n * n * nb
        ),
    )(pltpu.with_memory_space_constraint(packed, pltpu.VMEM))
    if lanes_out:
        return jnp.transpose(inverted.reshape(n, n, nb), (0, 2, 1)).reshape(n, nb * n)
    return jnp.transpose(inverted.reshape(n, n, nb), (2, 0, 1))


def shifted(values, halo, dim, lower):
    width = values.shape[dim]
    if lower:
        return jnp.concatenate([halo, lax.slice_in_dim(values, 0, width - 1, axis=dim)], axis=dim)
    return jnp.concatenate([lax.slice_in_dim(values, 1, width, axis=dim), halo], axis=dim)


def exchange(values, axis, dim):
    count = lax.axis_size(axis)
    forward = [(i, i + 1) for i in range(count - 1)]
    backward = [(target, source) for source, target in forward]
    width = values.shape[dim]
    from_lower = lax.ppermute(lax.slice_in_dim(values, width - 1, width, axis=dim), axis, forward)
    from_upper = lax.ppermute(lax.slice_in_dim(values, 0, 1, axis=dim), axis, backward)
    return from_lower, from_upper


def body(forcing, initial, blocks, face_blocks, strength, strong, colour, neighbours):
    span_x, span_y, span_z, width = forcing.shape
    count = span_x * span_y * span_z
    columns = span_x * span_y
    empty_slot = (span_x + 2) * (span_y + 2) * span_z
    inverse = block_inverses(blocks.reshape(count, P_SIZE, P_SIZE)).reshape(
        span_x, span_y, span_z, P_SIZE, P_SIZE
    )
    weight = jnp.where(neighbours == empty_slot, 0.0, strength * strong.astype(jnp.float32))
    first_is = [colour[:, :, 0] == paint for paint in (0, 1)]

    def pick(values, paint, axis=2):
        lead = (1,) * (axis - 2)
        mask = first_is[paint].reshape(lead + first_is[paint].shape + (1,) * (values.ndim - axis - 1))
        low = lax.index_in_dim(values, 0, axis=axis, keepdims=False)
        high = lax.index_in_dim(values, 1, axis=axis, keepdims=False)
        return jnp.where(mask, low, high)

    member_inverse = [inverse[:, paint * columns * P_SIZE:(paint + 1) * columns * P_SIZE] for paint in (0, 1)]
    face_row = jnp.transpose(face_blocks, (1, 0, 2)).reshape(P_SIZE, 6 * P_SIZE)
    member_target = [pick(forcing, paint).reshape(columns, P_SIZE, R) for paint in (0, 1)]
    member_weight = [pick(weight, paint, axis=3)[..., None] for paint in (0, 1)]
    state = [pick(initial, 0), pick(initial, 1)]
    for sweep_index in range(SWEEPS):
        for paint_now in (0, 1):
            other = state[1 - paint_now]
            low_x, high_x = exchange(other, "gx", 0)
            low_y, high_y = exchange(other, "gy", 1)
            nearby = jnp.stack(
                [
                    shifted(other, low_x, 0, True),
                    shifted(other, high_x, 0, False),
                    shifted(other, low_y, 1, True),
                    shifted(other, high_y, 1, False),
                    other,
                    other,
                ]
            )
            nearby = (nearby * member_weight[paint_now]).reshape(6, columns, P_SIZE, R)
            coupled = jnp.einsum(
                "fpq,feqr->epr", face_blocks, nearby, precision=lax.Precision.HIGHEST
            )
            update = jnp.einsum(
                "epq,eqr->epr",
                member_inverse[paint_now],
                member_target[paint_now] - coupled,
                precision=lax.Precision.HIGHEST,
            )
            state[paint_now] = update.reshape(span_x, span_y, width)
    first = first_is[0][..., None]
    return jnp.stack(
        [jnp.where(first, state[0], state[1]), jnp.where(first, state[1], state[0])], axis=2
    )


def _local_kernel(other_ref, face_ref, weight_ref, previous_ref, out_ref, *, span_x):
    tile = 2 * R
    other = other_ref[...]
    lanes = other.shape[1]
    lane = lax.broadcasted_iota(jnp.int32, (P_SIZE, tile), 1)
    low_half = lane < R
    rolled = [pltpu.roll(other[:, t * tile:(t + 1) * tile], R, 1) for t in range(span_x)]
    empty = jnp.zeros((P_SIZE, tile), jnp.float32)
    nearby = [
        jnp.concatenate([empty, other[:, :lanes - tile]], axis=1),
        jnp.concatenate([other[:, tile:], empty], axis=1),
        jnp.concatenate([jnp.where(low_half, 0.0, part) for part in rolled], axis=1),
        jnp.concatenate([jnp.where(low_half, part, 0.0) for part in rolled], axis=1),
        other,
        other,
    ]
    stacked = jnp.concatenate(
        [weight_ref[face:face + 1, :] * nearby[face] for face in range(6)], axis=0
    )
    out_ref[...] = jnp.dot(
        face_ref[...], stacked, precision=lax.Precision.HIGHEST, preferred_element_type=jnp.float32
    )


def local_part(other, face_blocks, weight, previous, span_x):
    vmem = pl.BlockSpec(memory_space=pltpu.VMEM)
    return pl.pallas_call(
        functools.partial(_local_kernel, span_x=span_x),
        out_shape=jax.ShapeDtypeStruct(other.shape, jnp.float32),
        in_specs=[vmem] * 4,
        out_specs=vmem,
        input_output_aliases={3: 0},
    )(*[pltpu.with_memory_space_constraint(v, pltpu.VMEM) for v in (other, face_blocks, weight, previous)])


def _half_sweep_kernel(
    local_ref, lo_x_ref, hi_x_ref, lo_y_ref, hi_y_ref, face_ref, weight_ref, inverse_ref,
    target_ref, previous_ref, old_lo_x, old_hi_x, old_lo_y, old_hi_y, out_ref, send_lo_x_ref,
    send_hi_x_ref, send_lo_y_ref, send_hi_y_ref, *, span_x
):
    tile = 2 * R
    highest = lax.Precision.HIGHEST
    lanes = local_ref.shape[1]
    lane = lax.broadcasted_iota(jnp.int32, (P_SIZE, tile), 1)
    low_half = lane < R
    lo_y = lo_y_ref[...]
    hi_y = hi_y_ref[...]

    def y_block(packed, x):
        held = packed[:, (x // 2) * tile:(x // 2 + 1) * tile]
        return held if x % 2 == 0 else pltpu.roll(held, R, 1)

    empty = jnp.zeros((P_SIZE, lanes - tile), jnp.float32)
    nearby = [
        jnp.concatenate([lo_x_ref[...], empty], axis=1),
        jnp.concatenate([empty, hi_x_ref[...]], axis=1),
        jnp.concatenate([jnp.where(low_half, y_block(lo_y, x), 0.0) for x in range(span_x)], axis=1),
        jnp.concatenate(
            [jnp.where(low_half, 0.0, pltpu.roll(y_block(hi_y, x), R, 1)) for x in range(span_x)], axis=1
        ),
    ]
    stacked = jnp.concatenate(
        [weight_ref[face:face + 1, :] * nearby[face] for face in range(4)], axis=0
    )
    coupled = local_ref[...] + jnp.dot(
        face_ref[:, :4 * P_SIZE], stacked, precision=highest, preferred_element_type=jnp.float32
    )
    rhs = target_ref[...] - coupled
    outs = []
    for x in range(span_x):
        part = rhs[:, x * tile:(x + 1) * tile]
        split = jnp.concatenate([jnp.where(low_half, part, 0.0), jnp.where(low_half, 0.0, part)], axis=0)
        outs.append(
            jnp.dot(
                inverse_ref[:, x * tile:(x + 1) * tile], split, precision=highest,
                preferred_element_type=jnp.float32,
            )
        )
    out_ref[...] = jnp.concatenate(outs, axis=1)
    send_lo_x_ref[...] = outs[-1]
    send_hi_x_ref[...] = outs[0]
    for t in range(span_x // 2):
        even, odd = outs[2 * t], outs[2 * t + 1]
        send_lo_y_ref[:, t * tile:(t + 1) * tile] = jnp.where(low_half, pltpu.roll(even, R, 1), odd)
        send_hi_y_ref[:, t * tile:(t + 1) * tile] = jnp.where(low_half, even, pltpu.roll(odd, R, 1))


def half_sweep(local, halos, face_blocks, weight, inverse, target, previous, old_sends, span_x):
    lanes = local.shape[1]
    x_shape = jax.ShapeDtypeStruct((P_SIZE, 2 * R), jnp.float32)
    y_shape = jax.ShapeDtypeStruct((P_SIZE, span_x * R), jnp.float32)
    vmem = pl.BlockSpec(memory_space=pltpu.VMEM)
    return pl.pallas_call(
        functools.partial(_half_sweep_kernel, span_x=span_x),
        out_shape=(jax.ShapeDtypeStruct((P_SIZE, lanes), jnp.float32), x_shape, x_shape, y_shape, y_shape),
        in_specs=[vmem] * 14,
        out_specs=(vmem,) * 5,
        input_output_aliases={9: 0, 10: 1, 11: 2, 12: 3, 13: 4},
    )(*[
        pltpu.with_memory_space_constraint(value, pltpu.VMEM)
        for value in (local, *halos, face_blocks, weight, inverse, target, previous, *old_sends)
    ])


def send_buffers(state, span_x):
    blocks = state.reshape(P_SIZE, span_x, 2, R)
    return (
        blocks[:, -1].reshape(P_SIZE, 2 * R),
        blocks[:, 0].reshape(P_SIZE, 2 * R),
        blocks[:, :, 1].reshape(P_SIZE, span_x * R),
        blocks[:, :, 0].reshape(P_SIZE, span_x * R),
    )


def trade(sends):
    lo_x, hi_x = (
        lax.ppermute(sends[0], "gx", shift_pairs("gx", 1)),
        lax.ppermute(sends[1], "gx", shift_pairs("gx", -1)),
    )
    lo_y, hi_y = (
        lax.ppermute(sends[2], "gy", shift_pairs("gy", 1)),
        lax.ppermute(sends[3], "gy", shift_pairs("gy", -1)),
    )
    return lo_x, hi_x, lo_y, hi_y


def shift_pairs(axis, step):
    count = lax.axis_size(axis)
    return [(i, (i + step) % count) for i in range(count)]


def lane_body(forcing, initial, blocks, face_blocks, strength, strong, colour, neighbours):
    span_x, span_y, span_z, width = forcing.shape
    count = span_x * span_y * span_z
    columns = span_x * span_y
    empty_slot = (span_x + 2) * (span_y + 2) * span_z
    first_is = [colour[:, :, 0] == paint for paint in (0, 1)]

    def pick(values, paint, axis=2):
        lead = (1,) * (axis - 2)
        mask = first_is[paint].reshape(lead + first_is[paint].shape + (1,) * (values.ndim - axis - 1))
        low = lax.index_in_dim(values, 0, axis=axis, keepdims=False)
        high = lax.index_in_dim(values, 1, axis=axis, keepdims=False)
        return jnp.where(mask, low, high)

    def to_lanes(values):
        return jnp.transpose(values.reshape(columns, P_SIZE, R), (1, 0, 2)).reshape(P_SIZE, columns * R)

    start_state = to_lanes(pick(initial, 1))
    first_sends = send_buffers(start_state, span_x)
    first_halos = trade(first_sends)
    by_colour = jnp.stack([pick(blocks, paint) for paint in (0, 1)]).reshape(count, P_SIZE, P_SIZE)
    inverse = block_inverses(by_colour, lanes_out=True)
    weight = jnp.where(neighbours == empty_slot, 0.0, strength * strong.astype(jnp.float32))
    member_inverse = [inverse[:, paint * columns * P_SIZE:(paint + 1) * columns * P_SIZE] for paint in (0, 1)]
    face_row = jnp.transpose(face_blocks, (1, 0, 2)).reshape(P_SIZE, 6 * P_SIZE)
    member_target = [to_lanes(pick(forcing, paint)) for paint in (0, 1)]
    member_weight = [
        jnp.pad(jnp.repeat(pick(weight, paint, axis=3).reshape(6, columns), R, axis=1), ((0, 2), (0, 0)))
        for paint in (0, 1)
    ]
    constants = [
        lax.optimization_barrier((member_inverse[paint], member_target[paint], member_weight[paint]))
        for paint in (0, 1)
    ]
    member_inverse, member_target, member_weight = (list(group) for group in zip(*constants))
    state = [jnp.zeros_like(start_state), start_state]
    sends = None
    local = jnp.zeros_like(start_state)
    for sweep_index in range(SWEEPS):
        for paint_now in (0, 1):
            halos = first_halos if sends is None else trade(sends)
            local = local_part(
                state[1 - paint_now], face_row, member_weight[paint_now], local, span_x
            )
            state[paint_now], *sends = half_sweep(
                local,
                halos,
                face_row,
                member_weight[paint_now],
                member_inverse[paint_now],
                member_target[paint_now],
                state[paint_now],
                first_sends if sends is None else sends,
                span_x,
            )
    whole = [
        jnp.transpose(part.reshape(P_SIZE, columns, R), (1, 0, 2)).reshape(span_x, span_y, 1, width)
        for part in state
    ]
    return jnp.where((colour == 0)[..., None], whole[0], whole[1])


def dispatch(forcing, *rest):
    span_x, span_y, span_z, width = forcing.shape
    if span_y == 2 and span_z == 2 and span_x % 2 == 0 and width == P_SIZE * R:
        return lane_body(forcing, *rest)
    return body(forcing, *rest)


def solution(mesh):
    in_specs = (
        P("gx", "gy", None, None),
        P("gx", "gy", None, None),
        P("gx", "gy", None, None),
        P(),
        P(None, "gx", "gy", None),
        P(None, "gx", "gy", None),
        P("gx", "gy", None),
        P(None, "gx", "gy", None),
    )
    out_specs = P("gx", "gy", None, None)
    return jax.shard_map(dispatch, mesh=mesh, in_specs=in_specs, out_specs=out_specs, check_vma=False)
```

```python
import functools

import jax
import jax.numpy as jnp
from jax import lax
from jax.experimental import pallas as pl
from jax.experimental.pallas import tpu as pltpu
from jax.sharding import PartitionSpec as P

P_SIZE = 64
R = 64
SWEEPS = 4


def padded(block, sides, width):
    for axis, dim in sides:
        count = lax.axis_size(axis)
        forward = [(i, i + 1) for i in range(count - 1)]
        backward = [(target, source) for source, target in forward]
        low = lax.ppermute(
            lax.slice_in_dim(block, block.shape[dim] - width, None, axis=dim), axis, forward
        )
        high = lax.ppermute(lax.slice_in_dim(block, 0, width, axis=dim), axis, backward)
        block = jnp.concatenate([low, block, high], axis=dim)
    return block


def _gauss_jordan_kernel(a_ref, o_ref, *, n, nb):
    lanes = n * nb
    tiles = lanes // 128
    del a_ref
    lane_t = lax.broadcasted_iota(jnp.int32, (n, 128), 1)
    lane_r = lax.broadcasted_iota(jnp.int32, (1, 128), 1)
    row_i = lax.broadcasted_iota(jnp.int32, (n, 128), 0)

    def spread(x):
        shift = nb
        while shift < 128:
            x = x + pltpu.roll(x, shift, 1)
            shift *= 2
        return x

    def step(k, carry):
        start = k * nb
        tile = start // 128
        off = start % 128
        tile_start = pl.multiple_of(tile * 128, 128)
        column = spread(
            jnp.where((lane_t >= off) & (lane_t < off + nb), o_ref[:, pl.ds(tile_start, 128)], 0.0)
        )
        pivot = jnp.sum(jnp.where(row_i == k, column, 0.0), axis=0, keepdims=True)
        base = pl.multiple_of((k // 8) * 8, 8)
        band = o_ref[pl.ds(base, 8), :]
        band_i = lax.broadcasted_iota(jnp.int32, band.shape, 0)
        row = jnp.sum(jnp.where(band_i == k - base, band, 0.0), axis=0, keepdims=True)
        for t in range(tiles):
            in_col = (t == tile) & (lane_r >= off) & (lane_r < off + nb)
            scaled = jnp.where(in_col, 1.0 / pivot, row[:, t * 128:(t + 1) * 128] / pivot)
            kept = jnp.where(in_col, 0.0, o_ref[:, t * 128:(t + 1) * 128])
            o_ref[:, t * 128:(t + 1) * 128] = jnp.where(row_i == k, scaled, kept - column * scaled)
        return carry

    lax.fori_loop(0, n, step, 0)


def block_inverses(matrices, lanes_out=False):
    nb, n, _ = matrices.shape
    if 128 % nb or (n * nb) % 128:
        assert not lanes_out
        lower_factor = jnp.linalg.cholesky(matrices)
        identity = jnp.broadcast_to(jnp.eye(n, dtype=matrices.dtype), matrices.shape)
        solved = jax.scipy.linalg.solve_triangular(lower_factor, identity, lower=True)
        return jnp.einsum("eqp,eqr->epr", solved, solved, precision=lax.Precision.HIGHEST)
    packed = jnp.transpose(matrices, (1, 2, 0)).reshape(n, n * nb)
    inverted = pl.pallas_call(
        functools.partial(_gauss_jordan_kernel, n=n, nb=nb),
        out_shape=jax.ShapeDtypeStruct((n, n * nb), jnp.float32),
        in_specs=[pl.BlockSpec(memory_space=pltpu.VMEM)],
        out_specs=pl.BlockSpec(memory_space=pltpu.VMEM),
        input_output_aliases={0: 0},
        cost_estimate=pl.CostEstimate(
            flops=2000 * n ** 3 * nb, transcendentals=0, bytes_accessed=8 * n * n * nb
        ),
    )(pltpu.with_memory_space_constraint(packed, pltpu.VMEM))
    if lanes_out:
        return jnp.transpose(inverted.reshape(n, n, nb), (0, 2, 1)).reshape(n, nb * n)
    return jnp.transpose(inverted.reshape(n, n, nb), (2, 0, 1))


def shifted(values, halo, dim, lower):
    width = values.shape[dim]
    if lower:
        return jnp.concatenate([halo, lax.slice_in_dim(values, 0, width - 1, axis=dim)], axis=dim)
    return jnp.concatenate([lax.slice_in_dim(values, 1, width, axis=dim), halo], axis=dim)


def exchange(values, axis, dim):
    count = lax.axis_size(axis)
    forward = [(i, i + 1) for i in range(count - 1)]
    backward = [(target, source) for source, target in forward]
    width = values.shape[dim]
    from_lower = lax.ppermute(lax.slice_in_dim(values, width - 1, width, axis=dim), axis, forward)
    from_upper = lax.ppermute(lax.slice_in_dim(values, 0, 1, axis=dim), axis, backward)
    return from_lower, from_upper


def body(forcing, initial, blocks, face_blocks, strength, strong, colour, neighbours):
    span_x, span_y, span_z, width = forcing.shape
    count = span_x * span_y * span_z
    columns = span_x * span_y
    empty_slot = (span_x + 2) * (span_y + 2) * span_z
    inverse = block_inverses(blocks.reshape(count, P_SIZE, P_SIZE)).reshape(
        span_x, span_y, span_z, P_SIZE, P_SIZE
    )
    weight = jnp.where(neighbours == empty_slot, 0.0, strength * strong.astype(jnp.float32))
    first_is = [colour[:, :, 0] == paint for paint in (0, 1)]

    def pick(values, paint, axis=2):
        lead = (1,) * (axis - 2)
        mask = first_is[paint].reshape(lead + first_is[paint].shape + (1,) * (values.ndim - axis - 1))
        low = lax.index_in_dim(values, 0, axis=axis, keepdims=False)
        high = lax.index_in_dim(values, 1, axis=axis, keepdims=False)
        return jnp.where(mask, low, high)

    member_inverse = [
        jnp.where(
            first_is[paint].reshape(1, columns, 1),
            inverse[:, :, 0],
            inverse[:, :, 1],
        ).reshape(P_SIZE, columns * P_SIZE)
        for paint in (0, 1)
    ]
    face_row = jnp.transpose(face_blocks, (1, 0, 2)).reshape(P_SIZE, 6 * P_SIZE)
    member_target = [pick(forcing, paint).reshape(columns, P_SIZE, R) for paint in (0, 1)]
    member_weight = [pick(weight, paint, axis=3)[..., None] for paint in (0, 1)]
    state = [pick(initial, 0), pick(initial, 1)]
    for sweep_index in range(SWEEPS):
        for paint_now in (0, 1):
            other = state[1 - paint_now]
            low_x, high_x = exchange(other, "gx", 0)
            low_y, high_y = exchange(other, "gy", 1)
            nearby = jnp.stack(
                [
                    shifted(other, low_x, 0, True),
                    shifted(other, high_x, 0, False),
                    shifted(other, low_y, 1, True),
                    shifted(other, high_y, 1, False),
                    other,
                    other,
                ]
            )
            nearby = (nearby * member_weight[paint_now]).reshape(6, columns, P_SIZE, R)
            coupled = jnp.einsum(
                "fpq,feqr->epr", face_blocks, nearby, precision=lax.Precision.HIGHEST
            )
            update = jnp.einsum(
                "epq,eqr->epr",
                member_inverse[paint_now],
                member_target[paint_now] - coupled,
                precision=lax.Precision.HIGHEST,
            )
            state[paint_now] = update.reshape(span_x, span_y, width)
    first = first_is[0][..., None]
    return jnp.stack(
        [jnp.where(first, state[0], state[1]), jnp.where(first, state[1], state[0])], axis=2
    )


def _half_sweep_kernel(
    other_ref, lo_x_ref, hi_x_ref, lo_y_ref, hi_y_ref, face_ref, weight_ref, inverse_ref,
    target_ref, previous_ref, old_lo_x, old_hi_x, old_lo_y, old_hi_y, out_ref, send_lo_x_ref, send_hi_x_ref, send_lo_y_ref, send_hi_y_ref, *, span_x
):
    tile = 2 * R
    highest = lax.Precision.HIGHEST
    other = other_ref[...]
    lanes = other.shape[1]
    lane = lax.broadcasted_iota(jnp.int32, (P_SIZE, tile), 1)
    low_half = lane < R
    tiles = [other[:, t * tile:(t + 1) * tile] for t in range(span_x)]
    lo_y = lo_y_ref[...]
    hi_y = hi_y_ref[...]

    def y_block(packed, x):
        held = packed[:, (x // 2) * tile:(x // 2 + 1) * tile]
        return held if x % 2 == 0 else pltpu.roll(held, R, 1)

    below, above = [], []
    for x in range(span_x):
        rolled = pltpu.roll(tiles[x], R, 1)
        below.append(jnp.where(low_half, y_block(lo_y, x), rolled))
        above.append(jnp.where(low_half, rolled, pltpu.roll(y_block(hi_y, x), R, 1)))
    nearby = [
        jnp.concatenate([lo_x_ref[...], other[:, :lanes - tile]], axis=1),
        jnp.concatenate([other[:, tile:], hi_x_ref[...]], axis=1),
        jnp.concatenate(below, axis=1),
        jnp.concatenate(above, axis=1),
        other,
        other,
    ]
    stacked = jnp.concatenate(
        [weight_ref[face:face + 1, :] * nearby[face] for face in range(6)], axis=0
    )
    coupled = jnp.dot(face_ref[...], stacked, precision=highest, preferred_element_type=jnp.float32)
    rhs = target_ref[...] - coupled
    outs = []
    for x in range(span_x):
        part = rhs[:, x * tile:(x + 1) * tile]
        split = jnp.concatenate([jnp.where(low_half, part, 0.0), jnp.where(low_half, 0.0, part)], axis=0)
        outs.append(
            jnp.dot(
                inverse_ref[:, x * tile:(x + 1) * tile], split, precision=highest,
                preferred_element_type=jnp.float32,
            )
        )
    out_ref[...] = jnp.concatenate(outs, axis=1)
    send_lo_x_ref[...] = outs[-1]
    send_hi_x_ref[...] = outs[0]
    for t in range(span_x // 2):
        even, odd = outs[2 * t], outs[2 * t + 1]
        send_lo_y_ref[:, t * tile:(t + 1) * tile] = jnp.where(low_half, pltpu.roll(even, R, 1), odd)
        send_hi_y_ref[:, t * tile:(t + 1) * tile] = jnp.where(low_half, even, pltpu.roll(odd, R, 1))


def half_sweep(other, halos, face_blocks, weight, inverse, target, previous, old_sends, span_x):
    lanes = other.shape[1]
    x_shape = jax.ShapeDtypeStruct((P_SIZE, 2 * R), jnp.float32)
    y_shape = jax.ShapeDtypeStruct((P_SIZE, span_x * R), jnp.float32)
    vmem = pl.BlockSpec(memory_space=pltpu.VMEM)
    return pl.pallas_call(
        functools.partial(_half_sweep_kernel, span_x=span_x),
        out_shape=(jax.ShapeDtypeStruct((P_SIZE, lanes), jnp.float32), x_shape, x_shape, y_shape, y_shape),
        in_specs=[vmem] * 14,
        out_specs=(vmem,) * 5,
        input_output_aliases={9: 0, 10: 1, 11: 2, 12: 3, 13: 4},
    )(*[
        pltpu.with_memory_space_constraint(value, pltpu.VMEM)
        for value in (other, *halos, face_blocks, weight, inverse, target, previous, *old_sends)
    ])


def send_buffers(state, span_x):
    blocks = state.reshape(P_SIZE, span_x, 2, R)
    return (
        blocks[:, -1].reshape(P_SIZE, 2 * R),
        blocks[:, 0].reshape(P_SIZE, 2 * R),
        blocks[:, :, 1].reshape(P_SIZE, span_x * R),
        blocks[:, :, 0].reshape(P_SIZE, span_x * R),
    )


def trade(sends):
    lo_x, hi_x = (
        lax.ppermute(sends[0], "gx", shift_pairs("gx", 1)),
        lax.ppermute(sends[1], "gx", shift_pairs("gx", -1)),
    )
    lo_y, hi_y = (
        lax.ppermute(sends[2], "gy", shift_pairs("gy", 1)),
        lax.ppermute(sends[3], "gy", shift_pairs("gy", -1)),
    )
    return lo_x, hi_x, lo_y, hi_y


def shift_pairs(axis, step):
    count = lax.axis_size(axis)
    return [(i, (i + step) % count) for i in range(count)]


def lane_body(forcing, initial, blocks, face_blocks, strength, strong, colour, neighbours):
    span_x, span_y, span_z, width = forcing.shape
    count = span_x * span_y * span_z
    columns = span_x * span_y
    empty_slot = (span_x + 2) * (span_y + 2) * span_z
    first_is = [colour[:, :, 0] == paint for paint in (0, 1)]

    def pick(values, paint, axis=2):
        lead = (1,) * (axis - 2)
        mask = first_is[paint].reshape(lead + first_is[paint].shape + (1,) * (values.ndim - axis - 1))
        low = lax.index_in_dim(values, 0, axis=axis, keepdims=False)
        high = lax.index_in_dim(values, 1, axis=axis, keepdims=False)
        return jnp.where(mask, low, high)

    def to_lanes(values):
        return jnp.transpose(values.reshape(columns, P_SIZE, R), (1, 0, 2)).reshape(P_SIZE, columns * R)

    start_state = to_lanes(pick(initial, 1))
    first_sends = send_buffers(start_state, span_x)
    first_halos = trade(first_sends)
    inverse = block_inverses(blocks.reshape(count, P_SIZE, P_SIZE), lanes_out=True).reshape(
        P_SIZE, columns, span_z, P_SIZE
    )
    weight = jnp.where(neighbours == empty_slot, 0.0, strength * strong.astype(jnp.float32))
    member_inverse = [
        jnp.where(
            first_is[paint].reshape(1, columns, 1),
            inverse[:, :, 0],
            inverse[:, :, 1],
        ).reshape(P_SIZE, columns * P_SIZE)
        for paint in (0, 1)
    ]
    face_row = jnp.transpose(face_blocks, (1, 0, 2)).reshape(P_SIZE, 6 * P_SIZE)
    member_target = [to_lanes(pick(forcing, paint)) for paint in (0, 1)]
    member_weight = [
        jnp.pad(jnp.repeat(pick(weight, paint, axis=3).reshape(6, columns), R, axis=1), ((0, 2), (0, 0)))
        for paint in (0, 1)
    ]
    constants = [
        lax.optimization_barrier((member_inverse[paint], member_target[paint], member_weight[paint]))
        for paint in (0, 1)
    ]
    member_inverse, member_target, member_weight = (list(group) for group in zip(*constants))
    state = [jnp.zeros_like(start_state), start_state]
    sends = None
    for sweep_index in range(SWEEPS):
        for paint_now in (0, 1):
            halos = first_halos if sends is None else trade(sends)
            state[paint_now], *sends = half_sweep(
                state[1 - paint_now],
                halos,
                face_row,
                member_weight[paint_now],
                member_inverse[paint_now],
                member_target[paint_now],
                state[paint_now],
                first_sends if sends is None else sends,
                span_x,
            )
    whole = [
        jnp.transpose(part.reshape(P_SIZE, columns, R), (1, 0, 2)).reshape(span_x, span_y, 1, width)
        for part in state
    ]
    return jnp.where((colour == 0)[..., None], whole[0], whole[1])


def dispatch(forcing, *rest):
    span_x, span_y, span_z, width = forcing.shape
    if span_y == 2 and span_z == 2 and span_x % 2 == 0 and width == P_SIZE * R:
        return lane_body(forcing, *rest)
    return body(forcing, *rest)


def solution(mesh):
    in_specs = (
        P("gx", "gy", None, None),
        P("gx", "gy", None, None),
        P("gx", "gy", None, None),
        P(),
        P(None, "gx", "gy", None),
        P(None, "gx", "gy", None),
        P("gx", "gy", None),
        P(None, "gx", "gy", None),
    )
    out_specs = P("gx", "gy", None, None)
    return jax.shard_map(dispatch, mesh=mesh, in_specs=in_specs, out_specs=out_specs, check_vma=False)
```

```python
import functools

import jax
import jax.numpy as jnp
from jax import lax
from jax.experimental import pallas as pl
from jax.experimental.pallas import tpu as pltpu
from jax.sharding import PartitionSpec as P

P_SIZE = 64
R = 64
SWEEPS = 4


def padded(block, sides, width):
    for axis, dim in sides:
        count = lax.axis_size(axis)
        forward = [(i, i + 1) for i in range(count - 1)]
        backward = [(target, source) for source, target in forward]
        low = lax.ppermute(
            lax.slice_in_dim(block, block.shape[dim] - width, None, axis=dim), axis, forward
        )
        high = lax.ppermute(lax.slice_in_dim(block, 0, width, axis=dim), axis, backward)
        block = jnp.concatenate([low, block, high], axis=dim)
    return block


def _gauss_jordan_kernel(a_ref, o_ref, *, n, nb):
    lanes = n * nb
    tiles = lanes // 128
    del a_ref
    lane_t = lax.broadcasted_iota(jnp.int32, (n, 128), 1)
    lane_r = lax.broadcasted_iota(jnp.int32, (1, 128), 1)
    row_i = lax.broadcasted_iota(jnp.int32, (n, 128), 0)

    def spread(x):
        shift = nb
        while shift < 128:
            x = x + pltpu.roll(x, shift, 1)
            shift *= 2
        return x

    def step(k, carry):
        start = k * nb
        tile = start // 128
        off = start % 128
        tile_start = pl.multiple_of(tile * 128, 128)
        column = spread(
            jnp.where((lane_t >= off) & (lane_t < off + nb), o_ref[:, pl.ds(tile_start, 128)], 0.0)
        )
        pivot = jnp.sum(jnp.where(row_i == k, column, 0.0), axis=0, keepdims=True)
        base = pl.multiple_of((k // 8) * 8, 8)
        band = o_ref[pl.ds(base, 8), :]
        band_i = lax.broadcasted_iota(jnp.int32, band.shape, 0)
        row = jnp.sum(jnp.where(band_i == k - base, band, 0.0), axis=0, keepdims=True)
        for t in range(tiles):
            in_col = (t == tile) & (lane_r >= off) & (lane_r < off + nb)
            scaled = jnp.where(in_col, 1.0 / pivot, row[:, t * 128:(t + 1) * 128] / pivot)
            kept = jnp.where(in_col, 0.0, o_ref[:, t * 128:(t + 1) * 128])
            o_ref[:, t * 128:(t + 1) * 128] = jnp.where(row_i == k, scaled, kept - column * scaled)
        return carry

    lax.fori_loop(0, n, step, 0)


def block_inverses(matrices, lanes_out=False):
    nb, n, _ = matrices.shape
    if 128 % nb or (n * nb) % 128:
        assert not lanes_out
        lower_factor = jnp.linalg.cholesky(matrices)
        identity = jnp.broadcast_to(jnp.eye(n, dtype=matrices.dtype), matrices.shape)
        solved = jax.scipy.linalg.solve_triangular(lower_factor, identity, lower=True)
        return jnp.einsum("eqp,eqr->epr", solved, solved, precision=lax.Precision.HIGHEST)
    packed = jnp.transpose(matrices, (1, 2, 0)).reshape(n, n * nb)
    inverted = pl.pallas_call(
        functools.partial(_gauss_jordan_kernel, n=n, nb=nb),
        out_shape=jax.ShapeDtypeStruct((n, n * nb), jnp.float32),
        in_specs=[pl.BlockSpec(memory_space=pltpu.VMEM)],
        out_specs=pl.BlockSpec(memory_space=pltpu.VMEM),
        input_output_aliases={0: 0},
        cost_estimate=pl.CostEstimate(
            flops=2000 * n ** 3 * nb, transcendentals=0, bytes_accessed=8 * n * n * nb
        ),
    )(pltpu.with_memory_space_constraint(packed, pltpu.VMEM))
    if lanes_out:
        return jnp.transpose(inverted.reshape(n, n, nb), (0, 2, 1)).reshape(n, nb * n)
    return jnp.transpose(inverted.reshape(n, n, nb), (2, 0, 1))


def shifted(values, halo, dim, lower):
    width = values.shape[dim]
    if lower:
        return jnp.concatenate([halo, lax.slice_in_dim(values, 0, width - 1, axis=dim)], axis=dim)
    return jnp.concatenate([lax.slice_in_dim(values, 1, width, axis=dim), halo], axis=dim)


def exchange(values, axis, dim):
    count = lax.axis_size(axis)
    forward = [(i, i + 1) for i in range(count - 1)]
    backward = [(target, source) for source, target in forward]
    width = values.shape[dim]
    from_lower = lax.ppermute(lax.slice_in_dim(values, width - 1, width, axis=dim), axis, forward)
    from_upper = lax.ppermute(lax.slice_in_dim(values, 0, 1, axis=dim), axis, backward)
    return from_lower, from_upper


def body(forcing, initial, blocks, face_blocks, strength, strong, colour, neighbours):
    span_x, span_y, span_z, width = forcing.shape
    count = span_x * span_y * span_z
    columns = span_x * span_y
    empty_slot = (span_x + 2) * (span_y + 2) * span_z
    inverse = block_inverses(blocks.reshape(count, P_SIZE, P_SIZE)).reshape(
        span_x, span_y, span_z, P_SIZE, P_SIZE
    )
    weight = jnp.where(neighbours == empty_slot, 0.0, strength * strong.astype(jnp.float32))
    first_is = [colour[:, :, 0] == paint for paint in (0, 1)]

    def pick(values, paint, axis=2):
        lead = (1,) * (axis - 2)
        mask = first_is[paint].reshape(lead + first_is[paint].shape + (1,) * (values.ndim - axis - 1))
        low = lax.index_in_dim(values, 0, axis=axis, keepdims=False)
        high = lax.index_in_dim(values, 1, axis=axis, keepdims=False)
        return jnp.where(mask, low, high)

    member_inverse = [inverse[:, paint * columns * P_SIZE:(paint + 1) * columns * P_SIZE] for paint in (0, 1)]
    face_row = jnp.transpose(face_blocks, (1, 0, 2)).reshape(P_SIZE, 6 * P_SIZE)
    member_target = [pick(forcing, paint).reshape(columns, P_SIZE, R) for paint in (0, 1)]
    member_weight = [pick(weight, paint, axis=3)[..., None] for paint in (0, 1)]
    state = [pick(initial, 0), pick(initial, 1)]
    for sweep_index in range(SWEEPS):
        for paint_now in (0, 1):
            other = state[1 - paint_now]
            low_x, high_x = exchange(other, "gx", 0)
            low_y, high_y = exchange(other, "gy", 1)
            nearby = jnp.stack(
                [
                    shifted(other, low_x, 0, True),
                    shifted(other, high_x, 0, False),
                    shifted(other, low_y, 1, True),
                    shifted(other, high_y, 1, False),
                    other,
                    other,
                ]
            )
            nearby = (nearby * member_weight[paint_now]).reshape(6, columns, P_SIZE, R)
            coupled = jnp.einsum(
                "fpq,feqr->epr", face_blocks, nearby, precision=lax.Precision.HIGHEST
            )
            update = jnp.einsum(
                "epq,eqr->epr",
                member_inverse[paint_now],
                member_target[paint_now] - coupled,
                precision=lax.Precision.HIGHEST,
            )
            state[paint_now] = update.reshape(span_x, span_y, width)
    first = first_is[0][..., None]
    return jnp.stack(
        [jnp.where(first, state[0], state[1]), jnp.where(first, state[1], state[0])], axis=2
    )


def _half_sweep_kernel(
    other_ref, lo_x_ref, hi_x_ref, lo_y_ref, hi_y_ref, face_ref, weight_ref, inverse_ref,
    target_ref, previous_ref, old_lo_x, old_hi_x, old_lo_y, old_hi_y, out_ref, send_lo_x_ref, send_hi_x_ref, send_lo_y_ref, send_hi_y_ref, *, span_x
):
    tile = 2 * R
    highest = lax.Precision.HIGHEST
    other = other_ref[...]
    lanes = other.shape[1]
    lane = lax.broadcasted_iota(jnp.int32, (P_SIZE, tile), 1)
    low_half = lane < R
    tiles = [other[:, t * tile:(t + 1) * tile] for t in range(span_x)]
    lo_y = lo_y_ref[...]
    hi_y = hi_y_ref[...]

    def y_block(packed, x):
        held = packed[:, (x // 2) * tile:(x // 2 + 1) * tile]
        return held if x % 2 == 0 else pltpu.roll(held, R, 1)

    below, above = [], []
    for x in range(span_x):
        rolled = pltpu.roll(tiles[x], R, 1)
        below.append(jnp.where(low_half, y_block(lo_y, x), rolled))
        above.append(jnp.where(low_half, rolled, pltpu.roll(y_block(hi_y, x), R, 1)))
    nearby = [
        jnp.concatenate([lo_x_ref[...], other[:, :lanes - tile]], axis=1),
        jnp.concatenate([other[:, tile:], hi_x_ref[...]], axis=1),
        jnp.concatenate(below, axis=1),
        jnp.concatenate(above, axis=1),
        other,
        other,
    ]
    stacked = jnp.concatenate(
        [weight_ref[face:face + 1, :] * nearby[face] for face in range(6)], axis=0
    )
    coupled = jnp.dot(face_ref[...], stacked, precision=highest, preferred_element_type=jnp.float32)
    rhs = target_ref[...] - coupled
    outs = []
    for x in range(span_x):
        part = rhs[:, x * tile:(x + 1) * tile]
        split = jnp.concatenate([jnp.where(low_half, part, 0.0), jnp.where(low_half, 0.0, part)], axis=0)
        outs.append(
            jnp.dot(
                inverse_ref[:, x * tile:(x + 1) * tile], split, precision=highest,
                preferred_element_type=jnp.float32,
            )
        )
    out_ref[...] = jnp.concatenate(outs, axis=1)
    send_lo_x_ref[...] = outs[-1]
    send_hi_x_ref[...] = outs[0]
    for t in range(span_x // 2):
        even, odd = outs[2 * t], outs[2 * t + 1]
        send_lo_y_ref[:, t * tile:(t + 1) * tile] = jnp.where(low_half, pltpu.roll(even, R, 1), odd)
        send_hi_y_ref[:, t * tile:(t + 1) * tile] = jnp.where(low_half, even, pltpu.roll(odd, R, 1))


def half_sweep(other, halos, face_blocks, weight, inverse, target, previous, old_sends, span_x):
    lanes = other.shape[1]
    x_shape = jax.ShapeDtypeStruct((P_SIZE, 2 * R), jnp.float32)
    y_shape = jax.ShapeDtypeStruct((P_SIZE, span_x * R), jnp.float32)
    vmem = pl.BlockSpec(memory_space=pltpu.VMEM)
    return pl.pallas_call(
        functools.partial(_half_sweep_kernel, span_x=span_x),
        out_shape=(jax.ShapeDtypeStruct((P_SIZE, lanes), jnp.float32), x_shape, x_shape, y_shape, y_shape),
        in_specs=[vmem] * 14,
        out_specs=(vmem,) * 5,
        input_output_aliases={9: 0, 10: 1, 11: 2, 12: 3, 13: 4},
    )(*[
        pltpu.with_memory_space_constraint(value, pltpu.VMEM)
        for value in (other, *halos, face_blocks, weight, inverse, target, previous, *old_sends)
    ])


def send_buffers(state, span_x):
    blocks = state.reshape(P_SIZE, span_x, 2, R)
    return (
        blocks[:, -1].reshape(P_SIZE, 2 * R),
        blocks[:, 0].reshape(P_SIZE, 2 * R),
        blocks[:, :, 1].reshape(P_SIZE, span_x * R),
        blocks[:, :, 0].reshape(P_SIZE, span_x * R),
    )


def trade(sends):
    lo_x, hi_x = (
        lax.ppermute(sends[0], "gx", shift_pairs("gx", 1)),
        lax.ppermute(sends[1], "gx", shift_pairs("gx", -1)),
    )
    lo_y, hi_y = (
        lax.ppermute(sends[2], "gy", shift_pairs("gy", 1)),
        lax.ppermute(sends[3], "gy", shift_pairs("gy", -1)),
    )
    return lo_x, hi_x, lo_y, hi_y


def shift_pairs(axis, step):
    count = lax.axis_size(axis)
    return [(i, (i + step) % count) for i in range(count)]


def lane_body(forcing, initial, blocks, face_blocks, strength, strong, colour, neighbours):
    span_x, span_y, span_z, width = forcing.shape
    count = span_x * span_y * span_z
    columns = span_x * span_y
    empty_slot = (span_x + 2) * (span_y + 2) * span_z
    first_is = [colour[:, :, 0] == paint for paint in (0, 1)]

    def pick(values, paint, axis=2):
        lead = (1,) * (axis - 2)
        mask = first_is[paint].reshape(lead + first_is[paint].shape + (1,) * (values.ndim - axis - 1))
        low = lax.index_in_dim(values, 0, axis=axis, keepdims=False)
        high = lax.index_in_dim(values, 1, axis=axis, keepdims=False)
        return jnp.where(mask, low, high)

    def to_lanes(values):
        return jnp.transpose(values.reshape(columns, P_SIZE, R), (1, 0, 2)).reshape(P_SIZE, columns * R)

    face_row = jnp.transpose(face_blocks, (1, 0, 2)).reshape(P_SIZE, 6 * P_SIZE)
    start_state, face_row = lax.optimization_barrier((to_lanes(pick(initial, 1)), face_row))
    first_sends = send_buffers(start_state, span_x)
    first_halos = trade(first_sends)
    by_colour = jnp.stack([pick(blocks, paint) for paint in (0, 1)]).reshape(count, P_SIZE, P_SIZE)
    inverse = block_inverses(by_colour, lanes_out=True)
    weight = jnp.where(neighbours == empty_slot, 0.0, strength * strong.astype(jnp.float32))
    member_inverse = [inverse[:, paint * columns * P_SIZE:(paint + 1) * columns * P_SIZE] for paint in (0, 1)]
    member_target = [to_lanes(pick(forcing, paint)) for paint in (0, 1)]
    member_weight = [
        jnp.pad(jnp.repeat(pick(weight, paint, axis=3).reshape(6, columns), R, axis=1), ((0, 2), (0, 0)))
        for paint in (0, 1)
    ]
    constants = [
        lax.optimization_barrier((member_inverse[paint], member_target[paint], member_weight[paint]))
        for paint in (0, 1)
    ]
    member_inverse, member_target, member_weight = (list(group) for group in zip(*constants))
    state = [jnp.zeros_like(start_state), start_state]
    sends = None
    for sweep_index in range(SWEEPS):
        for paint_now in (0, 1):
            halos = first_halos if sends is None else trade(sends)
            state[paint_now], *sends = half_sweep(
                state[1 - paint_now],
                halos,
                face_row,
                member_weight[paint_now],
                member_inverse[paint_now],
                member_target[paint_now],
                state[paint_now],
                first_sends if sends is None else sends,
                span_x,
            )
    whole = [
        jnp.transpose(part.reshape(P_SIZE, columns, R), (1, 0, 2)).reshape(span_x, span_y, 1, width)
        for part in state
    ]
    return jnp.where((colour == 0)[..., None], whole[0], whole[1])


def dispatch(forcing, *rest):
    span_x, span_y, span_z, width = forcing.shape
    if span_y == 2 and span_z == 2 and span_x % 2 == 0 and width == P_SIZE * R:
        return lane_body(forcing, *rest)
    return body(forcing, *rest)


def solution(mesh):
    in_specs = (
        P("gx", "gy", None, None),
        P("gx", "gy", None, None),
        P("gx", "gy", None, None),
        P(),
        P(None, "gx", "gy", None),
        P(None, "gx", "gy", None),
        P("gx", "gy", None),
        P(None, "gx", "gy", None),
    )
    out_specs = P("gx", "gy", None, None)
    return jax.shard_map(dispatch, mesh=mesh, in_specs=in_specs, out_specs=out_specs, check_vma=False)
```
